128 devices in a mesh: wall: 8 (over z, core), sx: 4 (over x), sy: 4 (over y).
Axes of the slice: x: 4, y: 4, z: 4, core: 2. Of those that a mesh axis runs over, the one named last changes fastest.
Arguments:
- forcing: float32 [4, 8, 32, 384], P('sx', 'sy', 'wall'), may hold values from -17 to 17
- pivot_inverse: float32 [4, 8, 32, 384, 384], P('sx', 'sy', 'wall'), may hold values from -1 to 5
- lower_face: float32 [4, 8, 32, 96, 96], P('sx', 'sy', 'wall'), may hold values from -1 to 2
- upper_face: float32 [4, 8, 32, 96, 96], P('sx', 'sy', 'wall'), may hold values from -1 to 2
- side_coupling: float32 [4, 8, 32, 4, 96, 96], P('sx', 'sy', 'wall'), may hold values from -0.3125 to 0.3125
- orientation: int32 [4, 8, 32, 4], P('sx', 'sy', 'wall'), may hold values from 0 to 3
Outputs:
- solution: float32 [4, 8, 32, 384], P('sx', 'sy', 'wall')
- relative_residual: float32 [], replicated
- forcing_rms: float32 [], replicated
The draws below stay inside these ranges and needn't reach their ends.
All inputs are finite; a program needn't handle non-finite values.
Results may differ from the reference program's by a relative error of at most 0.0003.
Values sent between devices are 32-bit elements; how exact they have to be, the bound alone decides.
No kernel may reach another device: no remote copies, remote signals or barrier semaphores. Data moves between devices by JAX's collectives and lax.ppermute only.
A program may use at most 64 MiB of HBM per device.

```python
import math
import jax
import jax.numpy as jnp
from jax import lax

PTS = 4
VARS = 6
BLOCK = 384
FACE = 96
ITERS = 3
NLX = 4
NLY = 8
LINE_ELEMENTS = 32


def draw_forcing(key, part):
    full_shape = (NLX, NLY, LINE_ELEMENTS, BLOCK)
    position = lax.broadcasted_iota(jnp.int32, full_shape, 2).astype(jnp.float32) / (LINE_ELEMENTS - 1)
    values = jnp.clip(jax.random.normal(key, full_shape, jnp.float32), -4.0, 4.0)
    return values * jnp.exp(position * math.log(3.0))


def channel_rates(key, leading_dims):
    split_random_keys = jax.random.split(key, 3)
    lowest, highest = (0.5 / LINE_ELEMENTS, 0.15)
    falloff_factor = jnp.exp(jax.random.uniform(split_random_keys[0], (FACE,), jnp.float32, math.log(lowest), math.log(highest)))
    random_perturbation = jax.random.uniform(split_random_keys[1], leading_dims + (FACE,), jnp.float32, 0.7, 1.4)
    spike_threshold = jnp.where(jax.random.uniform(split_random_keys[2], leading_dims + (1,), jnp.float32) < 3.0 / LINE_ELEMENTS, 0.5, 1.0)
    return jnp.exp(-falloff_factor * random_perturbation) * spike_threshold


def draw_pivot_inverse(key, part):
    split_random_keys = jax.random.split(jax.random.fold_in(key, 11), 4)
    leading_dims = (NLX, NLY, LINE_ELEMENTS)
    full_shape = leading_dims + (BLOCK, BLOCK)
    scatter_part = jnp.clip(jax.random.normal(split_random_keys[0], full_shape, jnp.float32), -4.0, 4.0)
    middle = jnp.exp(jax.random.uniform(split_random_keys[1], leading_dims + (BLOCK,), jnp.float32, math.log(1.5), math.log(4.0)))
    upward = channel_rates(split_random_keys[2], leading_dims)
    downward = channel_rates(split_random_keys[3], leading_dims)
    row_ids = lax.broadcasted_iota(jnp.int32, (BLOCK, BLOCK), 0)
    col_ids = lax.broadcasted_iota(jnp.int32, (BLOCK, BLOCK), 1)
    offset = BLOCK - FACE
    upward_row = jnp.concatenate([jnp.zeros(leading_dims + (offset,), jnp.float32), upward], -1)
    downward_row = jnp.concatenate([downward, jnp.zeros(leading_dims + (offset,), jnp.float32)], -1)
    result = jnp.where(row_ids == col_ids, middle[..., :, None], scatter_part * (0.25 / math.sqrt(BLOCK)))
    result = result + jnp.where((row_ids >= offset) & (col_ids == row_ids - offset), upward_row[..., :, None], 0.0)
    result = result + jnp.where((row_ids < FACE) & (col_ids == row_ids + offset), downward_row[..., :, None], 0.0)
    return result


def face_coupling(key, salt):
    split_random_keys = jax.random.split(jax.random.fold_in(key, salt), 2)
    leading_dims = (NLX, NLY, LINE_ELEMENTS)
    full_shape = leading_dims + (FACE, FACE)
    scatter_part = jnp.clip(jax.random.normal(split_random_keys[0], full_shape, jnp.float32), -4.0, 4.0)
    gain_part = jax.random.uniform(split_random_keys[1], leading_dims + (FACE,), jnp.float32, 0.9, 1.0)
    row_ids = lax.broadcasted_iota(jnp.int32, (FACE, FACE), 0)
    col_ids = lax.broadcasted_iota(jnp.int32, (FACE, FACE), 1)
    return jnp.where(row_ids == col_ids, gain_part[..., :, None], 0.0) + scatter_part * (0.1 / math.sqrt(FACE))


def draw_lower_face(key, part):
    return face_coupling(key, 23)


def draw_upper_face(key, part):
    return face_coupling(key, 37)


def place_ends(values, stream_key, least, high):
    longest = values.shape.index(max(values.shape))
    spots = []
    for shift in (0, 1):
        where = [jax.random.randint(jax.random.fold_in(stream_key, axis), (), 0, length) for axis, length in enumerate(values.shape)]
        where[longest] = (where[longest] + shift) % values.shape[longest]
        spots.append(tuple(where))
    return values.at[spots[0]].set(least).at[spots[1]].set(high)


def shard_levels(own_key, shape, shards, low, largest):
    def one(dim, blocks):
        steps = jax.random.uniform(jax.random.fold_in(jax.random.fold_in(own_key, 6), dim), (blocks,), jnp.float32, low / len(shards), largest / len(shards))
        return jnp.repeat(jnp.exp(steps), shape[dim] // blocks).reshape((-1,) + (1,) * (len(shape) - dim - 1))

    gain = one(*shards[0])
    for cut in shards[1:]:
        gain = gain * one(*cut)
    return gain


def noise(key, shape, scale, bound, shards=(), held_as=jnp.bfloat16):
    values = scale * jax.random.normal(key, shape, jnp.float32)
    if shards:
        values = values * shard_levels(key, shape, shards, -0.22, 0.18)
    return jnp.clip(values, -bound, bound).astype(held_as)


def setup_inputs(seed: int = 0) -> dict:
    key_list = jax.random.split(jax.random.key(seed), 7)
    return {
        "forcing": draw_forcing(jax.random.fold_in(key_list[6], 71), 0),
        "pivot_inverse": draw_pivot_inverse(jax.random.fold_in(key_list[6], 71), 0),
        "lower_face": draw_lower_face(jax.random.fold_in(key_list[6], 71), 0),
        "upper_face": draw_upper_face(jax.random.fold_in(key_list[6], 71), 0),
        "side_coupling": noise(key_list[4], (NLX, NLY, LINE_ELEMENTS, 4, FACE, FACE), (4 * FACE) ** -0.5, 0.3125, ((0, 4), (1, 4), (2, 8)), jnp.float32),
        "orientation": place_ends(jax.random.randint(key_list[5], (NLX, NLY, LINE_ELEMENTS, 4), 0, 4), jax.random.fold_in(key_list[5], 1), 0, 3).astype(jnp.int32),
    }


precise = lax.Precision.HIGHEST

def face_traces(vector_in):
    leading = vector_in.shape[:-1]
    node_grid = vector_in.reshape(leading + (PTS, PTS, PTS, VARS))
    facets = [node_grid[..., :, :, 0, :], node_grid[..., :, :, PTS - 1, :], node_grid[..., :, 0, :, :], node_grid[..., :, PTS - 1, :, :]]
    flattened = [one_facet.reshape(leading + (FACE,)) for one_facet in facets]
    return jnp.stack(flattened, -2).reshape(leading + (4 * FACE,))

def lateral_term(vector_in, padded, side_coupling, orientation):
    single_row_block, rows_two = (vector_in.shape[0], vector_in.shape[1])
    beside_all = padded.reshape(padded.shape[:3] + (4, FACE))
    across = jnp.stack([beside_all[0:single_row_block, 1:rows_two + 1, :, 1], beside_all[2:single_row_block + 2, 1:rows_two + 1, :, 0], beside_all[1:single_row_block + 1, 0:rows_two, :, 3], beside_all[1:single_row_block + 1, 2:rows_two + 2, :, 2]], 3)
    shaped = across.reshape(across.shape[:4] + (PTS, PTS, VARS))
    turned = jnp.zeros(shaped.shape, jnp.float32)
    for quarter in range(4):
        picked = (orientation == quarter).astype(jnp.float32)[..., None, None, None]
        turned = turned + picked * jnp.rot90(shaped, quarter, axes=(4, 5))
    coupled = jnp.einsum('xyefab,xyefb->xyefa', side_coupling, turned.reshape(across.shape), precision=precise)
    pieces = coupled.reshape(across.shape[:4] + (PTS, PTS, VARS))
    result = jnp.zeros(vector_in.shape[:3] + (PTS, PTS, PTS, VARS), jnp.float32)
    result = result.at[:, :, :, :, :, 0, :].add(pieces[:, :, :, 0])
    result = result.at[:, :, :, :, :, PTS - 1, :].add(pieces[:, :, :, 1])
    result = result.at[:, :, :, :, 0, :, :].add(pieces[:, :, :, 2])
    result = result.at[:, :, :, :, PTS - 1, :, :].add(pieces[:, :, :, 3])
    return result.reshape(vector_in.shape)

def precondition(resid, pivot_inverse, lower_face, upper_face):
    elements = resid.shape[2]
    carried = jnp.zeros(resid.shape[:2] + (FACE,), jnp.float32)
    reduced = []
    for i in range(elements):
        lowered = jnp.einsum('xyab,xyb->xya', lower_face[:, :, i], carried, precision=precise)
        block_row = jnp.concatenate([resid[:, :, i, :FACE] - lowered, resid[:, :, i, FACE:]], -1)
        reduced.append(block_row)
        carried = jnp.einsum('xyab,xyb->xya', pivot_inverse[:, :, i, BLOCK - FACE:, :], block_row, precision=precise)
    carried = jnp.zeros(resid.shape[:2] + (FACE,), jnp.float32)
    solved = [None] * elements
    for i in reversed(range(elements)):
        raised = jnp.einsum('xyab,xyb->xya', upper_face[:, :, i], carried, precision=precise)
        block_row = jnp.concatenate([reduced[i][..., :BLOCK - FACE], reduced[i][..., BLOCK - FACE:] - raised], -1)
        answer = jnp.einsum('xyab,xyb->xya', pivot_inverse[:, :, i], block_row, precision=precise)
        solved[i] = answer
        carried = answer[..., :FACE]
    return jnp.stack(solved, 2)

def solve_small(matrix, vector):
    extent = matrix.shape[0]
    index_ids = jnp.arange(extent)
    for k in range(extent):
        factor_col = jnp.where(index_ids > k, matrix[:, k] / matrix[k, k], 0.0)
        matrix = matrix - factor_col[:, None] * matrix[k][None, :]
        vector = vector - factor_col * vector[k]
    solved = jnp.zeros((extent,), jnp.float32)
    for k in reversed(range(extent)):
        solved = solved.at[k].set((vector[k] - jnp.sum(matrix[k] * solved)) / matrix[k, k])
    return solved

def least_squares(hessenberg, initial_norm):
    target = jnp.zeros((hessenberg.shape[0],), jnp.float32).at[0].set(initial_norm)
    normal = jnp.dot(hessenberg.T, hessenberg, precision=precise)
    weights = solve_small(normal, jnp.dot(hessenberg.T, target, precision=precise))
    misfit = target - jnp.dot(hessenberg, weights, precision=precise)
    return (weights, jnp.sqrt(jnp.sum(misfit * misfit)) / initial_norm)

def reference(forcing, pivot_inverse, lower_face, upper_face, side_coupling, orientation):
    squares = jnp.sum(forcing * forcing)
    forcing_rms = jnp.sqrt(squares / (NLX * NLY * LINE_ELEMENTS * BLOCK))
    initial_norm = jnp.sqrt(squares)
    krylov = [forcing / initial_norm]
    directions = []
    columns = []
    for j in range(ITERS):
        direction = precondition(krylov[j], pivot_inverse, lower_face, upper_face)
        directions.append(direction)
        traces = face_traces(direction)
        padded = jnp.pad(traces, ((1, 1), (1, 1), (0, 0), (0, 0)))
        vector_w = krylov[j] + lateral_term(direction, padded, side_coupling, orientation)
        listed = []
        for i in range(j + 1):
            projected = jnp.sum(vector_w * krylov[i])
            vector_w = vector_w - projected * krylov[i]
            listed.append(projected)
        length = jnp.sqrt(jnp.sum(vector_w * vector_w))
        krylov.append(vector_w / length)
        columns.append(jnp.concatenate([jnp.stack(listed), length[None], jnp.zeros((ITERS - 1 - j,), jnp.float32)]))
    hessenberg = jnp.stack(columns, 1)
    weights, relative = least_squares(hessenberg, initial_norm)
    solution = weights[0] * directions[0]
    for j in range(1, ITERS):
        solution = solution + weights[j] * directions[j]
    return (solution, relative, forcing_rms)
```

```python
import jax
import jax.numpy as jnp
from jax import lax
from jax.sharding import PartitionSpec as P

PTS = 4
VARS = 6
BLOCK = 384
FACE = 96
ITERS = 3


precise = lax.Precision.HIGHEST


def entering(part, axis, combine, identity, reverse):
    count = lax.axis_size(axis)
    place = lax.axis_index(axis)
    ahead = count - 1 - place if reverse else place
    gathered = jax.tree.map(lambda a: lax.all_gather(a, axis), part)
    state = jax.tree.map(lambda a, e: jnp.zeros_like(a) + jnp.asarray(e, a.dtype), part, identity)

    def one(step, state):
        source = count - 1 - step if reverse else step
        return combine(
            state, jax.tree.map(lambda a: lax.dynamic_index_in_dim(a, source, 0, False), gathered)
        )

    return lax.fori_loop(0, ahead, one, state)


def extended(block, sides, width):
    for axis, dim in sides:
        count = lax.axis_size(axis)
        forward = [(i, i + 1) for i in range(count - 1)]
        backward = [(target, source) for source, target in forward]
        low = lax.ppermute(
            lax.slice_in_dim(block, block.shape[dim] - width, None, axis=dim), axis, forward
        )
        high = lax.ppermute(lax.slice_in_dim(block, 0, width, axis=dim), axis, backward)
        block = jnp.concatenate([low, block, high], axis=dim)
    return block


def face_traces(vector_in):
    leading = vector_in.shape[:-1]
    node_grid = vector_in.reshape(leading + (PTS, PTS, PTS, VARS))
    facets = [
        node_grid[..., :, :, 0, :],
        node_grid[..., :, :, PTS - 1, :],
        node_grid[..., :, 0, :, :],
        node_grid[..., :, PTS - 1, :, :],
    ]
    flattened = [one_facet.reshape(leading + (FACE,)) for one_facet in facets]
    return jnp.stack(flattened, -2).reshape(leading + (4 * FACE,))


def lateral_term(vector_in, padded, side_coupling, orientation):
    single_row_block, rows_two = (vector_in.shape[0], vector_in.shape[1])
    beside_all = padded.reshape(padded.shape[:3] + (4, FACE))
    across = jnp.stack(
        [
            beside_all[0:single_row_block, 1 : rows_two + 1, :, 1],
            beside_all[2 : single_row_block + 2, 1 : rows_two + 1, :, 0],
            beside_all[1 : single_row_block + 1, 0:rows_two, :, 3],
            beside_all[1 : single_row_block + 1, 2 : rows_two + 2, :, 2],
        ],
        3,
    )
    shaped = across.reshape(across.shape[:4] + (PTS, PTS, VARS))
    turned = jnp.zeros(shaped.shape, jnp.float32)
    for quarter in range(4):
        picked = (orientation == quarter).astype(jnp.float32)[..., None, None, None]
        turned = turned + picked * jnp.rot90(shaped, quarter, axes=(4, 5))
    coupled = jnp.einsum(
        "xyefab,xyefb->xyefa", side_coupling, turned.reshape(across.shape), precision=precise
    )
    pieces = coupled.reshape(across.shape[:4] + (PTS, PTS, VARS))
    result = jnp.zeros(vector_in.shape[:3] + (PTS, PTS, PTS, VARS), jnp.float32)
    result = result.at[:, :, :, :, :, 0, :].add(pieces[:, :, :, 0])
    result = result.at[:, :, :, :, :, PTS - 1, :].add(pieces[:, :, :, 1])
    result = result.at[:, :, :, :, 0, :, :].add(pieces[:, :, :, 2])
    result = result.at[:, :, :, :, PTS - 1, :, :].add(pieces[:, :, :, 3])
    return result.reshape(vector_in.shape)


def apply_map(matrix, vector):
    return jnp.einsum("xyab,xyb->xya", matrix, vector, precision=precise)


def compose(earlier, later):
    return (
        jnp.einsum("xyab,xybc->xyac", later[0], earlier[0], precision=precise),
        apply_map(later[0], earlier[1]) + later[1],
    )


def pass_lower(outgoing, lower_total, identity):
    mapped = entering(
        (lower_total, outgoing), "wall", compose, (identity, jnp.zeros_like(outgoing)), False
    )
    return mapped[1]


def pass_upper(outgoing, upper_total, identity):
    mapped = entering(
        (upper_total, outgoing), "wall", compose, (identity, jnp.zeros_like(outgoing)), True
    )
    return mapped[1]


def solve_small(matrix, vector):
    extent = matrix.shape[0]
    index_ids = jnp.arange(extent)
    for k in range(extent):
        factor_col = jnp.where(index_ids > k, matrix[:, k] / matrix[k, k], 0.0)
        matrix = matrix - factor_col[:, None] * matrix[k][None, :]
        vector = vector - factor_col * vector[k]
    solved = jnp.zeros((extent,), jnp.float32)
    for k in reversed(range(extent)):
        solved = solved.at[k].set((vector[k] - jnp.sum(matrix[k] * solved)) / matrix[k, k])
    return solved


def least_squares(hessenberg, initial_norm):
    target = jnp.zeros((hessenberg.shape[0],), jnp.float32).at[0].set(initial_norm)
    normal = jnp.dot(hessenberg.T, hessenberg, precision=precise)
    weights = solve_small(normal, jnp.dot(hessenberg.T, target, precision=precise))
    misfit = target - jnp.dot(hessenberg, weights, precision=precise)
    return (weights, jnp.sqrt(jnp.sum(misfit * misfit)) / initial_norm)


def allreduce(values):
    for axis in ("wall", "sx", "sy"):
        count = lax.axis_size(axis)
        step = 1
        while step < count:
            pairs = [(i, i ^ step) for i in range(count)]
            values = values + lax.ppermute(values, axis, pairs)
            step *= 2
    return values


def shards(forcing, pivot_inverse, lower_face, upper_face, side_coupling, orientation):
    elements = forcing.shape[2]
    lower_maps = -jnp.einsum(
        "xyeab,xyebc->xyeac",
        pivot_inverse[..., BLOCK - FACE :, :FACE],
        lower_face,
        precision=precise,
    )
    upper_maps = -jnp.einsum(
        "xyeab,xyebc->xyeac",
        pivot_inverse[..., :FACE, BLOCK - FACE :],
        upper_face,
        precision=precise,
    )
    identity = jnp.broadcast_to(jnp.eye(FACE, dtype=jnp.float32), forcing.shape[:2] + (FACE, FACE))
    lower_total = identity
    for i in range(elements):
        lower_total = jnp.einsum(
            "xyab,xybc->xyac", lower_maps[:, :, i], lower_total, precision=precise
        )
    upper_total = identity
    for i in reversed(range(elements)):
        upper_total = jnp.einsum(
            "xyab,xybc->xyac", upper_maps[:, :, i], upper_total, precision=precise
        )
    def precond(resid):
        ahead_part = jnp.einsum(
            "xyeab,xyeb->xyea", pivot_inverse[..., BLOCK - FACE :, :], resid, precision=precise
        )
        carried = jnp.zeros(resid.shape[:2] + (FACE,), jnp.float32)
        for precondition_i in range(elements):
            carried = ahead_part[:, :, precondition_i] + apply_map(
                lower_maps[:, :, precondition_i], carried
            )
        carried = pass_lower(carried, lower_total, identity)
        rows_out = []
        for precondition_i in range(elements):
            lowered = apply_map(lower_face[:, :, precondition_i], carried)
            rows_out.append(
                jnp.concatenate(
                    [
                        resid[:, :, precondition_i, :FACE] - lowered,
                        resid[:, :, precondition_i, FACE:],
                    ],
                    -1,
                )
            )
            carried = ahead_part[:, :, precondition_i] + apply_map(
                lower_maps[:, :, precondition_i], carried
            )
        reduced = jnp.stack(rows_out, 2)
        trailing_rows = jnp.einsum(
            "xyeab,xyeb->xyea", pivot_inverse[..., :FACE, :], reduced, precision=precise
        )
        carried = jnp.zeros(resid.shape[:2] + (FACE,), jnp.float32)
        for precondition_i in reversed(range(elements)):
            carried = trailing_rows[:, :, precondition_i] + apply_map(
                upper_maps[:, :, precondition_i], carried
            )
        carried = pass_upper(carried, upper_total, identity)
        rows_back = [None] * elements
        for precondition_i in reversed(range(elements)):
            raised = apply_map(upper_face[:, :, precondition_i], carried)
            rows_back[precondition_i] = jnp.concatenate(
                [
                    reduced[:, :, precondition_i, : BLOCK - FACE],
                    reduced[:, :, precondition_i, BLOCK - FACE :] - raised,
                ],
                -1,
            )
            carried = trailing_rows[:, :, precondition_i] + apply_map(
                upper_maps[:, :, precondition_i], carried
            )
        return jnp.einsum(
            "xyeab,xyeb->xyea", pivot_inverse, jnp.stack(rows_back, 2), precision=precise
        )

    def lateral(direction):
        traces = face_traces(direction)
        padded = extended(traces, (("sx", 0), ("sy", 1)), 1)
        return lateral_term(direction, padded, side_coupling, orientation)

    def dot(a, b):
        return jnp.sum(a * b)

    entry_count = forcing.size * lax.axis_size("wall") * lax.axis_size("sx") * lax.axis_size("sy")
    basis = [forcing]
    precon = []
    norms = []
    gram = {}
    columns = []
    squares = None
    for j in range(ITERS):
        current = basis[j]
        pre = precond(current)
        precon.append(pre)
        mapped = current + lateral(pre)
        partial = [dot(current, current)] + [dot(mapped, basis[i]) for i in range(j + 1)]
        partial += [dot(basis[i], current) for i in range(j)]
        total = allreduce(jnp.stack(partial))
        norm_sq = total[0]
        if j == 0:
            squares = norm_sq
        norms.append(jnp.sqrt(norm_sq))
        for i in range(j):
            gram[(i, j)] = total[2 + j + i] / (norms[i] * norms[j])
        listed = []
        for i in range(j + 1):
            projected = total[1 + i] / (norms[i] * norms[j])
            for l in range(i):
                projected = projected - listed[l] * gram[(l, i)]
            listed.append(projected)
        following = mapped / norms[j]
        for i in range(j + 1):
            following = following - (listed[i] / norms[i]) * basis[i]
        basis.append(following)
        columns.append(listed)
    last = allreduce(jnp.stack([dot(basis[ITERS], basis[ITERS])]))
    norms.append(jnp.sqrt(last[0]))
    full_columns = []
    for j in range(ITERS):
        full_columns.append(
            jnp.concatenate(
                [jnp.stack(columns[j]), norms[j + 1][None], jnp.zeros((ITERS - 1 - j,), jnp.float32)]
            )
        )
    hessenberg = jnp.stack(full_columns, 1)
    forcing_rms = jnp.sqrt(squares / entry_count)
    initial_norm = jnp.sqrt(squares)
    weights, relative = least_squares(hessenberg, initial_norm)
    solution = (weights[0] / norms[0]) * precon[0]
    for j in range(1, ITERS):
        solution = solution + (weights[j] / norms[j]) * precon[j]
    return (solution, relative, forcing_rms)


def solution(mesh):
    return jax.shard_map(
        shards,
        mesh=mesh,
        in_specs=(
            P("sx", "sy", "wall", None),
            P("sx", "sy", "wall", None, None),
            P("sx", "sy", "wall", None, None),
            P("sx", "sy", "wall", None, None),
            P("sx", "sy", "wall", None, None, None),
            P("sx", "sy", "wall", None),
        ),
        out_specs=(P("sx", "sy", "wall", None), P(), P()),
        check_vma=False,
    )
```

```python
import jax
import jax.numpy as jnp
from jax import lax
from jax.sharding import PartitionSpec as P

PTS = 4
VARS = 6
BLOCK = 384
FACE = 96
ITERS = 3


precise = lax.Precision.HIGHEST


def face_traces(vector_in):
    leading = vector_in.shape[:-1]
    node_grid = vector_in.reshape(leading + (PTS, PTS, PTS, VARS))
    facets = [
        node_grid[..., :, :, 0, :],
        node_grid[..., :, :, PTS - 1, :],
        node_grid[..., :, 0, :, :],
        node_grid[..., :, PTS - 1, :, :],
    ]
    flattened = [one_facet.reshape(leading + (FACE,)) for one_facet in facets]
    return jnp.stack(flattened, -2).reshape(leading + (4 * FACE,))


def mm(matrix, columns):
    return jnp.einsum("xyab,xybk->xyak", matrix, columns, precision=precise)


def lateral_from(direction, side_coupling, orientation):
    lead = direction.shape[:3]
    traces = face_traces(direction).reshape(lead + (4, FACE))
    sides = []
    for axis, dim, low_face, high_face in (("sx", 0, 1, 0), ("sy", 1, 3, 2)):
        count = lax.axis_size(axis)
        forward = [(i, i + 1) for i in range(count - 1)]
        backward = [(i + 1, i) for i in range(count - 1)]
        size = direction.shape[dim]
        last = lax.slice_in_dim(traces[..., low_face, :], size - 1, size, axis=dim)
        first = lax.slice_in_dim(traces[..., high_face, :], 0, 1, axis=dim)
        low = jnp.concatenate(
            [lax.ppermute(last, axis, forward), lax.slice_in_dim(traces[..., low_face, :], 0, size - 1, axis=dim)],
            axis=dim,
        )
        high = jnp.concatenate(
            [lax.slice_in_dim(traces[..., high_face, :], 1, size, axis=dim), lax.ppermute(first, axis, backward)],
            axis=dim,
        )
        sides += [low, high]
    across = jnp.stack(sides, 3)
    shaped = across.reshape(across.shape[:4] + (PTS, PTS, VARS))
    turned = jnp.zeros(shaped.shape, jnp.float32)
    for quarter in range(4):
        picked = (orientation == quarter).astype(jnp.float32)[..., None, None, None]
        turned = turned + picked * jnp.rot90(shaped, quarter, axes=(4, 5))
    coupled = jnp.einsum(
        "xyefab,xyefb->xyefa", side_coupling, turned.reshape(across.shape), precision=precise
    )
    pieces = coupled.reshape(across.shape[:4] + (PTS, PTS, VARS))
    result = jnp.zeros(lead + (PTS, PTS, PTS, VARS), jnp.float32)
    result = result.at[:, :, :, :, :, 0, :].add(pieces[:, :, :, 0])
    result = result.at[:, :, :, :, :, PTS - 1, :].add(pieces[:, :, :, 1])
    result = result.at[:, :, :, :, 0, :, :].add(pieces[:, :, :, 2])
    result = result.at[:, :, :, :, PTS - 1, :, :].add(pieces[:, :, :, 3])
    return result.reshape(direction.shape)


def line_maps(pivot_inverse, lower_face, upper_face):
    lead = pivot_inverse.shape[:2]
    elements = pivot_inverse.shape[2]
    from_below = -jnp.einsum(
        "xyeab,xyebc->xyeac", pivot_inverse[..., :FACE], lower_face, precision=precise
    )
    from_above = -jnp.einsum(
        "xyeab,xyebc->xyeac", pivot_inverse[..., BLOCK - FACE :], upper_face, precision=precise
    )
    lower_maps = from_below[..., BLOCK - FACE :, :]
    trail_maps = from_below[..., :FACE, :]
    upper_maps = from_above[..., :FACE, :]
    inputs = (2 + 2 * elements) * FACE
    unit = jnp.broadcast_to(jnp.eye(inputs, dtype=jnp.float32), lead + (inputs, inputs))
    pieces = unit.reshape(lead + (2 + 2 * elements, FACE, inputs))
    entering_low, entering_high = pieces[:, :, 0], pieces[:, :, 1]
    ahead = pieces[:, :, 2 : 2 + elements]
    trail0 = pieces[:, :, 2 + elements :]
    carried = entering_low
    before = []
    for i in range(elements):
        before.append(carried)
        carried = ahead[:, :, i] + mm(lower_maps[:, :, i], carried)
    leaving_high = carried
    trails = [trail0[:, :, i] + mm(trail_maps[:, :, i], before[i]) for i in range(elements)]
    carried = entering_high
    after = [None] * elements
    for i in reversed(range(elements)):
        after[i] = carried
        carried = trails[i] + mm(upper_maps[:, :, i], carried)
    leaving_low = carried
    carries = jnp.stack(before + after, 2)
    leaving = jnp.stack([leaving_high, leaving_low], 2)
    return from_below, from_above, carries, leaving


def wall_maps(leaving):
    axis = "wall"
    count = lax.axis_size(axis)
    lead = leaving.shape[:2]
    step = leaving[..., : 2 * FACE]
    gathered = lax.all_gather(step, axis)
    width = count * 2 * FACE
    unit = jnp.broadcast_to(jnp.eye(width, dtype=jnp.float32), lead + (width, width))
    pieces = unit.reshape(lead + (count, 2, FACE, width))
    low = [jnp.zeros(lead + (FACE, width), jnp.float32)]
    for d in range(count - 1):
        low.append(pieces[:, :, d, 0] + mm(gathered[d, :, :, 0, :, :FACE], low[d]))
    high = [None] * count
    high[count - 1] = jnp.zeros(lead + (FACE, width), jnp.float32)
    for d in range(count - 1, 0, -1):
        high[d - 1] = (
            pieces[:, :, d, 1]
            + mm(gathered[d, :, :, 1, :, FACE:], high[d])
            + mm(gathered[d, :, :, 1, :, :FACE], low[d])
        )
    table = jnp.stack([jnp.stack(low, 0), jnp.stack(high, 0)], 3)
    return lax.dynamic_index_in_dim(table, lax.axis_index(axis), 0, False)


def allreduce(values):
    for axis in ("wall", "sx", "sy"):
        count = lax.axis_size(axis)
        step = 1
        while step < count:
            pairs = [(i, i ^ step) for i in range(count)]
            values = values + lax.ppermute(values, axis, pairs)
            step *= 2
    return values


def solve_small(matrix, vector):
    extent = matrix.shape[0]
    index_ids = jnp.arange(extent)
    for k in range(extent):
        factor_col = jnp.where(index_ids > k, matrix[:, k] / matrix[k, k], 0.0)
        matrix = matrix - factor_col[:, None] * matrix[k][None, :]
        vector = vector - factor_col * vector[k]
    solved = jnp.zeros((extent,), jnp.float32)
    for k in reversed(range(extent)):
        solved = solved.at[k].set((vector[k] - jnp.sum(matrix[k] * solved)) / matrix[k, k])
    return solved


def least_squares(hessenberg, initial_norm):
    target = jnp.zeros((hessenberg.shape[0],), jnp.float32).at[0].set(initial_norm)
    normal = jnp.dot(hessenberg.T, hessenberg, precision=precise)
    weights = solve_small(normal, jnp.dot(hessenberg.T, target, precision=precise))
    misfit = target - jnp.dot(hessenberg, weights, precision=precise)
    return (weights, jnp.sqrt(jnp.sum(misfit * misfit)) / initial_norm)


def shards(forcing, pivot_inverse, lower_face, upper_face, side_coupling, orientation):
    lead = forcing.shape[:2]
    elements = forcing.shape[2]
    from_below, from_above, carries, leaving = line_maps(pivot_inverse, lower_face, upper_face)
    entry = wall_maps(leaving)
    local_leaving = leaving[..., 2 * FACE :]

    def precond(resid):
        rows = jnp.einsum("xyeab,xyeb->xyea", pivot_inverse, resid, precision=precise)
        local = jnp.concatenate(
            [rows[..., BLOCK - FACE :], rows[..., :FACE]], 2
        ).reshape(lead + (2 * elements * FACE,))
        outgoing = jnp.einsum("xysak,xyk->xysa", local_leaving, local, precision=precise)
        gathered = lax.all_gather(outgoing, "wall")
        gathered = jnp.moveaxis(gathered, 0, 2).reshape(lead + (-1,))
        entering = jnp.einsum("xysak,xyk->xysa", entry, gathered, precision=precise)
        full = jnp.concatenate([entering.reshape(lead + (2 * FACE,)), local], -1)
        faces = jnp.einsum("xyeak,xyk->xyea", carries, full, precision=precise)
        return (
            rows
            + jnp.einsum("xyeab,xyeb->xyea", from_below, faces[:, :, :elements], precision=precise)
            + jnp.einsum("xyeab,xyeb->xyea", from_above, faces[:, :, elements:], precision=precise)
        )

    def dot(a, b):
        return jnp.sum(a * b)

    entry_count = forcing.size * lax.axis_size("wall") * lax.axis_size("sx") * lax.axis_size("sy")
    basis = [forcing]
    precon = []
    norms = []
    gram = {}
    columns = []
    squares = None
    for j in range(ITERS):
        current = basis[j]
        pre = precond(current)
        precon.append(pre)
        mapped = current + lateral_from(pre, side_coupling, orientation)
        partial = [dot(current, current)] + [dot(mapped, basis[i]) for i in range(j + 1)]
        partial += [dot(basis[i], current) for i in range(j)]
        total = allreduce(jnp.stack(partial))
        norm_sq = total[0]
        if j == 0:
            squares = norm_sq
        norms.append(jnp.sqrt(norm_sq))
        for i in range(j):
            gram[(i, j)] = total[2 + j + i] / (norms[i] * norms[j])
        listed = []
        for i in range(j + 1):
            projected = total[1 + i] / (norms[i] * norms[j])
            for l in range(i):
                projected = projected - listed[l] * gram[(l, i)]
            listed.append(projected)
        following = mapped / norms[j]
        for i in range(j + 1):
            following = following - (listed[i] / norms[i]) * basis[i]
        basis.append(following)
        columns.append(listed)
    last = allreduce(jnp.stack([dot(basis[ITERS], basis[ITERS])]))
    norms.append(jnp.sqrt(last[0]))
    full_columns = []
    for j in range(ITERS):
        full_columns.append(
            jnp.concatenate(
                [jnp.stack(columns[j]), norms[j + 1][None], jnp.zeros((ITERS - 1 - j,), jnp.float32)]
            )
        )
    hessenberg = jnp.stack(full_columns, 1)
    forcing_rms = jnp.sqrt(squares / entry_count)
    initial_norm = jnp.sqrt(squares)
    weights, relative = least_squares(hessenberg, initial_norm)
    solution = (weights[0] / norms[0]) * precon[0]
    for j in range(1, ITERS):
        solution = solution + (weights[j] / norms[j]) * precon[j]
    return (solution, relative, forcing_rms)


def solution(mesh):
    return jax.shard_map(
        shards,
        mesh=mesh,
        in_specs=(
            P("sx", "sy", "wall", None),
            P("sx", "sy", "wall", None, None),
            P("sx", "sy", "wall", None, None),
            P("sx", "sy", "wall", None, None),
            P("sx", "sy", "wall", None, None, None),
            P("sx", "sy", "wall", None),
        ),
        out_specs=(P("sx", "sy", "wall", None), P(), P()),
        check_vma=False,
    )
```

```python
import numpy as np
import jax
import jax.numpy as jnp
from jax import lax
from jax.sharding import PartitionSpec as P

PTS = 4
VARS = 6
BLOCK = 384
FACE = 96
ITERS = 3


precise = lax.Precision.HIGHEST


def mm(matrix, columns):
    return jnp.einsum("xyab,xybk->xyak", matrix, columns, precision=precise)


def unit(size, shift=0):
    hidden = jnp.minimum(lax.axis_index("wall"), 0)
    rows = lax.broadcasted_iota(jnp.int32, (FACE, size), 0)
    cols = lax.broadcasted_iota(jnp.int32, (FACE, size), 1)
    return (cols == rows + shift + hidden).astype(jnp.float32)


def wall_gather(part, sums=None):
    axis = "wall"
    count = lax.axis_size(axis)
    place = lax.axis_index(axis)
    block = part[None]
    step = 1
    while step < count:
        pairs = [(i, i ^ step) for i in range(count)]
        flat = block.reshape(-1)
        if sums is not None:
            flat = jnp.concatenate([sums, flat])
        other = lax.ppermute(flat, axis, pairs)
        if sums is not None:
            sums = sums + other[: sums.shape[0]]
            other = other[sums.shape[0] :]
        other = other.reshape(block.shape)
        upper = (place // step) % 2 == 1
        block = jnp.where(
            upper, jnp.concatenate([other, block], 0), jnp.concatenate([block, other], 0)
        )
        step *= 2
    return block, sums


def allreduce(values, axes=("wall", "sx", "sy")):
    for axis in axes:
        count = lax.axis_size(axis)
        step = 1
        while step < count:
            pairs = [(i, i ^ step) for i in range(count)]
            values = values + lax.ppermute(values, axis, pairs)
            step *= 2
    return values


def lateral_maps(side_coupling, orientation):
    index = np.arange(FACE).reshape(PTS, PTS, VARS)
    picked = None
    for quarter in range(4):
        order = np.argsort(np.rot90(index, quarter, axes=(0, 1)).reshape(-1))
        turned = side_coupling[..., order]
        if picked is None:
            picked = turned
        else:
            picked = jnp.where((orientation == quarter)[..., None, None], turned, picked)
    nodes = np.arange(BLOCK).reshape(PTS, PTS, PTS, VARS)
    spots = [
        nodes[:, :, 0, :].reshape(-1),
        nodes[:, :, PTS - 1, :].reshape(-1),
        nodes[:, 0, :, :].reshape(-1),
        nodes[:, PTS - 1, :, :].reshape(-1),
    ]
    padded = jnp.concatenate([picked, jnp.zeros_like(picked[..., :1, :])], -2)
    placed = []
    for face in range(4):
        source = np.full((BLOCK,), FACE)
        source[spots[face]] = np.arange(FACE)
        placed.append(padded[..., face, source, :])
    return jnp.concatenate(placed, -1)


def neighbour(values, axis, dim, later):
    count = lax.axis_size(axis)
    size = values.shape[dim]
    if later:
        pairs = [(i + 1, i) for i in range(count - 1)]
        moved = lax.ppermute(lax.slice_in_dim(values, 0, 1, axis=dim), axis, pairs)
        return jnp.concatenate([lax.slice_in_dim(values, 1, size, axis=dim), moved], dim)
    pairs = [(i, i + 1) for i in range(count - 1)]
    moved = lax.ppermute(lax.slice_in_dim(values, size - 1, size, axis=dim), axis, pairs)
    return jnp.concatenate([moved, lax.slice_in_dim(values, 0, size - 1, axis=dim)], dim)


def lateral_from(direction, coupling):
    lead = direction.shape[:3]
    grid = direction.reshape(lead + (PTS, PTS, PTS, VARS))
    faces = [
        grid[..., :, :, 0, :],
        grid[..., :, :, PTS - 1, :],
        grid[..., :, 0, :, :],
        grid[..., :, PTS - 1, :, :],
    ]
    faces = [one.reshape(lead + (FACE,)) for one in faces]
    across = jnp.concatenate(
        [
            neighbour(faces[1], "sx", 0, False),
            neighbour(faces[0], "sx", 0, True),
            neighbour(faces[3], "sy", 1, False),
            neighbour(faces[2], "sy", 1, True),
        ],
        -1,
    )
    return jnp.einsum("xyeak,xyek->xyea", coupling, across, precision=precise)


def line_maps(pivot_inverse, lower_face, upper_face):
    lead = pivot_inverse.shape[:2]
    elements = pivot_inverse.shape[2]
    from_below = -jnp.einsum(
        "xyeab,xyebc->xyeac", pivot_inverse[..., :FACE], lower_face, precision=precise
    )
    from_above = -jnp.einsum(
        "xyeab,xyebc->xyeac", pivot_inverse[..., BLOCK - FACE :], upper_face, precision=precise
    )
    lower_maps = from_below[..., BLOCK - FACE :, :]
    trail_maps = from_below[..., :FACE, :]
    upper_maps = from_above[..., :FACE, :]
    inputs = (2 + 2 * elements) * FACE
    entering_low = unit(inputs, 0)
    entering_high = unit(inputs, FACE)
    ahead = [unit(inputs, (2 + i) * FACE) for i in range(elements)]
    trail0 = [unit(inputs, (2 + elements + i) * FACE) for i in range(elements)]
    carried = jnp.broadcast_to(entering_low, lead + entering_low.shape)
    before = []
    for i in range(elements):
        before.append(carried)
        carried = ahead[i] + mm(lower_maps[:, :, i], carried)
    leaving_high = carried
    trails = [trail0[i] + mm(trail_maps[:, :, i], before[i]) for i in range(elements)]
    carried = jnp.broadcast_to(entering_high, lead + entering_high.shape)
    after = [None] * elements
    for i in reversed(range(elements)):
        after[i] = carried
        carried = trails[i] + mm(upper_maps[:, :, i], carried)
    leaving_low = carried
    carries = jnp.stack(before + after, 2)
    leaving = jnp.stack([leaving_high, leaving_low], 2)
    return from_below, from_above, carries, leaving


def wall_maps(leaving):
    axis = "wall"
    count = lax.axis_size(axis)
    place = lax.axis_index(axis)
    lead = leaving.shape[:2]
    gathered, _ = wall_gather(leaving[..., : 2 * FACE])
    half = count * FACE
    low = [jnp.zeros(lead + (FACE, half), jnp.float32)]
    for d in range(count - 1):
        low.append(unit(half, d * FACE) + mm(gathered[d, :, :, 0, :, :FACE], low[d]))
    zeros = jnp.zeros(lead + (FACE, half), jnp.float32)
    picked_low = zeros
    for d in range(count):
        picked_low = jnp.where(place == d, low[d], picked_low)
    high = jnp.zeros(lead + (FACE, 2 * half), jnp.float32)
    picked_high = jnp.where(place == count - 1, high, high)
    for d in range(count - 1, 0, -1):
        high = mm(gathered[d, :, :, 1, :, FACE:], high) + jnp.concatenate(
            [
                mm(gathered[d, :, :, 1, :, :FACE], low[d]),
                jnp.broadcast_to(unit(half, d * FACE), lead + (FACE, half)),
            ],
            -1,
        )
        picked_high = jnp.where(place == d - 1, high, picked_high)
    picked_low = jnp.concatenate([picked_low, zeros], -1)
    return jnp.stack([picked_low, picked_high], 2)


def solve_small(matrix, vector):
    extent = matrix.shape[0]
    index_ids = jnp.arange(extent)
    for k in range(extent):
        factor_col = jnp.where(index_ids > k, matrix[:, k] / matrix[k, k], 0.0)
        matrix = matrix - factor_col[:, None] * matrix[k][None, :]
        vector = vector - factor_col * vector[k]
    solved = jnp.zeros((extent,), jnp.float32)
    for k in reversed(range(extent)):
        solved = solved.at[k].set((vector[k] - jnp.sum(matrix[k] * solved)) / matrix[k, k])
    return solved


def least_squares(hessenberg, initial_norm):
    target = jnp.zeros((hessenberg.shape[0],), jnp.float32).at[0].set(initial_norm)
    normal = jnp.dot(hessenberg.T, hessenberg, precision=precise)
    weights = solve_small(normal, jnp.dot(hessenberg.T, target, precision=precise))
    misfit = target - jnp.dot(hessenberg, weights, precision=precise)
    return (weights, jnp.sqrt(jnp.sum(misfit * misfit)) / initial_norm)


def shards(forcing, pivot_inverse, lower_face, upper_face, side_coupling, orientation):
    lead = forcing.shape[:2]
    elements = forcing.shape[2]
    from_below, from_above, carries, leaving = line_maps(pivot_inverse, lower_face, upper_face)
    entry = wall_maps(leaving)
    coupling = lateral_maps(side_coupling, orientation)
    split = leaving[..., 2 * FACE :].reshape(lead + (2, FACE, 2, elements, FACE))
    chosen = jnp.stack([pivot_inverse[..., BLOCK - FACE :, :], pivot_inverse[..., :FACE, :]], 3)
    outward = jnp.einsum(
        "xysawec,xyewcb->xysaeb", split, chosen, precision=precise
    ).reshape(lead + (2 * FACE, elements * BLOCK))

    def outgoing(vector):
        return jnp.einsum(
            "xyok,xyk->xyo", outward, vector.reshape(lead + (-1,)), precision=precise
        )

    def flat_gather(block):
        count = block.shape[0]
        block = block.reshape((count,) + lead + (2, FACE))
        return jnp.transpose(block, (1, 2, 3, 0, 4)).reshape(lead + (-1,))

    def precond(resid, gathered):
        rows = jnp.einsum("xyeab,xyeb->xyea", pivot_inverse, resid, precision=precise)
        local = jnp.concatenate(
            [rows[..., BLOCK - FACE :], rows[..., :FACE]], 2
        ).reshape(lead + (2 * elements * FACE,))
        entering = jnp.einsum("xysak,xyk->xysa", entry, gathered, precision=precise)
        full = jnp.concatenate([entering.reshape(lead + (2 * FACE,)), local], -1)
        faces = jnp.einsum("xyeak,xyk->xyea", carries, full, precision=precise)
        return (
            rows
            + jnp.einsum("xyeab,xyeb->xyea", from_below, faces[:, :, :elements], precision=precise)
            + jnp.einsum("xyeab,xyeb->xyea", from_above, faces[:, :, elements:], precision=precise)
        )

    def dot(a, b):
        return jnp.sum(a * b)

    entry_count = forcing.size * lax.axis_size("wall") * lax.axis_size("sx") * lax.axis_size("sy")
    basis = [forcing]
    first, _ = wall_gather(outgoing(forcing))
    spread = [flat_gather(first)]
    precon = []
    norms = []
    gram = {}
    columns = []
    squares = None
    for j in range(ITERS):
        current = basis[j]
        pre = precond(current, spread[j])
        precon.append(pre)
        mapped = current + lateral_from(pre, coupling)
        partial = [dot(current, current)] + [dot(mapped, basis[i]) for i in range(j + 1)]
        partial += [dot(basis[i], current) for i in range(j)]
        partial = jnp.stack(partial)
        if j + 1 < ITERS:
            mapped_out, partial = wall_gather(outgoing(mapped), partial)
            total = allreduce(partial, ("sx", "sy"))
        else:
            total = allreduce(partial)
        norm_sq = total[0]
        if j == 0:
            squares = norm_sq
        norms.append(jnp.sqrt(norm_sq))
        for i in range(j):
            gram[(i, j)] = total[2 + j + i] / (norms[i] * norms[j])
        listed = []
        for i in range(j + 1):
            projected = total[1 + i] / (norms[i] * norms[j])
            for l in range(i):
                projected = projected - listed[l] * gram[(l, i)]
            listed.append(projected)
        following = mapped / norms[j]
        for i in range(j + 1):
            following = following - (listed[i] / norms[i]) * basis[i]
        basis.append(following)
        if j + 1 < ITERS:
            moved = flat_gather(mapped_out) / norms[j]
            for i in range(j + 1):
                moved = moved - (listed[i] / norms[i]) * spread[i]
            spread.append(moved)
        columns.append(listed)
    last = allreduce(jnp.stack([dot(basis[ITERS], basis[ITERS])]))
    norms.append(jnp.sqrt(last[0]))
    full_columns = []
    for j in range(ITERS):
        full_columns.append(
            jnp.concatenate(
                [jnp.stack(columns[j]), norms[j + 1][None], jnp.zeros((ITERS - 1 - j,), jnp.float32)]
            )
        )
    hessenberg = jnp.stack(full_columns, 1)
    forcing_rms = jnp.sqrt(squares / entry_count)
    initial_norm = jnp.sqrt(squares)
    weights, relative = least_squares(hessenberg, initial_norm)
    solution = (weights[0] / norms[0]) * precon[0]
    for j in range(1, ITERS):
        solution = solution + (weights[j] / norms[j]) * precon[j]
    return (solution, relative, forcing_rms)


def solution(mesh):
    return jax.shard_map(
        shards,
        mesh=mesh,
        in_specs=(
            P("sx", "sy", "wall", None),
            P("sx", "sy", "wall", None, None),
            P("sx", "sy", "wall", None, None),
            P("sx", "sy", "wall", None, None),
            P("sx", "sy", "wall", None, None, None),
            P("sx", "sy", "wall", None),
        ),
        out_specs=(P("sx", "sy", "wall", None), P(), P()),
        check_vma=False,
    )
```

```python
import numpy as np
import jax
import jax.numpy as jnp
from jax import lax
from jax.sharding import PartitionSpec as P

PTS = 4
VARS = 6
BLOCK = 384
FACE = 96
ITERS = 3


precise = lax.Precision.HIGHEST


def mm(matrix, columns):
    return jnp.einsum("xyab,xybk->xyak", matrix, columns, precision=precise)


def unit(size, shift=0):
    hidden = jnp.minimum(lax.axis_index("wall"), 0)
    rows = lax.broadcasted_iota(jnp.int32, (FACE, size), 0)
    cols = lax.broadcasted_iota(jnp.int32, (FACE, size), 1)
    return (cols == rows + shift + hidden).astype(jnp.float32)


def wall_gather(part, sums=None):
    axis = "wall"
    count = lax.axis_size(axis)
    place = lax.axis_index(axis)
    block = part[None]
    step = 1
    while step < count:
        pairs = [(i, i ^ step) for i in range(count)]
        flat = block.reshape(-1)
        if sums is not None:
            flat = jnp.concatenate([sums, flat])
        other = lax.ppermute(flat, axis, pairs)
        if sums is not None:
            sums = sums + other[: sums.shape[0]]
            other = other[sums.shape[0] :]
        other = other.reshape(block.shape)
        upper = (place // step) % 2 == 1
        block = jnp.where(
            upper, jnp.concatenate([other, block], 0), jnp.concatenate([block, other], 0)
        )
        step *= 2
    return block, sums


def allreduce(values, axes=("wall", "sx", "sy")):
    for axis in axes:
        count = lax.axis_size(axis)
        step = 1
        while step < count:
            pairs = [(i, i ^ step) for i in range(count)]
            values = values + lax.ppermute(values, axis, pairs)
            step *= 2
    return values


def mv(matrix, vector):
    return jnp.sum(matrix * vector[..., None, :], -1)


def lateral_maps(side_coupling, orientation):
    grid = side_coupling.reshape(side_coupling.shape[:-1] + (PTS, PTS, VARS))
    picked = None
    for quarter in range(4):
        turned = jnp.rot90(grid, -quarter, axes=(-3, -2)).reshape(side_coupling.shape)
        if picked is None:
            picked = turned
        else:
            picked = jnp.where((orientation == quarter)[..., None, None], turned, picked)
    lead = picked.shape[:3]
    none = [(0, 0)] * len(lead)
    placed = []
    for face, (shape, gap) in enumerate(
        [
            ((PTS, PTS, 1), (0, 0, (0, PTS - 1))),
            ((PTS, PTS, 1), (0, 0, (PTS - 1, 0))),
            ((PTS, 1, PTS), (0, (0, PTS - 1), 0)),
            ((PTS, 1, PTS), (0, (PTS - 1, 0), 0)),
        ]
    ):
        one = picked[..., face, :, :].reshape(lead + shape + (VARS, FACE))
        widths = none + [g if g else (0, 0) for g in gap] + [(0, 0), (0, 0)]
        placed.append(jnp.pad(one, widths).reshape(lead + (BLOCK, FACE)))
    return jnp.concatenate(placed, -1)


def neighbour(values, axis, dim, later):
    count = lax.axis_size(axis)
    size = values.shape[dim]
    if later:
        pairs = [(i + 1, i) for i in range(count - 1)]
        moved = lax.ppermute(lax.slice_in_dim(values, 0, 1, axis=dim), axis, pairs)
        return jnp.concatenate([lax.slice_in_dim(values, 1, size, axis=dim), moved], dim)
    pairs = [(i, i + 1) for i in range(count - 1)]
    moved = lax.ppermute(lax.slice_in_dim(values, size - 1, size, axis=dim), axis, pairs)
    return jnp.concatenate([moved, lax.slice_in_dim(values, 0, size - 1, axis=dim)], dim)


def lateral_from(direction, coupling):
    lead = direction.shape[:3]
    grid = direction.reshape(lead + (PTS, PTS, PTS, VARS))
    faces = [
        grid[..., :, :, 0, :],
        grid[..., :, :, PTS - 1, :],
        grid[..., :, 0, :, :],
        grid[..., :, PTS - 1, :, :],
    ]
    faces = [one.reshape(lead + (FACE,)) for one in faces]
    across = jnp.concatenate(
        [
            neighbour(faces[1], "sx", 0, False),
            neighbour(faces[0], "sx", 0, True),
            neighbour(faces[3], "sy", 1, False),
            neighbour(faces[2], "sy", 1, True),
        ],
        -1,
    )
    return mv(coupling, across)


def line_maps(pivot_inverse, lower_face, upper_face):
    lead = pivot_inverse.shape[:2]
    elements = pivot_inverse.shape[2]
    from_below = -jnp.einsum(
        "xyeab,xyebc->xyeac", pivot_inverse[..., :FACE], lower_face, precision=precise
    )
    from_above = -jnp.einsum(
        "xyeab,xyebc->xyeac", pivot_inverse[..., BLOCK - FACE :], upper_face, precision=precise
    )
    lower_maps = from_below[..., BLOCK - FACE :, :]
    trail_maps = from_below[..., :FACE, :]
    upper_maps = from_above[..., :FACE, :]
    inputs = (2 + 2 * elements) * FACE
    entering_low = unit(inputs, 0)
    entering_high = unit(inputs, FACE)
    ahead = [unit(inputs, (2 + i) * FACE) for i in range(elements)]
    trail0 = [unit(inputs, (2 + elements + i) * FACE) for i in range(elements)]
    carried = jnp.broadcast_to(entering_low, lead + entering_low.shape)
    before = []
    for i in range(elements):
        before.append(carried)
        carried = ahead[i] + mm(lower_maps[:, :, i], carried)
    leaving_high = carried
    trails = [trail0[i] + mm(trail_maps[:, :, i], before[i]) for i in range(elements)]
    carried = jnp.broadcast_to(entering_high, lead + entering_high.shape)
    after = [None] * elements
    for i in reversed(range(elements)):
        after[i] = carried
        carried = trails[i] + mm(upper_maps[:, :, i], carried)
    leaving_low = carried
    carries = jnp.stack(before + after, 2)
    leaving = jnp.stack([leaving_high, leaving_low], 2)
    return from_below, from_above, carries, leaving


def wall_maps(leaving):
    axis = "wall"
    count = lax.axis_size(axis)
    place = lax.axis_index(axis)
    lead = leaving.shape[:2]
    gathered, _ = wall_gather(leaving[..., : 2 * FACE])
    half = count * FACE
    low = [jnp.zeros(lead + (FACE, half), jnp.float32)]
    for d in range(count - 1):
        low.append(unit(half, d * FACE) + mm(gathered[d, :, :, 0, :, :FACE], low[d]))
    zeros = jnp.zeros(lead + (FACE, half), jnp.float32)
    picked_low = zeros
    for d in range(count):
        picked_low = jnp.where(place == d, low[d], picked_low)
    high = jnp.zeros(lead + (FACE, 2 * half), jnp.float32)
    picked_high = jnp.where(place == count - 1, high, high)
    for d in range(count - 1, 0, -1):
        high = mm(gathered[d, :, :, 1, :, FACE:], high) + jnp.concatenate(
            [
                mm(gathered[d, :, :, 1, :, :FACE], low[d]),
                jnp.broadcast_to(unit(half, d * FACE), lead + (FACE, half)),
            ],
            -1,
        )
        picked_high = jnp.where(place == d - 1, high, picked_high)
    picked_low = jnp.concatenate([picked_low, zeros], -1)
    return jnp.stack([picked_low, picked_high], 2)


def solve_small(matrix, vector):
    extent = matrix.shape[0]
    index_ids = jnp.arange(extent)
    for k in range(extent):
        factor_col = jnp.where(index_ids > k, matrix[:, k] / matrix[k, k], 0.0)
        matrix = matrix - factor_col[:, None] * matrix[k][None, :]
        vector = vector - factor_col * vector[k]
    solved = jnp.zeros((extent,), jnp.float32)
    for k in reversed(range(extent)):
        solved = solved.at[k].set((vector[k] - jnp.sum(matrix[k] * solved)) / matrix[k, k])
    return solved


def least_squares(hessenberg, initial_norm):
    target = jnp.zeros((hessenberg.shape[0],), jnp.float32).at[0].set(initial_norm)
    normal = jnp.dot(hessenberg.T, hessenberg, precision=precise)
    weights = solve_small(normal, jnp.dot(hessenberg.T, target, precision=precise))
    misfit = target - jnp.dot(hessenberg, weights, precision=precise)
    return (weights, jnp.sqrt(jnp.sum(misfit * misfit)) / initial_norm)


def shards(forcing, pivot_inverse, lower_face, upper_face, side_coupling, orientation):
    lead = forcing.shape[:2]
    elements = forcing.shape[2]
    from_below, from_above, carries, leaving = line_maps(pivot_inverse, lower_face, upper_face)
    entry = wall_maps(leaving)
    coupling = lateral_maps(side_coupling, orientation)
    split = leaving[..., 2 * FACE :].reshape(lead + (2, FACE, 2, elements, FACE))
    chosen = jnp.stack([pivot_inverse[..., BLOCK - FACE :, :], pivot_inverse[..., :FACE, :]], 3)
    outward = jnp.einsum(
        "xysawec,xyewcb->xysaeb", split, chosen, precision=precise
    ).reshape(lead + (2 * FACE, elements * BLOCK))

    def outgoing(vector):
        return mv(outward, vector.reshape(lead + (-1,)))

    def flat_gather(block):
        count = block.shape[0]
        block = block.reshape((count,) + lead + (2, FACE))
        return jnp.transpose(block, (1, 2, 3, 0, 4)).reshape(lead + (-1,))

    def precond(resid, gathered):
        rows = mv(pivot_inverse, resid)
        local = jnp.concatenate(
            [rows[..., BLOCK - FACE :], rows[..., :FACE]], 2
        ).reshape(lead + (2 * elements * FACE,))
        entering = mv(entry, gathered[:, :, None])
        full = jnp.concatenate([entering.reshape(lead + (2 * FACE,)), local], -1)
        faces = mv(carries, full[:, :, None])
        return (
            rows
            + mv(from_below, faces[:, :, :elements])
            + mv(from_above, faces[:, :, elements:])
        )

    def dot(a, b):
        return jnp.sum(a * b)

    entry_count = forcing.size * lax.axis_size("wall") * lax.axis_size("sx") * lax.axis_size("sy")
    basis = [forcing]
    first, _ = wall_gather(outgoing(forcing))
    spread = [flat_gather(first)]
    precon = []
    norms = []
    gram = {}
    columns = []
    squares = None
    for j in range(ITERS):
        current = basis[j]
        pre = precond(current, spread[j])
        precon.append(pre)
        mapped = current + lateral_from(pre, coupling)
        partial = [dot(current, current)] + [dot(mapped, basis[i]) for i in range(j + 1)]
        partial += [dot(basis[i], current) for i in range(j)]
        partial = jnp.stack(partial)
        if j + 1 < ITERS:
            mapped_out, partial = wall_gather(outgoing(mapped), partial)
            total = allreduce(partial, ("sx", "sy"))
        else:
            total = allreduce(partial)
        norm_sq = total[0]
        if j == 0:
            squares = norm_sq
        norms.append(jnp.sqrt(norm_sq))
        for i in range(j):
            gram[(i, j)] = total[2 + j + i] / (norms[i] * norms[j])
        listed = []
        for i in range(j + 1):
            projected = total[1 + i] / (norms[i] * norms[j])
            for l in range(i):
                projected = projected - listed[l] * gram[(l, i)]
            listed.append(projected)
        following = mapped / norms[j]
        for i in range(j + 1):
            following = following - (listed[i] / norms[i]) * basis[i]
        basis.append(following)
        if j + 1 < ITERS:
            moved = flat_gather(mapped_out) / norms[j]
            for i in range(j + 1):
                moved = moved - (listed[i] / norms[i]) * spread[i]
            spread.append(moved)
        columns.append(listed)
    last = allreduce(jnp.stack([dot(basis[ITERS], basis[ITERS])]))
    norms.append(jnp.sqrt(last[0]))
    full_columns = []
    for j in range(ITERS):
        full_columns.append(
            jnp.concatenate(
                [jnp.stack(columns[j]), norms[j + 1][None], jnp.zeros((ITERS - 1 - j,), jnp.float32)]
            )
        )
    hessenberg = jnp.stack(full_columns, 1)
    forcing_rms = jnp.sqrt(squares / entry_count)
    initial_norm = jnp.sqrt(squares)
    weights, relative = least_squares(hessenberg, initial_norm)
    solution = (weights[0] / norms[0]) * precon[0]
    for j in range(1, ITERS):
        solution = solution + (weights[j] / norms[j]) * precon[j]
    return (solution, relative, forcing_rms)


def solution(mesh):
    return jax.shard_map(
        shards,
        mesh=mesh,
        in_specs=(
            P("sx", "sy", "wall", None),
            P("sx", "sy", "wall", None, None),
            P("sx", "sy", "wall", None, None),
            P("sx", "sy", "wall", None, None),
            P("sx", "sy", "wall", None, None, None),
            P("sx", "sy", "wall", None),
        ),
        out_specs=(P("sx", "sy", "wall", None), P(), P()),
        check_vma=False,
    )
```

```python
import numpy as np
import jax
import jax.numpy as jnp
from jax import lax
from jax.sharding import PartitionSpec as P

PTS = 4
VARS = 6
BLOCK = 384
FACE = 96
ITERS = 3


precise = lax.Precision.HIGHEST


def mm(matrix, columns):
    return jnp.einsum("xyab,xybk->xyak", matrix, columns, precision=precise)


def unit(size, shift=0):
    hidden = jnp.minimum(lax.axis_index("wall"), 0)
    rows = lax.broadcasted_iota(jnp.int32, (FACE, size), 0)
    cols = lax.broadcasted_iota(jnp.int32, (FACE, size), 1)
    return (cols == rows + shift + hidden).astype(jnp.float32)


def wall_gather(part, sums=None):
    axis = "wall"
    count = lax.axis_size(axis)
    place = lax.axis_index(axis)
    block = part[None]
    step = 1
    while step < count:
        pairs = [(i, i ^ step) for i in range(count)]
        flat = block.reshape(-1)
        if sums is not None:
            flat = jnp.concatenate([sums, flat])
        other = lax.ppermute(flat, axis, pairs)
        if sums is not None:
            sums = sums + other[: sums.shape[0]]
            other = other[sums.shape[0] :]
        other = other.reshape(block.shape)
        upper = (place // step) % 2 == 1
        block = jnp.where(
            upper, jnp.concatenate([other, block], 0), jnp.concatenate([block, other], 0)
        )
        step *= 2
    return block, sums


def allreduce(values, axes=("wall", "sx", "sy")):
    for axis in axes:
        count = lax.axis_size(axis)
        step = 1
        while step < count:
            pairs = [(i, i ^ step) for i in range(count)]
            values = values + lax.ppermute(values, axis, pairs)
            step *= 2
    return values


def mv(matrix, vector):
    return jnp.sum(matrix * vector[..., None, :], -1)


def lateral_maps(side_coupling, orientation):
    grid = side_coupling.reshape(side_coupling.shape[:-1] + (PTS, PTS, VARS))
    picked = None
    for quarter in range(4):
        turned = jnp.rot90(grid, -quarter, axes=(-3, -2)).reshape(side_coupling.shape)
        if picked is None:
            picked = turned
        else:
            picked = jnp.where((orientation == quarter)[..., None, None], turned, picked)
    lead = picked.shape[:3]
    none = [(0, 0)] * len(lead)
    placed = []
    for face, (shape, gap) in enumerate(
        [
            ((PTS, PTS, 1), (0, 0, (0, PTS - 1))),
            ((PTS, PTS, 1), (0, 0, (PTS - 1, 0))),
            ((PTS, 1, PTS), (0, (0, PTS - 1), 0)),
            ((PTS, 1, PTS), (0, (PTS - 1, 0), 0)),
        ]
    ):
        one = picked[..., face, :, :].reshape(lead + shape + (VARS, FACE))
        widths = none + [g if g else (0, 0) for g in gap] + [(0, 0), (0, 0)]
        placed.append(jnp.pad(one, widths).reshape(lead + (BLOCK, FACE)))
    return jnp.concatenate(placed, -1)


def neighbour(values, axis, dim, later):
    count = lax.axis_size(axis)
    size = values.shape[dim]
    if later:
        pairs = [(i + 1, i) for i in range(count - 1)]
        moved = lax.ppermute(lax.slice_in_dim(values, 0, 1, axis=dim), axis, pairs)
        return jnp.concatenate([lax.slice_in_dim(values, 1, size, axis=dim), moved], dim)
    pairs = [(i, i + 1) for i in range(count - 1)]
    moved = lax.ppermute(lax.slice_in_dim(values, size - 1, size, axis=dim), axis, pairs)
    return jnp.concatenate([moved, lax.slice_in_dim(values, 0, size - 1, axis=dim)], dim)


def lateral_from(direction, coupling):
    lead = direction.shape[:3]
    grid = direction.reshape(lead + (PTS, PTS, PTS, VARS))
    faces = [
        grid[..., :, :, 0, :],
        grid[..., :, :, PTS - 1, :],
        grid[..., :, 0, :, :],
        grid[..., :, PTS - 1, :, :],
    ]
    faces = [one.reshape(lead + (FACE,)) for one in faces]
    across = jnp.concatenate(
        [
            neighbour(faces[1], "sx", 0, False),
            neighbour(faces[0], "sx", 0, True),
            neighbour(faces[3], "sy", 1, False),
            neighbour(faces[2], "sy", 1, True),
        ],
        -1,
    )
    return mv(coupling, across)


def line_maps(pivot_inverse, lower_face, upper_face):
    lead = pivot_inverse.shape[:2]
    elements = pivot_inverse.shape[2]
    from_below = -jnp.einsum(
        "xyeab,xyebc->xyeac", pivot_inverse[..., :FACE], lower_face, precision=precise
    )
    from_above = -jnp.einsum(
        "xyeab,xyebc->xyeac", pivot_inverse[..., BLOCK - FACE :], upper_face, precision=precise
    )
    lower_maps = from_below[..., BLOCK - FACE :, :]
    trail_maps = from_below[..., :FACE, :]
    upper_maps = from_above[..., :FACE, :]
    inputs = (2 + 2 * elements) * FACE
    entering_low = unit(inputs, 0)
    entering_high = unit(inputs, FACE)
    ahead = [unit(inputs, (2 + i) * FACE) for i in range(elements)]
    trail0 = [unit(inputs, (2 + elements + i) * FACE) for i in range(elements)]
    carried = jnp.broadcast_to(entering_low, lead + entering_low.shape)
    before = []
    for i in range(elements):
        before.append(carried)
        carried = ahead[i] + mm(lower_maps[:, :, i], carried)
    leaving_high = carried
    trails = [trail0[i] + mm(trail_maps[:, :, i], before[i]) for i in range(elements)]
    carried = jnp.broadcast_to(entering_high, lead + entering_high.shape)
    after = [None] * elements
    for i in reversed(range(elements)):
        after[i] = carried
        carried = trails[i] + mm(upper_maps[:, :, i], carried)
    leaving_low = carried
    carries = jnp.stack(before + after, 2)
    leaving = jnp.stack([leaving_high, leaving_low], 2)
    return from_below, from_above, carries, leaving


def wall_maps(leaving):
    axis = "wall"
    count = lax.axis_size(axis)
    place = lax.axis_index(axis)
    lead = leaving.shape[:2]
    needed = jnp.stack(
        [leaving[..., 0, :, :FACE], leaving[..., 1, :, FACE : 2 * FACE], leaving[..., 1, :, :FACE]], 2
    )
    gathered = lax.all_gather(needed, axis)
    half = count * FACE
    low = [jnp.zeros(lead + (FACE, half), jnp.float32)]
    for d in range(count - 1):
        low.append(unit(half, d * FACE) + mm(gathered[d, :, :, 0], low[d]))
    zeros = jnp.zeros(lead + (FACE, half), jnp.float32)
    picked_low = zeros
    for d in range(count):
        picked_low = jnp.where(place == d, low[d], picked_low)
    high = jnp.zeros(lead + (FACE, 2 * half), jnp.float32)
    picked_high = jnp.where(place == count - 1, high, high)
    for d in range(count - 1, 0, -1):
        high = mm(gathered[d, :, :, 1], high) + jnp.concatenate(
            [
                mm(gathered[d, :, :, 2], low[d]),
                jnp.broadcast_to(unit(half, d * FACE), lead + (FACE, half)),
            ],
            -1,
        )
        picked_high = jnp.where(place == d - 1, high, picked_high)
    picked_low = jnp.concatenate([picked_low, zeros], -1)
    return jnp.stack([picked_low, picked_high], 2)


def solve_small(matrix, vector):
    extent = matrix.shape[0]
    index_ids = jnp.arange(extent)
    for k in range(extent):
        factor_col = jnp.where(index_ids > k, matrix[:, k] / matrix[k, k], 0.0)
        matrix = matrix - factor_col[:, None] * matrix[k][None, :]
        vector = vector - factor_col * vector[k]
    solved = jnp.zeros((extent,), jnp.float32)
    for k in reversed(range(extent)):
        solved = solved.at[k].set((vector[k] - jnp.sum(matrix[k] * solved)) / matrix[k, k])
    return solved


def least_squares(hessenberg, initial_norm):
    target = jnp.zeros((hessenberg.shape[0],), jnp.float32).at[0].set(initial_norm)
    normal = jnp.dot(hessenberg.T, hessenberg, precision=precise)
    weights = solve_small(normal, jnp.dot(hessenberg.T, target, precision=precise))
    misfit = target - jnp.dot(hessenberg, weights, precision=precise)
    return (weights, jnp.sqrt(jnp.sum(misfit * misfit)) / initial_norm)


def shards(forcing, pivot_inverse, lower_face, upper_face, side_coupling, orientation):
    lead = forcing.shape[:2]
    elements = forcing.shape[2]
    from_below, from_above, carries, leaving = line_maps(pivot_inverse, lower_face, upper_face)
    entry = wall_maps(leaving)
    coupling = lateral_maps(side_coupling, orientation)
    local_leaving = leaving[..., 2 * FACE :]

    def local_of(rows):
        return jnp.concatenate(
            [rows[..., BLOCK - FACE :], rows[..., :FACE]], 2
        ).reshape(lead + (2 * elements * FACE,))

    def outgoing(rows):
        return mv(local_leaving, local_of(rows)[:, :, None]).reshape(lead + (2 * FACE,))

    def flat_gather(block):
        count = block.shape[0]
        block = block.reshape((count,) + lead + (2, FACE))
        return jnp.transpose(block, (1, 2, 3, 0, 4)).reshape(lead + (-1,))

    def precond(rows, gathered):
        local = local_of(rows)
        entering = mv(entry, gathered[:, :, None])
        full = jnp.concatenate([entering.reshape(lead + (2 * FACE,)), local], -1)
        faces = mv(carries, full[:, :, None])
        return (
            rows
            + mv(from_below, faces[:, :, :elements])
            + mv(from_above, faces[:, :, elements:])
        )

    def dot(a, b):
        return jnp.sum(a * b)

    entry_count = forcing.size * lax.axis_size("wall") * lax.axis_size("sx") * lax.axis_size("sy")
    basis = [forcing]
    images = [mv(pivot_inverse, forcing)]
    first, _ = wall_gather(outgoing(images[0]))
    spread = [flat_gather(first)]
    precon = []
    norms = []
    gram = {}
    columns = []
    squares = None
    for j in range(ITERS):
        current = basis[j]
        pre = precond(images[j], spread[j])
        precon.append(pre)
        mapped = current + lateral_from(pre, coupling)
        partial = [dot(current, current)] + [dot(mapped, basis[i]) for i in range(j + 1)]
        partial += [dot(basis[i], current) for i in range(j)]
        partial = jnp.stack(partial)
        if j + 1 < ITERS:
            mapped_rows = mv(pivot_inverse, mapped)
            mapped_out, partial = wall_gather(outgoing(mapped_rows), partial)
            total = allreduce(partial, ("sx", "sy"))
        else:
            total = allreduce(partial)
        norm_sq = total[0]
        if j == 0:
            squares = norm_sq
        norms.append(jnp.sqrt(norm_sq))
        for i in range(j):
            gram[(i, j)] = total[2 + j + i] / (norms[i] * norms[j])
        listed = []
        for i in range(j + 1):
            projected = total[1 + i] / (norms[i] * norms[j])
            for l in range(i):
                projected = projected - listed[l] * gram[(l, i)]
            listed.append(projected)
        following = mapped / norms[j]
        for i in range(j + 1):
            following = following - (listed[i] / norms[i]) * basis[i]
        basis.append(following)
        if j + 1 < ITERS:
            moved = flat_gather(mapped_out) / norms[j]
            image = mapped_rows / norms[j]
            for i in range(j + 1):
                moved = moved - (listed[i] / norms[i]) * spread[i]
                image = image - (listed[i] / norms[i]) * images[i]
            spread.append(moved)
            images.append(image)
        columns.append(listed)
    last = allreduce(jnp.stack([dot(basis[ITERS], basis[ITERS])]))
    norms.append(jnp.sqrt(last[0]))
    full_columns = []
    for j in range(ITERS):
        full_columns.append(
            jnp.concatenate(
                [jnp.stack(columns[j]), norms[j + 1][None], jnp.zeros((ITERS - 1 - j,), jnp.float32)]
            )
        )
    hessenberg = jnp.stack(full_columns, 1)
    forcing_rms = jnp.sqrt(squares / entry_count)
    initial_norm = jnp.sqrt(squares)
    weights, relative = least_squares(hessenberg, initial_norm)
    solution = (weights[0] / norms[0]) * precon[0]
    for j in range(1, ITERS):
        solution = solution + (weights[j] / norms[j]) * precon[j]
    return (solution, relative, forcing_rms)


def solution(mesh):
    return jax.shard_map(
        shards,
        mesh=mesh,
        in_specs=(
            P("sx", "sy", "wall", None),
            P("sx", "sy", "wall", None, None),
            P("sx", "sy", "wall", None, None),
            P("sx", "sy", "wall", None, None),
            P("sx", "sy", "wall", None, None, None),
            P("sx", "sy", "wall", None),
        ),
        out_specs=(P("sx", "sy", "wall", None), P(), P()),
        check_vma=False,
    )
```

```python
import numpy as np
import jax
import jax.numpy as jnp
from jax import lax
from jax.sharding import PartitionSpec as P

PTS = 4
VARS = 6
BLOCK = 384
FACE = 96
ITERS = 3


precise = lax.Precision.HIGHEST


def mm(matrix, columns):
    return jnp.einsum("xyab,xybk->xyak", matrix, columns, precision=precise)


def unit(size, shift=0):
    hidden = jnp.minimum(lax.axis_index("wall"), 0)
    rows = lax.broadcasted_iota(jnp.int32, (FACE, size), 0)
    cols = lax.broadcasted_iota(jnp.int32, (FACE, size), 1)
    return (cols == rows + shift + hidden).astype(jnp.float32)


def wall_gather(part, sums):
    count = lax.axis_size("wall")
    slots = lax.broadcasted_iota(jnp.int32, (count,) + part.shape, 0)
    spread = jnp.where(slots == lax.axis_index("wall"), part[None], 0.0)
    packed = allreduce(jnp.concatenate([sums, spread.reshape(-1)]), ("wall",))
    return packed[sums.shape[0] :].reshape(spread.shape), packed[: sums.shape[0]]


def allreduce(values, axes=("wall", "sx", "sy")):
    for axis in axes:
        count = lax.axis_size(axis)
        step = 1
        while step < count:
            pairs = [(i, i ^ step) for i in range(count)]
            values = values + lax.ppermute(values, axis, pairs)
            step *= 2
    return values


def mv(matrix, vector):
    return jnp.sum(matrix * vector[..., None, :], -1)


def lateral_maps(side_coupling, orientation):
    grid = side_coupling.reshape(side_coupling.shape[:-1] + (PTS, PTS, VARS))
    picked = None
    for quarter in range(4):
        turned = jnp.rot90(grid, -quarter, axes=(-3, -2)).reshape(side_coupling.shape)
        if picked is None:
            picked = turned
        else:
            picked = jnp.where((orientation == quarter)[..., None, None], turned, picked)
    lead = picked.shape[:3]
    none = [(0, 0)] * len(lead)
    placed = []
    for face, (shape, gap) in enumerate(
        [
            ((PTS, PTS, 1), (0, 0, (0, PTS - 1))),
            ((PTS, PTS, 1), (0, 0, (PTS - 1, 0))),
            ((PTS, 1, PTS), (0, (0, PTS - 1), 0)),
            ((PTS, 1, PTS), (0, (PTS - 1, 0), 0)),
        ]
    ):
        one = picked[..., face, :, :].reshape(lead + shape + (VARS, FACE))
        widths = none + [g if g else (0, 0) for g in gap] + [(0, 0), (0, 0)]
        placed.append(jnp.pad(one, widths).reshape(lead + (BLOCK, FACE)))
    return jnp.concatenate(placed, -1)


def neighbour(values, axis, dim, later):
    count = lax.axis_size(axis)
    size = values.shape[dim]
    if later:
        pairs = [(i + 1, i) for i in range(count - 1)]
        moved = lax.ppermute(lax.slice_in_dim(values, 0, 1, axis=dim), axis, pairs)
        return jnp.concatenate([lax.slice_in_dim(values, 1, size, axis=dim), moved], dim)
    pairs = [(i, i + 1) for i in range(count - 1)]
    moved = lax.ppermute(lax.slice_in_dim(values, size - 1, size, axis=dim), axis, pairs)
    return jnp.concatenate([moved, lax.slice_in_dim(values, 0, size - 1, axis=dim)], dim)


def lateral_from(direction, coupling):
    lead = direction.shape[:3]
    grid = direction.reshape(lead + (PTS, PTS, PTS, VARS))
    faces = [
        grid[..., :, :, 0, :],
        grid[..., :, :, PTS - 1, :],
        grid[..., :, 0, :, :],
        grid[..., :, PTS - 1, :, :],
    ]
    faces = [one.reshape(lead + (FACE,)) for one in faces]
    across = jnp.concatenate(
        [
            neighbour(faces[1], "sx", 0, False),
            neighbour(faces[0], "sx", 0, True),
            neighbour(faces[3], "sy", 1, False),
            neighbour(faces[2], "sy", 1, True),
        ],
        -1,
    )
    return mv(coupling, across)


def line_maps(pivot_inverse, lower_face, upper_face):
    lead = pivot_inverse.shape[:2]
    elements = pivot_inverse.shape[2]
    from_below = -jnp.einsum(
        "xyeab,xyebc->xyeac", pivot_inverse[..., :FACE], lower_face, precision=precise
    )
    from_above = -jnp.einsum(
        "xyeab,xyebc->xyeac", pivot_inverse[..., BLOCK - FACE :], upper_face, precision=precise
    )
    lower_maps = from_below[..., BLOCK - FACE :, :]
    trail_maps = from_below[..., :FACE, :]
    upper_maps = from_above[..., :FACE, :]
    inputs = (2 + 2 * elements) * FACE
    entering_low = unit(inputs, 0)
    entering_high = unit(inputs, FACE)
    ahead = [unit(inputs, (2 + i) * FACE) for i in range(elements)]
    trail0 = [unit(inputs, (2 + elements + i) * FACE) for i in range(elements)]
    carried = jnp.broadcast_to(entering_low, lead + entering_low.shape)
    before = []
    for i in range(elements):
        before.append(carried)
        carried = ahead[i] + mm(lower_maps[:, :, i], carried)
    leaving_high = carried
    trails = [trail0[i] + mm(trail_maps[:, :, i], before[i]) for i in range(elements)]
    carried = jnp.broadcast_to(entering_high, lead + entering_high.shape)
    after = [None] * elements
    for i in reversed(range(elements)):
        after[i] = carried
        carried = trails[i] + mm(upper_maps[:, :, i], carried)
    leaving_low = carried
    carries = jnp.stack(before + after, 2)
    leaving = jnp.stack([leaving_high, leaving_low], 2)
    return from_below, from_above, carries, leaving


def wall_maps(gathered):
    axis = "wall"
    count = lax.axis_size(axis)
    place = lax.axis_index(axis)
    lead = gathered.shape[1:3]
    half = count * FACE
    low = [jnp.zeros(lead + (FACE, half), jnp.float32)]
    for d in range(count - 1):
        low.append(unit(half, d * FACE) + mm(gathered[d, :, :, 0], low[d]))
    zeros = jnp.zeros(lead + (FACE, half), jnp.float32)
    picked_low = zeros
    for d in range(count):
        picked_low = jnp.where(place == d, low[d], picked_low)
    high = jnp.zeros(lead + (FACE, 2 * half), jnp.float32)
    picked_high = jnp.where(place == count - 1, high, high)
    for d in range(count - 1, 0, -1):
        high = mm(gathered[d, :, :, 1], high) + jnp.concatenate(
            [
                mm(gathered[d, :, :, 2], low[d]),
                jnp.broadcast_to(unit(half, d * FACE), lead + (FACE, half)),
            ],
            -1,
        )
        picked_high = jnp.where(place == d - 1, high, picked_high)
    picked_low = jnp.concatenate([picked_low, zeros], -1)
    return jnp.stack([picked_low, picked_high], 2)


def solve_small(matrix, vector):
    extent = matrix.shape[0]
    index_ids = jnp.arange(extent)
    for k in range(extent):
        factor_col = jnp.where(index_ids > k, matrix[:, k] / matrix[k, k], 0.0)
        matrix = matrix - factor_col[:, None] * matrix[k][None, :]
        vector = vector - factor_col * vector[k]
    solved = jnp.zeros((extent,), jnp.float32)
    for k in reversed(range(extent)):
        solved = solved.at[k].set((vector[k] - jnp.sum(matrix[k] * solved)) / matrix[k, k])
    return solved


def least_squares(hessenberg, initial_norm):
    target = jnp.zeros((hessenberg.shape[0],), jnp.float32).at[0].set(initial_norm)
    normal = jnp.dot(hessenberg.T, hessenberg, precision=precise)
    weights = solve_small(normal, jnp.dot(hessenberg.T, target, precision=precise))
    misfit = target - jnp.dot(hessenberg, weights, precision=precise)
    return (weights, jnp.sqrt(jnp.sum(misfit * misfit)) / initial_norm)


def shards(forcing, pivot_inverse, lower_face, upper_face, side_coupling, orientation):
    lead = forcing.shape[:2]
    elements = forcing.shape[2]
    from_below, from_above, carries, leaving = line_maps(pivot_inverse, lower_face, upper_face)
    coupling = lateral_maps(side_coupling, orientation)
    local_leaving = leaving[..., 2 * FACE :]

    def local_of(rows):
        return jnp.concatenate(
            [rows[..., BLOCK - FACE :], rows[..., :FACE]], 2
        ).reshape(lead + (2 * elements * FACE,))

    def outgoing(rows):
        return mv(local_leaving, local_of(rows)[:, :, None]).reshape(lead + (2 * FACE,))

    def flat_gather(block):
        count = block.shape[0]
        block = block.reshape((count,) + lead + (2, FACE))
        return jnp.transpose(block, (1, 2, 3, 0, 4)).reshape(lead + (-1,))

    def precond(rows, gathered):
        local = local_of(rows)
        entering = mv(entry, gathered[:, :, None])
        full = jnp.concatenate([entering.reshape(lead + (2 * FACE,)), local], -1)
        faces = mv(carries, full[:, :, None])
        return (
            rows
            + mv(from_below, faces[:, :, :elements])
            + mv(from_above, faces[:, :, elements:])
        )

    def dot(a, b):
        return jnp.sum(a * b)

    entry_count = forcing.size * lax.axis_size("wall") * lax.axis_size("sx") * lax.axis_size("sy")
    basis = [forcing]
    images = [mv(pivot_inverse, forcing)]
    needed = jnp.stack(
        [leaving[..., 0, :, :FACE], leaving[..., 1, :, FACE : 2 * FACE], leaving[..., 1, :, :FACE]], 2
    )
    together = lax.all_gather(
        jnp.concatenate([needed.reshape(lead + (-1,)), outgoing(images[0])], -1), "wall"
    )
    entry = wall_maps(together[..., : 3 * FACE * FACE].reshape(together.shape[:3] + needed.shape[2:]))
    spread = [flat_gather(together[..., 3 * FACE * FACE :])]
    precon = []
    norms = []
    gram = {}
    columns = []
    squares = None
    for j in range(ITERS):
        current = basis[j]
        pre = precond(images[j], spread[j])
        precon.append(pre)
        mapped = current + lateral_from(pre, coupling)
        partial = [dot(current, current)] + [dot(mapped, basis[i]) for i in range(j + 1)]
        partial += [dot(basis[i], current) for i in range(j)]
        partial = jnp.stack(partial)
        if j + 1 < ITERS:
            mapped_rows = mv(pivot_inverse, mapped)
            mapped_out, partial = wall_gather(outgoing(mapped_rows), partial)
            total = allreduce(partial, ("sx", "sy"))
        else:
            total = allreduce(partial)
        norm_sq = total[0]
        if j == 0:
            squares = norm_sq
        norms.append(jnp.sqrt(norm_sq))
        for i in range(j):
            gram[(i, j)] = total[2 + j + i] / (norms[i] * norms[j])
        listed = []
        for i in range(j + 1):
            projected = total[1 + i] / (norms[i] * norms[j])
            for l in range(i):
                projected = projected - listed[l] * gram[(l, i)]
            listed.append(projected)
        following = mapped / norms[j]
        for i in range(j + 1):
            following = following - (listed[i] / norms[i]) * basis[i]
        basis.append(following)
        if j + 1 < ITERS:
            moved = flat_gather(mapped_out) / norms[j]
            image = mapped_rows / norms[j]
            for i in range(j + 1):
                moved = moved - (listed[i] / norms[i]) * spread[i]
                image = image - (listed[i] / norms[i]) * images[i]
            spread.append(moved)
            images.append(image)
        columns.append(listed)
    last = allreduce(jnp.stack([dot(basis[ITERS], basis[ITERS])]))
    norms.append(jnp.sqrt(last[0]))
    full_columns = []
    for j in range(ITERS):
        full_columns.append(
            jnp.concatenate(
                [jnp.stack(columns[j]), norms[j + 1][None], jnp.zeros((ITERS - 1 - j,), jnp.float32)]
            )
        )
    hessenberg = jnp.stack(full_columns, 1)
    forcing_rms = jnp.sqrt(squares / entry_count)
    initial_norm = jnp.sqrt(squares)
    weights, relative = least_squares(hessenberg, initial_norm)
    solution = (weights[0] / norms[0]) * precon[0]
    for j in range(1, ITERS):
        solution = solution + (weights[j] / norms[j]) * precon[j]
    return (solution, relative, forcing_rms)


def solution(mesh):
    return jax.shard_map(
        shards,
        mesh=mesh,
        in_specs=(
            P("sx", "sy", "wall", None),
            P("sx", "sy", "wall", None, None),
            P("sx", "sy", "wall", None, None),
            P("sx", "sy", "wall", None, None),
            P("sx", "sy", "wall", None, None, None),
            P("sx", "sy", "wall", None),
        ),
        out_specs=(P("sx", "sy", "wall", None), P(), P()),
        check_vma=False,
    )
```

```python
import numpy as np
import jax
import jax.numpy as jnp
from jax import lax
from jax.sharding import PartitionSpec as P

PTS = 4
VARS = 6
BLOCK = 384
FACE = 96
ITERS = 3


precise = lax.Precision.HIGHEST


def mm(matrix, columns):
    return jnp.einsum("xyab,xybk->xyak", matrix, columns, precision=precise)


def unit(size, shift=0):
    hidden = jnp.minimum(lax.axis_index("wall"), 0)
    rows = lax.broadcasted_iota(jnp.int32, (FACE, size), 0)
    cols = lax.broadcasted_iota(jnp.int32, (FACE, size), 1)
    return (cols == rows + shift + hidden).astype(jnp.float32)


def wall_gather(part, sums):
    count = lax.axis_size("wall")
    slots = lax.broadcasted_iota(jnp.int32, (count,) + part.shape, 0)
    spread = jnp.where(slots == lax.axis_index("wall"), part[None], 0.0)
    packed = allreduce(jnp.concatenate([sums, spread.reshape(-1)]), ("wall",))
    return packed[sums.shape[0] :].reshape(spread.shape), packed[: sums.shape[0]]


def allreduce(values, axes=("wall", "sx", "sy")):
    for axis in axes:
        count = lax.axis_size(axis)
        step = 1
        while step < count:
            pairs = [(i, i ^ step) for i in range(count)]
            values = values + lax.ppermute(values, axis, pairs)
            step *= 2
    return values


def mv(matrix, vector):
    return jnp.sum(matrix * vector[..., None, :], -1)


def lateral_maps(side_coupling, orientation):
    grid = side_coupling.reshape(side_coupling.shape[:-1] + (PTS, PTS, VARS))
    picked = None
    for quarter in range(4):
        turned = jnp.rot90(grid, -quarter, axes=(-3, -2)).reshape(side_coupling.shape)
        if picked is None:
            picked = turned
        else:
            picked = jnp.where((orientation == quarter)[..., None, None], turned, picked)
    lead = picked.shape[:3]
    none = [(0, 0)] * len(lead)
    placed = []
    for face, (shape, gap) in enumerate(
        [
            ((PTS, PTS, 1), (0, 0, (0, PTS - 1))),
            ((PTS, PTS, 1), (0, 0, (PTS - 1, 0))),
            ((PTS, 1, PTS), (0, (0, PTS - 1), 0)),
            ((PTS, 1, PTS), (0, (PTS - 1, 0), 0)),
        ]
    ):
        one = picked[..., face, :, :].reshape(lead + shape + (VARS, FACE))
        widths = none + [g if g else (0, 0) for g in gap] + [(0, 0), (0, 0)]
        placed.append(jnp.pad(one, widths).reshape(lead + (BLOCK, FACE)))
    return jnp.concatenate(placed, -1)


def neighbour(values, axis, dim, later):
    count = lax.axis_size(axis)
    size = values.shape[dim]
    if later:
        pairs = [(i + 1, i) for i in range(count - 1)]
        moved = lax.ppermute(lax.slice_in_dim(values, 0, 1, axis=dim), axis, pairs)
        return jnp.concatenate([lax.slice_in_dim(values, 1, size, axis=dim), moved], dim)
    pairs = [(i, i + 1) for i in range(count - 1)]
    moved = lax.ppermute(lax.slice_in_dim(values, size - 1, size, axis=dim), axis, pairs)
    return jnp.concatenate([moved, lax.slice_in_dim(values, 0, size - 1, axis=dim)], dim)


def lateral_from(direction, coupling):
    lead = direction.shape[:3]
    grid = direction.reshape(lead + (PTS, PTS, PTS, VARS))
    faces = [
        grid[..., :, :, 0, :],
        grid[..., :, :, PTS - 1, :],
        grid[..., :, 0, :, :],
        grid[..., :, PTS - 1, :, :],
    ]
    faces = [one.reshape(lead + (FACE,)) for one in faces]
    across = jnp.concatenate(
        [
            neighbour(faces[1], "sx", 0, False),
            neighbour(faces[0], "sx", 0, True),
            neighbour(faces[3], "sy", 1, False),
            neighbour(faces[2], "sy", 1, True),
        ],
        -1,
    )
    return mv(coupling, across)


def line_maps(pivot_inverse, lower_face, upper_face):
    lead = pivot_inverse.shape[:2]
    elements = pivot_inverse.shape[2]
    from_below = -jnp.einsum(
        "xyeab,xyebc->xyeac", pivot_inverse[..., :FACE], lower_face, precision=precise
    )
    from_above = -jnp.einsum(
        "xyeab,xyebc->xyeac", pivot_inverse[..., BLOCK - FACE :], upper_face, precision=precise
    )
    lower_maps = from_below[..., BLOCK - FACE :, :]
    trail_maps = from_below[..., :FACE, :]
    upper_maps = from_above[..., :FACE, :]
    inputs = (2 + 2 * elements) * FACE
    entering_low = unit(inputs, 0)
    entering_high = unit(inputs, FACE)
    ahead = [unit(inputs, (2 + i) * FACE) for i in range(elements)]
    trail0 = [unit(inputs, (2 + elements + i) * FACE) for i in range(elements)]
    carried = jnp.broadcast_to(entering_low, lead + entering_low.shape)
    before = []
    for i in range(elements):
        before.append(carried)
        carried = ahead[i] + mm(lower_maps[:, :, i], carried)
    leaving_high = carried
    trails = [trail0[i] + mm(trail_maps[:, :, i], before[i]) for i in range(elements)]
    carried = jnp.broadcast_to(entering_high, lead + entering_high.shape)
    after = [None] * elements
    for i in reversed(range(elements)):
        after[i] = carried
        carried = trails[i] + mm(upper_maps[:, :, i], carried)
    leaving_low = carried
    carries = jnp.stack(before + after, 2)
    leaving = jnp.stack([leaving_high, leaving_low], 2)
    return from_below, from_above, carries, leaving


def wall_maps(gathered):
    axis = "wall"
    count = lax.axis_size(axis)
    place = lax.axis_index(axis)
    lead = gathered.shape[1:3]
    half = count * FACE
    low = [jnp.zeros(lead + (FACE, half), jnp.float32)]
    for d in range(count - 1):
        low.append(unit(half, d * FACE) + mm(gathered[d, :, :, 0], low[d]))
    zeros = jnp.zeros(lead + (FACE, half), jnp.float32)
    picked_low = zeros
    for d in range(count):
        picked_low = jnp.where(place == d, low[d], picked_low)
    high = jnp.zeros(lead + (FACE, 2 * half), jnp.float32)
    picked_high = jnp.where(place == count - 1, high, high)
    for d in range(count - 1, 0, -1):
        high = mm(gathered[d, :, :, 1], high) + jnp.concatenate(
            [
                mm(gathered[d, :, :, 2], low[d]),
                jnp.broadcast_to(unit(half, d * FACE), lead + (FACE, half)),
            ],
            -1,
        )
        picked_high = jnp.where(place == d - 1, high, picked_high)
    picked_low = jnp.concatenate([picked_low, zeros], -1)
    return jnp.stack([picked_low, picked_high], 2)


def solve_small(matrix, vector):
    extent = matrix.shape[0]
    index_ids = jnp.arange(extent)
    for k in range(extent):
        factor_col = jnp.where(index_ids > k, matrix[:, k] / matrix[k, k], 0.0)
        matrix = matrix - factor_col[:, None] * matrix[k][None, :]
        vector = vector - factor_col * vector[k]
    solved = jnp.zeros((extent,), jnp.float32)
    for k in reversed(range(extent)):
        solved = solved.at[k].set((vector[k] - jnp.sum(matrix[k] * solved)) / matrix[k, k])
    return solved


def least_squares(hessenberg, initial_norm):
    target = jnp.zeros((hessenberg.shape[0],), jnp.float32).at[0].set(initial_norm)
    normal = jnp.dot(hessenberg.T, hessenberg, precision=precise)
    weights = solve_small(normal, jnp.dot(hessenberg.T, target, precision=precise))
    misfit = target - jnp.dot(hessenberg, weights, precision=precise)
    return (weights, jnp.sqrt(jnp.sum(misfit * misfit)) / initial_norm)


def shards(forcing, pivot_inverse, lower_face, upper_face, side_coupling, orientation):
    lead = forcing.shape[:2]
    elements = forcing.shape[2]
    from_below, from_above, carries, leaving = line_maps(pivot_inverse, lower_face, upper_face)
    coupling = lateral_maps(side_coupling, orientation)
    local_leaving = leaving[..., 2 * FACE :]

    def local_of(rows):
        return jnp.concatenate(
            [rows[..., BLOCK - FACE :], rows[..., :FACE]], 2
        ).reshape(lead + (2 * elements * FACE,))

    def outgoing(rows):
        return mv(local_leaving, local_of(rows)[:, :, None]).reshape(lead + (2 * FACE,))

    def flat_gather(block):
        count = block.shape[0]
        block = block.reshape((count,) + lead + (2, FACE))
        return jnp.transpose(block, (1, 2, 3, 0, 4)).reshape(lead + (-1,))

    def precond(rows, gathered):
        local = local_of(rows)
        entering = mv(entry, gathered[:, :, None])
        full = jnp.concatenate([entering.reshape(lead + (2 * FACE,)), local], -1)
        faces = mv(carries, full[:, :, None])
        return (
            rows
            + mv(from_below, faces[:, :, :elements])
            + mv(from_above, faces[:, :, elements:])
        )

    def dot(a, b):
        return jnp.sum(a * b)

    entry_count = forcing.size * lax.axis_size("wall") * lax.axis_size("sx") * lax.axis_size("sy")
    basis = [forcing]
    images = [mv(pivot_inverse, forcing)]
    needed = jnp.stack(
        [leaving[..., 0, :, :FACE], leaving[..., 1, :, FACE : 2 * FACE], leaving[..., 1, :, :FACE]], 2
    )
    entry = wall_maps(lax.all_gather(needed, "wall"))
    spread = [flat_gather(lax.all_gather(outgoing(images[0]), "wall"))]
    precon = []
    norms = []
    gram = {}
    columns = []
    squares = None
    for j in range(ITERS):
        current = basis[j]
        pre = precond(images[j], spread[j])
        precon.append(pre)
        mapped = current + lateral_from(pre, coupling)
        partial = [dot(current, current)] + [dot(mapped, basis[i]) for i in range(j + 1)]
        partial += [dot(basis[i], current) for i in range(j)]
        partial = jnp.stack(partial)
        if j + 1 < ITERS:
            mapped_rows = mv(pivot_inverse, mapped)
            mapped_out, partial = wall_gather(outgoing(mapped_rows), partial)
            total = allreduce(partial, ("sx", "sy"))
        else:
            total = allreduce(partial)
        norm_sq = total[0]
        if j == 0:
            squares = norm_sq
        norms.append(jnp.sqrt(norm_sq))
        for i in range(j):
            gram[(i, j)] = total[2 + j + i] / (norms[i] * norms[j])
        listed = []
        for i in range(j + 1):
            projected = total[1 + i] / (norms[i] * norms[j])
            for l in range(i):
                projected = projected - listed[l] * gram[(l, i)]
            listed.append(projected)
        following = mapped / norms[j]
        for i in range(j + 1):
            following = following - (listed[i] / norms[i]) * basis[i]
        basis.append(following)
        if j + 1 < ITERS:
            moved = flat_gather(mapped_out) / norms[j]
            image = mapped_rows / norms[j]
            for i in range(j + 1):
                moved = moved - (listed[i] / norms[i]) * spread[i]
                image = image - (listed[i] / norms[i]) * images[i]
            spread.append(moved)
            images.append(image)
        columns.append(listed)
    last = allreduce(jnp.stack([dot(basis[ITERS], basis[ITERS])]))
    norms.append(jnp.sqrt(last[0]))
    full_columns = []
    for j in range(ITERS):
        full_columns.append(
            jnp.concatenate(
                [jnp.stack(columns[j]), norms[j + 1][None], jnp.zeros((ITERS - 1 - j,), jnp.float32)]
            )
        )
    hessenberg = jnp.stack(full_columns, 1)
    forcing_rms = jnp.sqrt(squares / entry_count)
    initial_norm = jnp.sqrt(squares)
    weights, relative = least_squares(hessenberg, initial_norm)
    solution = (weights[0] / norms[0]) * precon[0]
    for j in range(1, ITERS):
        solution = solution + (weights[j] / norms[j]) * precon[j]
    return (solution, relative, forcing_rms)


def solution(mesh):
    return jax.shard_map(
        shards,
        mesh=mesh,
        in_specs=(
            P("sx", "sy", "wall", None),
            P("sx", "sy", "wall", None, None),
            P("sx", "sy", "wall", None, None),
            P("sx", "sy", "wall", None, None),
            P("sx", "sy", "wall", None, None, None),
            P("sx", "sy", "wall", None),
        ),
        out_specs=(P("sx", "sy", "wall", None), P(), P()),
        check_vma=False,
    )
```

```python
import numpy as np
import jax
import jax.numpy as jnp
from jax import lax
from jax.sharding import PartitionSpec as P

PTS = 4
VARS = 6
BLOCK = 384
FACE = 96
ITERS = 3


precise = lax.Precision.HIGHEST


def mm(matrix, columns):
    return jnp.einsum("xyab,xybk->xyak", matrix, columns, precision=precise)


def unit(size, shift=0):
    hidden = jnp.minimum(lax.axis_index("wall"), 0)
    rows = lax.broadcasted_iota(jnp.int32, (FACE, size), 0)
    cols = lax.broadcasted_iota(jnp.int32, (FACE, size), 1)
    return (cols == rows + shift + hidden).astype(jnp.float32)


def wall_gather(part, sums):
    count = lax.axis_size("wall")
    slots = lax.broadcasted_iota(jnp.int32, (count,) + part.shape, 0)
    spread = jnp.where(slots == lax.axis_index("wall"), part[None], 0.0)
    packed = allreduce(jnp.concatenate([sums, spread.reshape(-1)]), ("wall",))
    return packed[sums.shape[0] :].reshape(spread.shape), packed[: sums.shape[0]]


def allreduce(values, axes=("wall", "sx", "sy")):
    for axis in axes:
        count = lax.axis_size(axis)
        step = 1
        while step < count:
            pairs = [(i, i ^ step) for i in range(count)]
            values = values + lax.ppermute(values, axis, pairs)
            step *= 2
    return values


def mv(matrix, vector):
    return jnp.sum(matrix * vector[..., None, :], -1)


def lateral_maps(side_coupling, orientation):
    grid = side_coupling.reshape(side_coupling.shape[:-1] + (PTS, PTS, VARS))
    picked = None
    for quarter in range(4):
        turned = jnp.rot90(grid, -quarter, axes=(-3, -2)).reshape(side_coupling.shape)
        if picked is None:
            picked = turned
        else:
            picked = jnp.where((orientation == quarter)[..., None, None], turned, picked)
    lead = picked.shape[:3]
    none = [(0, 0)] * len(lead)
    placed = []
    for face, (shape, gap) in enumerate(
        [
            ((PTS, PTS, 1), (0, 0, (0, PTS - 1))),
            ((PTS, PTS, 1), (0, 0, (PTS - 1, 0))),
            ((PTS, 1, PTS), (0, (0, PTS - 1), 0)),
            ((PTS, 1, PTS), (0, (PTS - 1, 0), 0)),
        ]
    ):
        one = picked[..., face, :, :].reshape(lead + shape + (VARS, FACE))
        widths = none + [g if g else (0, 0) for g in gap] + [(0, 0), (0, 0)]
        placed.append(jnp.pad(one, widths).reshape(lead + (BLOCK, FACE)))
    return jnp.concatenate(placed, -1)


def neighbour(values, axis, dim, later):
    count = lax.axis_size(axis)
    size = values.shape[dim]
    if later:
        pairs = [(i + 1, i) for i in range(count - 1)]
        moved = lax.ppermute(lax.slice_in_dim(values, 0, 1, axis=dim), axis, pairs)
        return jnp.concatenate([lax.slice_in_dim(values, 1, size, axis=dim), moved], dim)
    pairs = [(i, i + 1) for i in range(count - 1)]
    moved = lax.ppermute(lax.slice_in_dim(values, size - 1, size, axis=dim), axis, pairs)
    return jnp.concatenate([moved, lax.slice_in_dim(values, 0, size - 1, axis=dim)], dim)


def lateral_from(direction, coupling):
    lead = direction.shape[:3]
    grid = direction.reshape(lead + (PTS, PTS, PTS, VARS))
    faces = [
        grid[..., :, :, 0, :],
        grid[..., :, :, PTS - 1, :],
        grid[..., :, 0, :, :],
        grid[..., :, PTS - 1, :, :],
    ]
    faces = [one.reshape(lead + (FACE,)) for one in faces]
    across = jnp.concatenate(
        [
            neighbour(faces[1], "sx", 0, False),
            neighbour(faces[0], "sx", 0, True),
            neighbour(faces[3], "sy", 1, False),
            neighbour(faces[2], "sy", 1, True),
        ],
        -1,
    )
    return mv(coupling, across)


def line_maps(pivot_inverse, lower_face, upper_face):
    lead = pivot_inverse.shape[:2]
    elements = pivot_inverse.shape[2]
    from_below = -jnp.einsum(
        "xyeab,xyebc->xyeac", pivot_inverse[..., :FACE], lower_face, precision=precise
    )
    from_above = -jnp.einsum(
        "xyeab,xyebc->xyeac", pivot_inverse[..., BLOCK - FACE :], upper_face, precision=precise
    )
    lower_maps = from_below[..., BLOCK - FACE :, :]
    trail_maps = from_below[..., :FACE, :]
    upper_maps = from_above[..., :FACE, :]
    inputs = (2 + 2 * elements) * FACE
    entering_low = unit(inputs, 0)
    entering_high = unit(inputs, FACE)
    ahead = [unit(inputs, (2 + i) * FACE) for i in range(elements)]
    trail0 = [unit(inputs, (2 + elements + i) * FACE) for i in range(elements)]
    carried = jnp.broadcast_to(entering_low, lead + entering_low.shape)
    before = []
    for i in range(elements):
        before.append(carried)
        carried = ahead[i] + mm(lower_maps[:, :, i], carried)
    leaving_high = carried
    trails = [trail0[i] + mm(trail_maps[:, :, i], before[i]) for i in range(elements)]
    carried = jnp.broadcast_to(entering_high, lead + entering_high.shape)
    after = [None] * elements
    for i in reversed(range(elements)):
        after[i] = carried
        carried = trails[i] + mm(upper_maps[:, :, i], carried)
    leaving_low = carried
    carries = jnp.stack(before + after, 2)
    leaving = jnp.stack([leaving_high, leaving_low], 2)
    return from_below, from_above, carries, leaving


def wall_maps(gathered):
    axis = "wall"
    count = lax.axis_size(axis)
    place = lax.axis_index(axis)
    lead = gathered.shape[1:3]
    half = count * FACE
    low = [jnp.zeros(lead + (FACE, half), jnp.float32)]
    for d in range(count - 1):
        low.append(unit(half, d * FACE) + mm(gathered[d, :, :, 0], low[d]))
    zeros = jnp.zeros(lead + (FACE, half), jnp.float32)
    picked_low = zeros
    for d in range(count):
        picked_low = jnp.where(place == d, low[d], picked_low)
    high = jnp.zeros(lead + (FACE, 2 * half), jnp.float32)
    picked_high = jnp.where(place == count - 1, high, high)
    for d in range(count - 1, 0, -1):
        high = mm(gathered[d, :, :, 1], high) + jnp.concatenate(
            [
                mm(gathered[d, :, :, 2], low[d]),
                jnp.broadcast_to(unit(half, d * FACE), lead + (FACE, half)),
            ],
            -1,
        )
        picked_high = jnp.where(place == d - 1, high, picked_high)
    picked_low = jnp.concatenate([picked_low, zeros], -1)
    return jnp.stack([picked_low, picked_high], 2)


def solve_small(matrix, vector):
    extent = matrix.shape[0]
    index_ids = jnp.arange(extent)
    for k in range(extent):
        factor_col = jnp.where(index_ids > k, matrix[:, k] / matrix[k, k], 0.0)
        matrix = matrix - factor_col[:, None] * matrix[k][None, :]
        vector = vector - factor_col * vector[k]
    solved = jnp.zeros((extent,), jnp.float32)
    for k in reversed(range(extent)):
        solved = solved.at[k].set((vector[k] - jnp.sum(matrix[k] * solved)) / matrix[k, k])
    return solved


def least_squares(hessenberg, initial_norm):
    target = jnp.zeros((hessenberg.shape[0],), jnp.float32).at[0].set(initial_norm)
    normal = jnp.dot(hessenberg.T, hessenberg, precision=precise)
    weights = solve_small(normal, jnp.dot(hessenberg.T, target, precision=precise))
    misfit = target - jnp.dot(hessenberg, weights, precision=precise)
    return (weights, jnp.sqrt(jnp.sum(misfit * misfit)) / initial_norm)


def shards(forcing, pivot_inverse, lower_face, upper_face, side_coupling, orientation):
    lead = forcing.shape[:2]
    elements = forcing.shape[2]
    from_below, from_above, carries, leaving = line_maps(pivot_inverse, lower_face, upper_face)
    coupling = lateral_maps(side_coupling, orientation)
    local_leaving = leaving[..., 2 * FACE :]

    def local_of(rows):
        return jnp.concatenate(
            [rows[..., BLOCK - FACE :], rows[..., :FACE]], 2
        ).reshape(lead + (2 * elements * FACE,))

    def outgoing(rows):
        return mv(local_leaving, local_of(rows)[:, :, None]).reshape(lead + (2 * FACE,))

    def flat_gather(block):
        count = block.shape[0]
        block = block.reshape((count,) + lead + (2, FACE))
        return jnp.transpose(block, (1, 2, 3, 0, 4)).reshape(lead + (-1,))

    def precond(rows, gathered):
        faces = mv(through, gathered[:, :, None]) + mv(inside, local_of(rows)[:, :, None])
        return (
            rows
            + mv(from_below, faces[:, :, :elements])
            + mv(from_above, faces[:, :, elements:])
        )

    def dot(a, b):
        return jnp.sum(a * b)

    entry_count = forcing.size * lax.axis_size("wall") * lax.axis_size("sx") * lax.axis_size("sy")
    basis = [forcing]
    images = [mv(pivot_inverse, forcing)]
    needed = jnp.stack(
        [leaving[..., 0, :, :FACE], leaving[..., 1, :, FACE : 2 * FACE], leaving[..., 1, :, :FACE]], 2
    )
    entry = wall_maps(lax.all_gather(needed, "wall"))
    through = jnp.einsum(
        "xyeak,xykm->xyeam",
        carries[..., : 2 * FACE],
        entry.reshape(lead + (2 * FACE, -1)),
        precision=precise,
    )
    inside = carries[..., 2 * FACE :]

    spread = [flat_gather(lax.all_gather(outgoing(images[0]), "wall"))]
    precon = []
    norms = []
    gram = {}
    columns = []
    squares = None
    for j in range(ITERS):
        current = basis[j]
        pre = precond(images[j], spread[j])
        precon.append(pre)
        mapped = current + lateral_from(pre, coupling)
        partial = [dot(current, current)] + [dot(mapped, basis[i]) for i in range(j + 1)]
        partial += [dot(basis[i], current) for i in range(j)]
        partial = jnp.stack(partial)
        if j + 1 < ITERS:
            mapped_rows = mv(pivot_inverse, mapped)
            mapped_out, partial = wall_gather(outgoing(mapped_rows), partial)
            total = allreduce(partial, ("sx", "sy"))
        else:
            total = allreduce(partial)
        norm_sq = total[0]
        if j == 0:
            squares = norm_sq
        norms.append(jnp.sqrt(norm_sq))
        for i in range(j):
            gram[(i, j)] = total[2 + j + i] / (norms[i] * norms[j])
        listed = []
        for i in range(j + 1):
            projected = total[1 + i] / (norms[i] * norms[j])
            for l in range(i):
                projected = projected - listed[l] * gram[(l, i)]
            listed.append(projected)
        following = mapped / norms[j]
        for i in range(j + 1):
            following = following - (listed[i] / norms[i]) * basis[i]
        basis.append(following)
        if j + 1 < ITERS:
            moved = flat_gather(mapped_out) / norms[j]
            image = mapped_rows / norms[j]
            for i in range(j + 1):
                moved = moved - (listed[i] / norms[i]) * spread[i]
                image = image - (listed[i] / norms[i]) * images[i]
            spread.append(moved)
            images.append(image)
        columns.append(listed)
    last = allreduce(jnp.stack([dot(basis[ITERS], basis[ITERS])]))
    norms.append(jnp.sqrt(last[0]))
    full_columns = []
    for j in range(ITERS):
        full_columns.append(
            jnp.concatenate(
                [jnp.stack(columns[j]), norms[j + 1][None], jnp.zeros((ITERS - 1 - j,), jnp.float32)]
            )
        )
    hessenberg = jnp.stack(full_columns, 1)
    forcing_rms = jnp.sqrt(squares / entry_count)
    initial_norm = jnp.sqrt(squares)
    weights, relative = least_squares(hessenberg, initial_norm)
    solution = (weights[0] / norms[0]) * precon[0]
    for j in range(1, ITERS):
        solution = solution + (weights[j] / norms[j]) * precon[j]
    return (solution, relative, forcing_rms)


def solution(mesh):
    return jax.shard_map(
        shards,
        mesh=mesh,
        in_specs=(
            P("sx", "sy", "wall", None),
            P("sx", "sy", "wall", None, None),
            P("sx", "sy", "wall", None, None),
            P("sx", "sy", "wall", None, None),
            P("sx", "sy", "wall", None, None, None),
            P("sx", "sy", "wall", None),
        ),
        out_specs=(P("sx", "sy", "wall", None), P(), P()),
        check_vma=False,
    )
```

```python
import numpy as np
import jax
import jax.numpy as jnp
from jax import lax
from jax.sharding import PartitionSpec as P

PTS = 4
VARS = 6
BLOCK = 384
FACE = 96
ITERS = 3


precise = lax.Precision.HIGHEST


def mm(matrix, columns):
    return jnp.einsum("xyab,xybk->xyak", matrix, columns, precision=precise)


def unit(size, shift=0):
    hidden = jnp.minimum(lax.axis_index("wall"), 0)
    rows = lax.broadcasted_iota(jnp.int32, (FACE, size), 0)
    cols = lax.broadcasted_iota(jnp.int32, (FACE, size), 1)
    return (cols == rows + shift + hidden).astype(jnp.float32)


def wall_gather(part, sums):
    count = lax.axis_size("wall")
    slots = lax.broadcasted_iota(jnp.int32, (count,) + part.shape, 0)
    spread = jnp.where(slots == lax.axis_index("wall"), part[None], 0.0)
    packed = allreduce(jnp.concatenate([sums, spread.reshape(-1)]), ("wall",))
    return packed[sums.shape[0] :].reshape(spread.shape), packed[: sums.shape[0]]


def allreduce(values, axes=("wall", "sx", "sy")):
    for axis in axes:
        count = lax.axis_size(axis)
        step = 1
        while step < count:
            pairs = [(i, i ^ step) for i in range(count)]
            values = values + lax.ppermute(values, axis, pairs)
            step *= 2
    return values


def mv(matrix, vector):
    return jnp.sum(matrix * vector[..., None, :], -1)


def lateral_maps(side_coupling, orientation):
    grid = side_coupling.reshape(side_coupling.shape[:-1] + (PTS, PTS, VARS))
    picked = None
    for quarter in range(4):
        turned = jnp.rot90(grid, -quarter, axes=(-3, -2)).reshape(side_coupling.shape)
        if picked is None:
            picked = turned
        else:
            picked = jnp.where((orientation == quarter)[..., None, None], turned, picked)
    lead = picked.shape[:3]
    none = [(0, 0)] * len(lead)
    placed = []
    for face, (shape, gap) in enumerate(
        [
            ((PTS, PTS, 1), (0, 0, (0, PTS - 1))),
            ((PTS, PTS, 1), (0, 0, (PTS - 1, 0))),
            ((PTS, 1, PTS), (0, (0, PTS - 1), 0)),
            ((PTS, 1, PTS), (0, (PTS - 1, 0), 0)),
        ]
    ):
        one = picked[..., face, :, :].reshape(lead + shape + (VARS, FACE))
        widths = none + [g if g else (0, 0) for g in gap] + [(0, 0), (0, 0)]
        placed.append(jnp.pad(one, widths).reshape(lead + (BLOCK, FACE)))
    return jnp.concatenate(placed, -1)


def neighbour(values, axis, dim, later):
    count = lax.axis_size(axis)
    size = values.shape[dim]
    if later:
        pairs = [(i + 1, i) for i in range(count - 1)]
        moved = lax.ppermute(lax.slice_in_dim(values, 0, 1, axis=dim), axis, pairs)
        return jnp.concatenate([lax.slice_in_dim(values, 1, size, axis=dim), moved], dim)
    pairs = [(i, i + 1) for i in range(count - 1)]
    moved = lax.ppermute(lax.slice_in_dim(values, size - 1, size, axis=dim), axis, pairs)
    return jnp.concatenate([moved, lax.slice_in_dim(values, 0, size - 1, axis=dim)], dim)


def lateral_from(direction, coupling):
    lead = direction.shape[:3]
    grid = direction.reshape(lead + (PTS, PTS, PTS, VARS))
    faces = [
        grid[..., :, :, 0, :],
        grid[..., :, :, PTS - 1, :],
        grid[..., :, 0, :, :],
        grid[..., :, PTS - 1, :, :],
    ]
    faces = [one.reshape(lead + (FACE,)) for one in faces]
    across = jnp.concatenate(
        [
            neighbour(faces[1], "sx", 0, False),
            neighbour(faces[0], "sx", 0, True),
            neighbour(faces[3], "sy", 1, False),
            neighbour(faces[2], "sy", 1, True),
        ],
        -1,
    )
    return mv(coupling, across)


def line_maps(pivot_inverse, lower_face, upper_face):
    lead = pivot_inverse.shape[:2]
    elements = pivot_inverse.shape[2]
    from_below = -jnp.einsum(
        "xyeab,xyebc->xyeac", pivot_inverse[..., :FACE], lower_face, precision=precise
    )
    from_above = -jnp.einsum(
        "xyeab,xyebc->xyeac", pivot_inverse[..., BLOCK - FACE :], upper_face, precision=precise
    )
    lower_maps = from_below[..., BLOCK - FACE :, :]
    trail_maps = from_below[..., :FACE, :]
    upper_maps = from_above[..., :FACE, :]
    inputs = (2 + 2 * elements) * FACE
    entering_low = unit(inputs, 0)
    entering_high = unit(inputs, FACE)
    ahead = [unit(inputs, (2 + i) * FACE) for i in range(elements)]
    trail0 = [unit(inputs, (2 + elements + i) * FACE) for i in range(elements)]
    carried = jnp.broadcast_to(entering_low, lead + entering_low.shape)
    before = []
    for i in range(elements):
        before.append(carried)
        carried = ahead[i] + mm(lower_maps[:, :, i], carried)
    leaving_high = carried
    trails = [trail0[i] + mm(trail_maps[:, :, i], before[i]) for i in range(elements)]
    carried = jnp.broadcast_to(entering_high, lead + entering_high.shape)
    after = [None] * elements
    for i in reversed(range(elements)):
        after[i] = carried
        carried = trails[i] + mm(upper_maps[:, :, i], carried)
    leaving_low = carried
    carries = jnp.stack(before + after, 2)
    leaving = jnp.stack([leaving_high, leaving_low], 2)
    return from_below, from_above, carries, leaving


def wall_maps(gathered):
    axis = "wall"
    count = lax.axis_size(axis)
    place = lax.axis_index(axis)
    lead = gathered.shape[1:3]
    half = count * FACE
    low = [jnp.zeros(lead + (FACE, half), jnp.float32)]
    for d in range(count - 1):
        low.append(unit(half, d * FACE) + mm(gathered[d, :, :, 0], low[d]))
    zeros = jnp.zeros(lead + (FACE, half), jnp.float32)
    picked_low = zeros
    for d in range(count):
        picked_low = jnp.where(place == d, low[d], picked_low)
    high = jnp.zeros(lead + (FACE, 2 * half), jnp.float32)
    picked_high = jnp.where(place == count - 1, high, high)
    for d in range(count - 1, 0, -1):
        high = mm(gathered[d, :, :, 1], high) + jnp.concatenate(
            [
                mm(gathered[d, :, :, 2], low[d]),
                jnp.broadcast_to(unit(half, d * FACE), lead + (FACE, half)),
            ],
            -1,
        )
        picked_high = jnp.where(place == d - 1, high, picked_high)
    picked_low = jnp.concatenate([picked_low, zeros], -1)
    return jnp.stack([picked_low, picked_high], 2)


def solve_small(matrix, vector):
    extent = matrix.shape[0]
    index_ids = jnp.arange(extent)
    for k in range(extent):
        factor_col = jnp.where(index_ids > k, matrix[:, k] / matrix[k, k], 0.0)
        matrix = matrix - factor_col[:, None] * matrix[k][None, :]
        vector = vector - factor_col * vector[k]
    solved = jnp.zeros((extent,), jnp.float32)
    for k in reversed(range(extent)):
        solved = solved.at[k].set((vector[k] - jnp.sum(matrix[k] * solved)) / matrix[k, k])
    return solved


def least_squares(hessenberg, initial_norm):
    target = jnp.zeros((hessenberg.shape[0],), jnp.float32).at[0].set(initial_norm)
    normal = jnp.dot(hessenberg.T, hessenberg, precision=precise)
    weights = solve_small(normal, jnp.dot(hessenberg.T, target, precision=precise))
    misfit = target - jnp.dot(hessenberg, weights, precision=precise)
    return (weights, jnp.sqrt(jnp.sum(misfit * misfit)) / initial_norm)


def shards(forcing, pivot_inverse, lower_face, upper_face, side_coupling, orientation):
    lead = forcing.shape[:2]
    elements = forcing.shape[2]
    from_below, from_above, carries, leaving = line_maps(pivot_inverse, lower_face, upper_face)
    coupling = lateral_maps(side_coupling, orientation)
    local_leaving = leaving[..., 2 * FACE :]

    def local_of(rows):
        return jnp.concatenate(
            [rows[..., BLOCK - FACE :], rows[..., :FACE]], 2
        ).reshape(lead + (2 * elements * FACE,))

    def outgoing(rows):
        return mv(local_leaving, local_of(rows)[:, :, None]).reshape(lead + (2 * FACE,))

    def flat_gather(block):
        count = block.shape[0]
        block = block.reshape((count,) + lead + (2, FACE))
        return jnp.transpose(block, (1, 2, 3, 0, 4)).reshape(lead + (-1,))

    def precond(rows, gathered):
        local = local_of(rows)
        entering = mv(entry, gathered[:, :, None])
        full = jnp.concatenate([entering.reshape(lead + (2 * FACE,)), local], -1)
        faces = mv(carries, full[:, :, None])
        return (
            rows
            + mv(from_below, faces[:, :, :elements])
            + mv(from_above, faces[:, :, elements:])
        )

    def dot(a, b):
        return jnp.sum(a * b)

    entry_count = forcing.size * lax.axis_size("wall") * lax.axis_size("sx") * lax.axis_size("sy")
    basis = [forcing]
    images = [mv(pivot_inverse, forcing)]
    needed = jnp.stack(
        [leaving[..., 0, :, :FACE], leaving[..., 1, :, FACE : 2 * FACE], leaving[..., 1, :, :FACE]], 2
    )
    first = outgoing(images[0]).reshape(lead + (1, 2, FACE))
    packed = jnp.concatenate(
        [needed, jnp.pad(first, ((0, 0), (0, 0), (0, 0), (0, FACE - 2), (0, 0)))], 2
    )
    together = lax.all_gather(packed, "wall")
    entry = wall_maps(together[:, :, :, :3])
    spread = [flat_gather(together[:, :, :, 3, :2, :])]
    precon = []
    norms = []
    gram = {}
    columns = []
    squares = None
    for j in range(ITERS):
        current = basis[j]
        pre = precond(images[j], spread[j])
        precon.append(pre)
        mapped = current + lateral_from(pre, coupling)
        partial = [dot(current, current)] + [dot(mapped, basis[i]) for i in range(j + 1)]
        partial += [dot(basis[i], current) for i in range(j)]
        partial = jnp.stack(partial)
        if j + 1 < ITERS:
            mapped_rows = mv(pivot_inverse, mapped)
            mapped_out, partial = wall_gather(outgoing(mapped_rows), partial)
            total = allreduce(partial, ("sx", "sy"))
        else:
            total = allreduce(partial)
        norm_sq = total[0]
        if j == 0:
            squares = norm_sq
        norms.append(jnp.sqrt(norm_sq))
        for i in range(j):
            gram[(i, j)] = total[2 + j + i] / (norms[i] * norms[j])
        listed = []
        for i in range(j + 1):
            projected = total[1 + i] / (norms[i] * norms[j])
            for l in range(i):
                projected = projected - listed[l] * gram[(l, i)]
            listed.append(projected)
        following = mapped / norms[j]
        for i in range(j + 1):
            following = following - (listed[i] / norms[i]) * basis[i]
        basis.append(following)
        if j + 1 < ITERS:
            moved = flat_gather(mapped_out) / norms[j]
            image = mapped_rows / norms[j]
            for i in range(j + 1):
                moved = moved - (listed[i] / norms[i]) * spread[i]
                image = image - (listed[i] / norms[i]) * images[i]
            spread.append(moved)
            images.append(image)
        columns.append(listed)
    last = allreduce(jnp.stack([dot(basis[ITERS], basis[ITERS])]))
    norms.append(jnp.sqrt(last[0]))
    full_columns = []
    for j in range(ITERS):
        full_columns.append(
            jnp.concatenate(
                [jnp.stack(columns[j]), norms[j + 1][None], jnp.zeros((ITERS - 1 - j,), jnp.float32)]
            )
        )
    hessenberg = jnp.stack(full_columns, 1)
    forcing_rms = jnp.sqrt(squares / entry_count)
    initial_norm = jnp.sqrt(squares)
    weights, relative = least_squares(hessenberg, initial_norm)
    solution = (weights[0] / norms[0]) * precon[0]
    for j in range(1, ITERS):
        solution = solution + (weights[j] / norms[j]) * precon[j]
    return (solution, relative, forcing_rms)


def solution(mesh):
    return jax.shard_map(
        shards,
        mesh=mesh,
        in_specs=(
            P("sx", "sy", "wall", None),
            P("sx", "sy", "wall", None, None),
            P("sx", "sy", "wall", None, None),
            P("sx", "sy", "wall", None, None),
            P("sx", "sy", "wall", None, None, None),
            P("sx", "sy", "wall", None),
        ),
        out_specs=(P("sx", "sy", "wall", None), P(), P()),
        check_vma=False,
    )
```

```python
import numpy as np
import jax
import jax.numpy as jnp
from jax import lax
from jax.sharding import PartitionSpec as P

PTS = 4
VARS = 6
BLOCK = 384
FACE = 96
ITERS = 3


precise = lax.Precision.HIGHEST


def mm(matrix, columns):
    return jnp.einsum("xyab,xybk->xyak", matrix, columns, precision=precise)


def unit(size, shift=0):
    hidden = jnp.minimum(lax.axis_index("wall"), 0)
    rows = lax.broadcasted_iota(jnp.int32, (FACE, size), 0)
    cols = lax.broadcasted_iota(jnp.int32, (FACE, size), 1)
    return (cols == rows + shift + hidden).astype(jnp.float32)


def wall_gather(part, sums):
    count = lax.axis_size("wall")
    slots = lax.broadcasted_iota(jnp.int32, (count,) + part.shape, 0)
    spread = jnp.where(slots == lax.axis_index("wall"), part[None], 0.0)
    packed = allreduce(jnp.concatenate([sums, spread.reshape(-1)]), ("wall",))
    return packed[sums.shape[0] :].reshape(spread.shape), packed[: sums.shape[0]]


def allreduce(values, axes=("wall", "sx", "sy")):
    for axis in axes:
        count = lax.axis_size(axis)
        step = 1
        while step < count:
            pairs = [(i, i ^ step) for i in range(count)]
            values = values + lax.ppermute(values, axis, pairs)
            step *= 2
    return values


def mv(matrix, vector):
    return jnp.sum(matrix * vector[..., None, :], -1)


def lateral_maps(side_coupling, orientation):
    grid = side_coupling.reshape(side_coupling.shape[:-1] + (PTS, PTS, VARS))
    picked = None
    for quarter in range(4):
        turned = jnp.rot90(grid, -quarter, axes=(-3, -2)).reshape(side_coupling.shape)
        if picked is None:
            picked = turned
        else:
            picked = jnp.where((orientation == quarter)[..., None, None], turned, picked)
    lead = picked.shape[:3]
    none = [(0, 0)] * len(lead)
    placed = []
    for face, (shape, gap) in enumerate(
        [
            ((PTS, PTS, 1), (0, 0, (0, PTS - 1))),
            ((PTS, PTS, 1), (0, 0, (PTS - 1, 0))),
            ((PTS, 1, PTS), (0, (0, PTS - 1), 0)),
            ((PTS, 1, PTS), (0, (PTS - 1, 0), 0)),
        ]
    ):
        one = picked[..., face, :, :].reshape(lead + shape + (VARS, FACE))
        widths = none + [g if g else (0, 0) for g in gap] + [(0, 0), (0, 0)]
        placed.append(jnp.pad(one, widths).reshape(lead + (BLOCK, FACE)))
    return jnp.concatenate(placed, -1)


def neighbour(values, axis, dim, later):
    count = lax.axis_size(axis)
    size = values.shape[dim]
    if later:
        pairs = [(i + 1, i) for i in range(count - 1)]
        moved = lax.ppermute(lax.slice_in_dim(values, 0, 1, axis=dim), axis, pairs)
        return jnp.concatenate([lax.slice_in_dim(values, 1, size, axis=dim), moved], dim)
    pairs = [(i, i + 1) for i in range(count - 1)]
    moved = lax.ppermute(lax.slice_in_dim(values, size - 1, size, axis=dim), axis, pairs)
    return jnp.concatenate([moved, lax.slice_in_dim(values, 0, size - 1, axis=dim)], dim)


def lateral_from(direction, coupling):
    lead = direction.shape[:3]
    grid = direction.reshape(lead + (PTS, PTS, PTS, VARS))
    faces = [
        grid[..., :, :, 0, :],
        grid[..., :, :, PTS - 1, :],
        grid[..., :, 0, :, :],
        grid[..., :, PTS - 1, :, :],
    ]
    faces = [one.reshape(lead + (FACE,)) for one in faces]
    across = jnp.concatenate(
        [
            neighbour(faces[1], "sx", 0, False),
            neighbour(faces[0], "sx", 0, True),
            neighbour(faces[3], "sy", 1, False),
            neighbour(faces[2], "sy", 1, True),
        ],
        -1,
    )
    return mv(coupling, across)


def line_maps(pivot_inverse, lower_face, upper_face):
    lead = pivot_inverse.shape[:2]
    elements = pivot_inverse.shape[2]
    from_below = -jnp.einsum(
        "xyeab,xyebc->xyeac", pivot_inverse[..., :FACE], lower_face, precision=precise
    )
    from_above = -jnp.einsum(
        "xyeab,xyebc->xyeac", pivot_inverse[..., BLOCK - FACE :], upper_face, precision=precise
    )
    lower_maps = from_below[..., BLOCK - FACE :, :]
    trail_maps = from_below[..., :FACE, :]
    upper_maps = from_above[..., :FACE, :]
    inputs = (2 + 2 * elements) * FACE
    entering_low = unit(inputs, 0)
    entering_high = unit(inputs, FACE)
    ahead = [unit(inputs, (2 + i) * FACE) for i in range(elements)]
    trail0 = [unit(inputs, (2 + elements + i) * FACE) for i in range(elements)]
    carried = jnp.broadcast_to(entering_low, lead + entering_low.shape)
    before = []
    for i in range(elements):
        before.append(carried)
        carried = ahead[i] + mm(lower_maps[:, :, i], carried)
    leaving_high = carried
    trails = [trail0[i] + mm(trail_maps[:, :, i], before[i]) for i in range(elements)]
    carried = jnp.broadcast_to(entering_high, lead + entering_high.shape)
    after = [None] * elements
    for i in reversed(range(elements)):
        after[i] = carried
        carried = trails[i] + mm(upper_maps[:, :, i], carried)
    leaving_low = carried
    carries = jnp.stack(before + after, 2)
    leaving = jnp.stack([leaving_high, leaving_low], 2)
    return from_below, from_above, carries, leaving


def wall_maps(gathered):
    axis = "wall"
    count = lax.axis_size(axis)
    place = lax.axis_index(axis)
    lead = gathered.shape[1:3]
    half = count * FACE
    low = [jnp.zeros(lead + (FACE, half), jnp.float32)]
    for d in range(count - 1):
        low.append(unit(half, d * FACE) + mm(gathered[d, :, :, 0], low[d]))
    zeros = jnp.zeros(lead + (FACE, half), jnp.float32)
    picked_low = zeros
    for d in range(count):
        picked_low = jnp.where(place == d, low[d], picked_low)
    high = jnp.zeros(lead + (FACE, 2 * half), jnp.float32)
    picked_high = jnp.where(place == count - 1, high, high)
    for d in range(count - 1, 0, -1):
        high = mm(gathered[d, :, :, 1], high) + jnp.concatenate(
            [
                mm(gathered[d, :, :, 2], low[d]),
                jnp.broadcast_to(unit(half, d * FACE), lead + (FACE, half)),
            ],
            -1,
        )
        picked_high = jnp.where(place == d - 1, high, picked_high)
    picked_low = jnp.concatenate([picked_low, zeros], -1)
    return jnp.stack([picked_low, picked_high], 2)


def solve_small(matrix, vector):
    extent = matrix.shape[0]
    index_ids = jnp.arange(extent)
    for k in range(extent):
        factor_col = jnp.where(index_ids > k, matrix[:, k] / matrix[k, k], 0.0)
        matrix = matrix - factor_col[:, None] * matrix[k][None, :]
        vector = vector - factor_col * vector[k]
    solved = jnp.zeros((extent,), jnp.float32)
    for k in reversed(range(extent)):
        solved = solved.at[k].set((vector[k] - jnp.sum(matrix[k] * solved)) / matrix[k, k])
    return solved


def least_squares(hessenberg, initial_norm):
    target = jnp.zeros((hessenberg.shape[0],), jnp.float32).at[0].set(initial_norm)
    normal = jnp.dot(hessenberg.T, hessenberg, precision=precise)
    weights = solve_small(normal, jnp.dot(hessenberg.T, target, precision=precise))
    misfit = target - jnp.dot(hessenberg, weights, precision=precise)
    return (weights, jnp.sqrt(jnp.sum(misfit * misfit)) / initial_norm)


def shards(forcing, pivot_inverse, lower_face, upper_face, side_coupling, orientation):
    lead = forcing.shape[:2]
    elements = forcing.shape[2]
    from_below, from_above, carries, leaving = line_maps(pivot_inverse, lower_face, upper_face)
    coupling = lateral_maps(side_coupling, orientation)
    local_leaving = leaving[..., 2 * FACE :]

    def local_of(rows):
        return jnp.concatenate(
            [rows[..., BLOCK - FACE :], rows[..., :FACE]], 2
        ).reshape(lead + (2 * elements * FACE,))

    def outgoing(rows):
        return mv(local_leaving, local_of(rows)[:, :, None]).reshape(lead + (2 * FACE,))

    def flat_gather(block):
        count = block.shape[0]
        block = block.reshape((count,) + lead + (2, FACE))
        return jnp.transpose(block, (1, 2, 3, 0, 4)).reshape(lead + (-1,))

    def precond(rows, gathered):
        local = local_of(rows)
        entering = mv(entry, gathered[:, :, None])
        full = jnp.concatenate([entering.reshape(lead + (2 * FACE,)), local], -1)
        faces = mv(carries, full[:, :, None])
        return (
            rows
            + mv(from_below, faces[:, :, :elements])
            + mv(from_above, faces[:, :, elements:])
        )

    def dot(a, b):
        return jnp.sum(a * b)

    entry_count = forcing.size * lax.axis_size("wall") * lax.axis_size("sx") * lax.axis_size("sy")
    basis = [forcing]
    images = [mv(pivot_inverse, forcing)]
    needed = jnp.stack(
        [leaving[..., 0, :, :FACE], leaving[..., 1, :, FACE : 2 * FACE], leaving[..., 1, :, :FACE]], 2
    )
    entry = wall_maps(lax.all_gather(needed, "wall"))
    spread = [flat_gather(lax.all_gather(outgoing(images[0]), "wall"))]
    precon = []
    norms = []
    gram = {}
    columns = []
    squares = None
    for j in range(ITERS):
        current = basis[j]
        pre = precond(images[j], spread[j])
        precon.append(pre)
        mapped = current + lateral_from(pre, coupling)
        pair = jnp.stack([current, mapped], 0)
        known = jnp.stack(basis[: j + 1], 0)
        block = jnp.sum(pair[:, None] * known[None], axis=tuple(range(2, pair.ndim + 1)))
        partial = jnp.concatenate([block[0, j:], block[1], block[0, :j]])
        if j + 1 < ITERS:
            mapped_rows = mv(pivot_inverse, mapped)
            mapped_out, partial = wall_gather(outgoing(mapped_rows), partial)
            total = allreduce(partial, ("sx", "sy"))
        else:
            total = allreduce(partial)
        norm_sq = total[0]
        if j == 0:
            squares = norm_sq
        norms.append(jnp.sqrt(norm_sq))
        for i in range(j):
            gram[(i, j)] = total[2 + j + i] / (norms[i] * norms[j])
        listed = []
        for i in range(j + 1):
            projected = total[1 + i] / (norms[i] * norms[j])
            for l in range(i):
                projected = projected - listed[l] * gram[(l, i)]
            listed.append(projected)
        following = mapped / norms[j]
        for i in range(j + 1):
            following = following - (listed[i] / norms[i]) * basis[i]
        basis.append(following)
        if j + 1 < ITERS:
            moved = flat_gather(mapped_out) / norms[j]
            image = mapped_rows / norms[j]
            for i in range(j + 1):
                moved = moved - (listed[i] / norms[i]) * spread[i]
                image = image - (listed[i] / norms[i]) * images[i]
            spread.append(moved)
            images.append(image)
        columns.append(listed)
    last = allreduce(jnp.stack([dot(basis[ITERS], basis[ITERS])]))
    norms.append(jnp.sqrt(last[0]))
    full_columns = []
    for j in range(ITERS):
        full_columns.append(
            jnp.concatenate(
                [jnp.stack(columns[j]), norms[j + 1][None], jnp.zeros((ITERS - 1 - j,), jnp.float32)]
            )
        )
    hessenberg = jnp.stack(full_columns, 1)
    forcing_rms = jnp.sqrt(squares / entry_count)
    initial_norm = jnp.sqrt(squares)
    weights, relative = least_squares(hessenberg, initial_norm)
    solution = (weights[0] / norms[0]) * precon[0]
    for j in range(1, ITERS):
        solution = solution + (weights[j] / norms[j]) * precon[j]
    return (solution, relative, forcing_rms)


def solution(mesh):
    return jax.shard_map(
        shards,
        mesh=mesh,
        in_specs=(
            P("sx", "sy", "wall", None),
            P("sx", "sy", "wall", None, None),
            P("sx", "sy", "wall", None, None),
            P("sx", "sy", "wall", None, None),
            P("sx", "sy", "wall", None, None, None),
            P("sx", "sy", "wall", None),
        ),
        out_specs=(P("sx", "sy", "wall", None), P(), P()),
        check_vma=False,
    )
```

```python
import numpy as np
import jax
import jax.numpy as jnp
from jax import lax
from jax.sharding import PartitionSpec as P

PTS = 4
VARS = 6
BLOCK = 384
FACE = 96
ITERS = 3


precise = lax.Precision.HIGHEST


def mm(matrix, columns):
    return jnp.einsum("xyab,xybk->xyak", matrix, columns, precision=precise)


def unit(size, shift=0):
    hidden = jnp.minimum(lax.axis_index("wall"), 0)
    rows = lax.broadcasted_iota(jnp.int32, (FACE, size), 0)
    cols = lax.broadcasted_iota(jnp.int32, (FACE, size), 1)
    return (cols == rows + shift + hidden).astype(jnp.float32)


def wall_gather(part, sums):
    count = lax.axis_size("wall")
    room = part.size
    slots = lax.broadcasted_iota(jnp.int32, (count + 1,) + part.shape, 0)
    extra = jnp.pad(sums, (0, room - sums.shape[0])).reshape(part.shape)
    spread = jnp.where(
        slots == lax.axis_index("wall"), part[None], jnp.where(slots == count, extra[None], 0.0)
    )
    packed = allreduce(spread, ("wall",))
    return packed[:count], packed[count].reshape(-1)[: sums.shape[0]]


def allreduce(values, axes=("wall", "sx", "sy")):
    for axis in axes:
        count = lax.axis_size(axis)
        step = 1
        while step < count:
            pairs = [(i, i ^ step) for i in range(count)]
            values = values + lax.ppermute(values, axis, pairs)
            step *= 2
    return values


def mv(matrix, vector):
    return jnp.sum(matrix * vector[..., None, :], -1)


def lateral_maps(side_coupling, orientation):
    grid = side_coupling.reshape(side_coupling.shape[:-1] + (PTS, PTS, VARS))
    picked = None
    for quarter in range(4):
        turned = jnp.rot90(grid, -quarter, axes=(-3, -2)).reshape(side_coupling.shape)
        if picked is None:
            picked = turned
        else:
            picked = jnp.where((orientation == quarter)[..., None, None], turned, picked)
    lead = picked.shape[:3]
    none = [(0, 0)] * len(lead)
    placed = []
    for face, (shape, gap) in enumerate(
        [
            ((PTS, PTS, 1), (0, 0, (0, PTS - 1))),
            ((PTS, PTS, 1), (0, 0, (PTS - 1, 0))),
            ((PTS, 1, PTS), (0, (0, PTS - 1), 0)),
            ((PTS, 1, PTS), (0, (PTS - 1, 0), 0)),
        ]
    ):
        one = picked[..., face, :, :].reshape(lead + shape + (VARS, FACE))
        widths = none + [g if g else (0, 0) for g in gap] + [(0, 0), (0, 0)]
        placed.append(jnp.pad(one, widths).reshape(lead + (BLOCK, FACE)))
    return jnp.concatenate(placed, -1)


def neighbour(values, axis, dim, later):
    count = lax.axis_size(axis)
    size = values.shape[dim]
    if later:
        pairs = [(i + 1, i) for i in range(count - 1)]
        moved = lax.ppermute(lax.slice_in_dim(values, 0, 1, axis=dim), axis, pairs)
        return jnp.concatenate([lax.slice_in_dim(values, 1, size, axis=dim), moved], dim)
    pairs = [(i, i + 1) for i in range(count - 1)]
    moved = lax.ppermute(lax.slice_in_dim(values, size - 1, size, axis=dim), axis, pairs)
    return jnp.concatenate([moved, lax.slice_in_dim(values, 0, size - 1, axis=dim)], dim)


def lateral_from(direction, coupling):
    lead = direction.shape[:3]
    grid = direction.reshape(lead + (PTS, PTS, PTS, VARS))
    faces = [
        grid[..., :, :, 0, :],
        grid[..., :, :, PTS - 1, :],
        grid[..., :, 0, :, :],
        grid[..., :, PTS - 1, :, :],
    ]
    faces = [one.reshape(lead + (FACE,)) for one in faces]
    across = jnp.concatenate(
        [
            neighbour(faces[1], "sx", 0, False),
            neighbour(faces[0], "sx", 0, True),
            neighbour(faces[3], "sy", 1, False),
            neighbour(faces[2], "sy", 1, True),
        ],
        -1,
    )
    return mv(coupling, across)


def line_maps(pivot_inverse, lower_face, upper_face):
    lead = pivot_inverse.shape[:2]
    elements = pivot_inverse.shape[2]
    from_below = -jnp.einsum(
        "xyeab,xyebc->xyeac", pivot_inverse[..., :FACE], lower_face, precision=precise
    )
    from_above = -jnp.einsum(
        "xyeab,xyebc->xyeac", pivot_inverse[..., BLOCK - FACE :], upper_face, precision=precise
    )
    lower_maps = from_below[..., BLOCK - FACE :, :]
    trail_maps = from_below[..., :FACE, :]
    upper_maps = from_above[..., :FACE, :]
    inputs = (2 + 2 * elements) * FACE
    entering_low = unit(inputs, 0)
    entering_high = unit(inputs, FACE)
    ahead = [unit(inputs, (2 + i) * FACE) for i in range(elements)]
    trail0 = [unit(inputs, (2 + elements + i) * FACE) for i in range(elements)]
    carried = jnp.broadcast_to(entering_low, lead + entering_low.shape)
    before = []
    for i in range(elements):
        before.append(carried)
        carried = ahead[i] + mm(lower_maps[:, :, i], carried)
    leaving_high = carried
    trails = [trail0[i] + mm(trail_maps[:, :, i], before[i]) for i in range(elements)]
    carried = jnp.broadcast_to(entering_high, lead + entering_high.shape)
    after = [None] * elements
    for i in reversed(range(elements)):
        after[i] = carried
        carried = trails[i] + mm(upper_maps[:, :, i], carried)
    leaving_low = carried
    carries = jnp.stack(before + after, 2)
    leaving = jnp.stack([leaving_high, leaving_low], 2)
    return from_below, from_above, carries, leaving


def wall_maps(gathered):
    axis = "wall"
    count = lax.axis_size(axis)
    place = lax.axis_index(axis)
    lead = gathered.shape[1:3]
    half = count * FACE
    low = [jnp.zeros(lead + (FACE, half), jnp.float32)]
    for d in range(count - 1):
        low.append(unit(half, d * FACE) + mm(gathered[d, :, :, 0], low[d]))
    zeros = jnp.zeros(lead + (FACE, half), jnp.float32)
    picked_low = zeros
    for d in range(count):
        picked_low = jnp.where(place == d, low[d], picked_low)
    high = jnp.zeros(lead + (FACE, 2 * half), jnp.float32)
    picked_high = jnp.where(place == count - 1, high, high)
    for d in range(count - 1, 0, -1):
        high = mm(gathered[d, :, :, 1], high) + jnp.concatenate(
            [
                mm(gathered[d, :, :, 2], low[d]),
                jnp.broadcast_to(unit(half, d * FACE), lead + (FACE, half)),
            ],
            -1,
        )
        picked_high = jnp.where(place == d - 1, high, picked_high)
    picked_low = jnp.concatenate([picked_low, zeros], -1)
    return jnp.stack([picked_low, picked_high], 2)


def solve_small(matrix, vector):
    extent = matrix.shape[0]
    index_ids = jnp.arange(extent)
    for k in range(extent):
        factor_col = jnp.where(index_ids > k, matrix[:, k] / matrix[k, k], 0.0)
        matrix = matrix - factor_col[:, None] * matrix[k][None, :]
        vector = vector - factor_col * vector[k]
    solved = jnp.zeros((extent,), jnp.float32)
    for k in reversed(range(extent)):
        solved = solved.at[k].set((vector[k] - jnp.sum(matrix[k] * solved)) / matrix[k, k])
    return solved


def least_squares(hessenberg, initial_norm):
    target = jnp.zeros((hessenberg.shape[0],), jnp.float32).at[0].set(initial_norm)
    normal = jnp.dot(hessenberg.T, hessenberg, precision=precise)
    weights = solve_small(normal, jnp.dot(hessenberg.T, target, precision=precise))
    misfit = target - jnp.dot(hessenberg, weights, precision=precise)
    return (weights, jnp.sqrt(jnp.sum(misfit * misfit)) / initial_norm)


def shards(forcing, pivot_inverse, lower_face, upper_face, side_coupling, orientation):
    lead = forcing.shape[:2]
    elements = forcing.shape[2]
    from_below, from_above, carries, leaving = line_maps(pivot_inverse, lower_face, upper_face)
    coupling = lateral_maps(side_coupling, orientation)
    local_leaving = leaving[..., 2 * FACE :]

    def local_of(rows):
        return jnp.concatenate(
            [rows[..., BLOCK - FACE :], rows[..., :FACE]], 2
        ).reshape(lead + (2 * elements * FACE,))

    def outgoing(rows):
        return mv(local_leaving, local_of(rows)[:, :, None]).reshape(lead + (2 * FACE,))

    def flat_gather(block):
        count = block.shape[0]
        block = block.reshape((count,) + lead + (2, FACE))
        return jnp.transpose(block, (1, 2, 3, 0, 4)).reshape(lead + (-1,))

    def precond(rows, gathered):
        local = local_of(rows)
        entering = mv(entry, gathered[:, :, None])
        full = jnp.concatenate([entering.reshape(lead + (2 * FACE,)), local], -1)
        faces = mv(carries, full[:, :, None])
        return (
            rows
            + mv(from_below, faces[:, :, :elements])
            + mv(from_above, faces[:, :, elements:])
        )

    def dot(a, b):
        return jnp.sum(a * b)

    entry_count = forcing.size * lax.axis_size("wall") * lax.axis_size("sx") * lax.axis_size("sy")
    basis = [forcing]
    images = [mv(pivot_inverse, forcing)]
    needed = jnp.stack(
        [leaving[..., 0, :, :FACE], leaving[..., 1, :, FACE : 2 * FACE], leaving[..., 1, :, :FACE]], 2
    )
    entry = wall_maps(lax.all_gather(needed, "wall"))
    spread = [flat_gather(lax.all_gather(outgoing(images[0]), "wall"))]
    precon = []
    norms = []
    gram = {}
    columns = []
    squares = None
    for j in range(ITERS):
        current = basis[j]
        pre = precond(images[j], spread[j])
        precon.append(pre)
        mapped = current + lateral_from(pre, coupling)
        pair = jnp.stack([current, mapped], 0)
        known = jnp.stack(basis[: j + 1], 0)
        block = jnp.sum(pair[:, None] * known[None], axis=tuple(range(2, pair.ndim + 1)))
        partial = jnp.concatenate([block[0, j:], block[1], block[0, :j]])
        if j + 1 < ITERS:
            mapped_rows = mv(pivot_inverse, mapped)
            mapped_out, partial = wall_gather(outgoing(mapped_rows), partial)
            total = allreduce(partial, ("sx", "sy"))
        else:
            total = allreduce(partial)
        norm_sq = total[0]
        if j == 0:
            squares = norm_sq
        norms.append(jnp.sqrt(norm_sq))
        for i in range(j):
            gram[(i, j)] = total[2 + j + i] / (norms[i] * norms[j])
        listed = []
        for i in range(j + 1):
            projected = total[1 + i] / (norms[i] * norms[j])
            for l in range(i):
                projected = projected - listed[l] * gram[(l, i)]
            listed.append(projected)
        following = mapped / norms[j]
        for i in range(j + 1):
            following = following - (listed[i] / norms[i]) * basis[i]
        basis.append(following)
        if j + 1 < ITERS:
            moved = flat_gather(mapped_out) / norms[j]
            image = mapped_rows / norms[j]
            for i in range(j + 1):
                moved = moved - (listed[i] / norms[i]) * spread[i]
                image = image - (listed[i] / norms[i]) * images[i]
            spread.append(moved)
            images.append(image)
        columns.append(listed)
    last = allreduce(jnp.stack([dot(basis[ITERS], basis[ITERS])]))
    norms.append(jnp.sqrt(last[0]))
    full_columns = []
    for j in range(ITERS):
        full_columns.append(
            jnp.concatenate(
                [jnp.stack(columns[j]), norms[j + 1][None], jnp.zeros((ITERS - 1 - j,), jnp.float32)]
            )
        )
    hessenberg = jnp.stack(full_columns, 1)
    forcing_rms = jnp.sqrt(squares / entry_count)
    initial_norm = jnp.sqrt(squares)
    weights, relative = least_squares(hessenberg, initial_norm)
    solution = (weights[0] / norms[0]) * precon[0]
    for j in range(1, ITERS):
        solution = solution + (weights[j] / norms[j]) * precon[j]
    return (solution, relative, forcing_rms)


def solution(mesh):
    return jax.shard_map(
        shards,
        mesh=mesh,
        in_specs=(
            P("sx", "sy", "wall", None),
            P("sx", "sy", "wall", None, None),
            P("sx", "sy", "wall", None, None),
            P("sx", "sy", "wall", None, None),
            P("sx", "sy", "wall", None, None, None),
            P("sx", "sy", "wall", None),
        ),
        out_specs=(P("sx", "sy", "wall", None), P(), P()),
        check_vma=False,
    )
```

```python
import numpy as np
import jax
import jax.numpy as jnp
from jax import lax
from jax.sharding import PartitionSpec as P

PTS = 4
VARS = 6
BLOCK = 384
FACE = 96
ITERS = 3


precise = lax.Precision.HIGHEST


def mm(matrix, columns):
    return jnp.einsum("xyab,xybk->xyak", matrix, columns, precision=precise)


def unit(size, shift=0):
    hidden = jnp.minimum(lax.axis_index("wall"), 0)
    rows = lax.broadcasted_iota(jnp.int32, (FACE, size), 0)
    cols = lax.broadcasted_iota(jnp.int32, (FACE, size), 1)
    return (cols == rows + shift + hidden).astype(jnp.float32)


def wall_gather(part, sums):
    count = lax.axis_size("wall")
    slots = lax.broadcasted_iota(jnp.int32, (count,) + part.shape, 0)
    spread = jnp.where(slots == lax.axis_index("wall"), part[None], 0.0)
    packed = allreduce(jnp.concatenate([sums, spread.reshape(-1)]), ("wall",))
    return packed[sums.shape[0] :].reshape(spread.shape), packed[: sums.shape[0]]


def allreduce(values, axes=("wall", "sx", "sy")):
    for axis in axes:
        count = lax.axis_size(axis)
        step = 1
        while step < count:
            pairs = [(i, i ^ step) for i in range(count)]
            values = values + lax.ppermute(values, axis, pairs)
            step *= 2
    return values


def mv(matrix, vector):
    return jnp.sum(matrix * vector[..., None, :], -1)


def lateral_maps(side_coupling, orientation):
    grid = side_coupling.reshape(side_coupling.shape[:-1] + (PTS, PTS, VARS))
    picked = None
    for quarter in range(4):
        turned = jnp.rot90(grid, -quarter, axes=(-3, -2)).reshape(side_coupling.shape)
        if picked is None:
            picked = turned
        else:
            picked = jnp.where((orientation == quarter)[..., None, None], turned, picked)
    lead = picked.shape[:3]
    none = [(0, 0)] * len(lead)
    placed = []
    for face, (shape, gap) in enumerate(
        [
            ((PTS, PTS, 1), (0, 0, (0, PTS - 1))),
            ((PTS, PTS, 1), (0, 0, (PTS - 1, 0))),
            ((PTS, 1, PTS), (0, (0, PTS - 1), 0)),
            ((PTS, 1, PTS), (0, (PTS - 1, 0), 0)),
        ]
    ):
        one = picked[..., face, :, :].reshape(lead + shape + (VARS, FACE))
        widths = none + [g if g else (0, 0) for g in gap] + [(0, 0), (0, 0)]
        placed.append(jnp.pad(one, widths).reshape(lead + (BLOCK, FACE)))
    return jnp.concatenate(placed, -1)


def neighbour(values, axis, dim, later):
    count = lax.axis_size(axis)
    size = values.shape[dim]
    if later:
        pairs = [(i + 1, i) for i in range(count - 1)]
        moved = lax.ppermute(lax.slice_in_dim(values, 0, 1, axis=dim), axis, pairs)
        return jnp.concatenate([lax.slice_in_dim(values, 1, size, axis=dim), moved], dim)
    pairs = [(i, i + 1) for i in range(count - 1)]
    moved = lax.ppermute(lax.slice_in_dim(values, size - 1, size, axis=dim), axis, pairs)
    return jnp.concatenate([moved, lax.slice_in_dim(values, 0, size - 1, axis=dim)], dim)


def lateral_from(direction, coupling):
    lead = direction.shape[:3]
    grid = direction.reshape(lead + (PTS, PTS, PTS, VARS))
    faces = [
        grid[..., :, :, 0, :],
        grid[..., :, :, PTS - 1, :],
        grid[..., :, 0, :, :],
        grid[..., :, PTS - 1, :, :],
    ]
    faces = [one.reshape(lead + (FACE,)) for one in faces]
    across = jnp.concatenate(
        [
            neighbour(faces[1], "sx", 0, False),
            neighbour(faces[0], "sx", 0, True),
            neighbour(faces[3], "sy", 1, False),
            neighbour(faces[2], "sy", 1, True),
        ],
        -1,
    )
    return mv(coupling, across)


def line_maps(pivot_inverse, lower_face, upper_face):
    lead = pivot_inverse.shape[:2]
    elements = pivot_inverse.shape[2]
    from_below = -jnp.einsum(
        "xyeab,xyebc->xyeac", pivot_inverse[..., :FACE], lower_face, precision=precise
    )
    from_above = -jnp.einsum(
        "xyeab,xyebc->xyeac", pivot_inverse[..., BLOCK - FACE :], upper_face, precision=precise
    )
    lower_maps = from_below[..., BLOCK - FACE :, :]
    trail_maps = from_below[..., :FACE, :]
    upper_maps = from_above[..., :FACE, :]
    inputs = (2 + 2 * elements) * FACE
    entering_low = unit(inputs, 0)
    entering_high = unit(inputs, FACE)
    ahead = [unit(inputs, (2 + i) * FACE) for i in range(elements)]
    trail0 = [unit(inputs, (2 + elements + i) * FACE) for i in range(elements)]
    carried = jnp.broadcast_to(entering_low, lead + entering_low.shape)
    before = []
    for i in range(elements):
        before.append(carried)
        carried = ahead[i] + mm(lower_maps[:, :, i], carried)
    leaving_high = carried
    trails = [trail0[i] + mm(trail_maps[:, :, i], before[i]) for i in range(elements)]
    carried = jnp.broadcast_to(entering_high, lead + entering_high.shape)
    after = [None] * elements
    for i in reversed(range(elements)):
        after[i] = carried
        carried = trails[i] + mm(upper_maps[:, :, i], carried)
    leaving_low = carried
    carries = jnp.stack(before + after, 2)
    leaving = jnp.stack([leaving_high, leaving_low], 2)
    return from_below, from_above, carries, leaving


def wall_maps(gathered):
    axis = "wall"
    count = lax.axis_size(axis)
    place = lax.axis_index(axis)
    lead = gathered.shape[1:3]
    half = count * FACE
    low = [jnp.zeros(lead + (FACE, half), jnp.float32)]
    for d in range(count - 1):
        low.append(unit(half, d * FACE) + mm(gathered[d, :, :, 0], low[d]))
    zeros = jnp.zeros(lead + (FACE, half), jnp.float32)
    picked_low = zeros
    for d in range(count):
        picked_low = jnp.where(place == d, low[d], picked_low)
    high = jnp.zeros(lead + (FACE, 2 * half), jnp.float32)
    picked_high = jnp.where(place == count - 1, high, high)
    for d in range(count - 1, 0, -1):
        high = mm(gathered[d, :, :, 1], high) + jnp.concatenate(
            [
                mm(gathered[d, :, :, 2], low[d]),
                jnp.broadcast_to(unit(half, d * FACE), lead + (FACE, half)),
            ],
            -1,
        )
        picked_high = jnp.where(place == d - 1, high, picked_high)
    picked_low = jnp.concatenate([picked_low, zeros], -1)
    return jnp.stack([picked_low, picked_high], 2)


def solve_small(matrix, vector):
    extent = matrix.shape[0]
    index_ids = jnp.arange(extent)
    for k in range(extent):
        factor_col = jnp.where(index_ids > k, matrix[:, k] / matrix[k, k], 0.0)
        matrix = matrix - factor_col[:, None] * matrix[k][None, :]
        vector = vector - factor_col * vector[k]
    solved = jnp.zeros((extent,), jnp.float32)
    for k in reversed(range(extent)):
        solved = solved.at[k].set((vector[k] - jnp.sum(matrix[k] * solved)) / matrix[k, k])
    return solved


def least_squares(hessenberg, initial_norm):
    target = jnp.zeros((hessenberg.shape[0],), jnp.float32).at[0].set(initial_norm)
    normal = jnp.dot(hessenberg.T, hessenberg, precision=precise)
    weights = solve_small(normal, jnp.dot(hessenberg.T, target, precision=precise))
    misfit = target - jnp.dot(hessenberg, weights, precision=precise)
    return (weights, jnp.sqrt(jnp.sum(misfit * misfit)) / initial_norm)


def shards(forcing, pivot_inverse, lower_face, upper_face, side_coupling, orientation):
    lead = forcing.shape[:2]
    elements = forcing.shape[2]
    from_below, from_above, carries, leaving = line_maps(pivot_inverse, lower_face, upper_face)
    coupling = lateral_maps(side_coupling, orientation)
    local_leaving = leaving[..., 2 * FACE :]

    def local_of(rows):
        return jnp.concatenate(
            [rows[..., BLOCK - FACE :], rows[..., :FACE]], 2
        ).reshape(lead + (2 * elements * FACE,))

    def outgoing(rows):
        return mv(local_leaving, local_of(rows)[:, :, None]).reshape(lead + (2 * FACE,))

    def flat_gather(block):
        count = block.shape[0]
        block = block.reshape((count,) + lead + (2, FACE))
        return jnp.transpose(block, (1, 2, 3, 0, 4)).reshape(lead + (-1,))

    def precond(rows, gathered):
        local = local_of(rows)
        entering = mv(entry, gathered[:, :, None])
        full = jnp.concatenate([entering.reshape(lead + (2 * FACE,)), local], -1)
        faces = mv(carries, full[:, :, None])
        return (
            rows
            + mv(from_below, faces[:, :, :elements])
            + mv(from_above, faces[:, :, elements:])
        )

    def dot(a, b):
        return jnp.sum(a * b)

    entry_count = forcing.size * lax.axis_size("wall") * lax.axis_size("sx") * lax.axis_size("sy")
    basis = [forcing]
    images = [mv(pivot_inverse, forcing)]
    needed = jnp.stack(
        [leaving[..., 0, :, :FACE], leaving[..., 1, :, FACE : 2 * FACE], leaving[..., 1, :, :FACE]], 2
    )
    entry = wall_maps(lax.all_gather(needed, "wall"))
    first, _ = wall_gather(outgoing(images[0]), jnp.zeros((1,), jnp.float32))
    spread = [flat_gather(first)]
    precon = []
    norms = []
    gram = {}
    columns = []
    squares = None
    for j in range(ITERS):
        current = basis[j]
        pre = precond(images[j], spread[j])
        precon.append(pre)
        mapped = current + lateral_from(pre, coupling)
        pair = jnp.stack([current, mapped], 0)
        known = jnp.stack(basis[: j + 1], 0)
        block = jnp.sum(pair[:, None] * known[None], axis=tuple(range(2, pair.ndim + 1)))
        partial = jnp.concatenate([block[0, j:], block[1], block[0, :j]])
        if j + 1 < ITERS:
            mapped_rows = mv(pivot_inverse, mapped)
            mapped_out, partial = wall_gather(outgoing(mapped_rows), partial)
            total = allreduce(partial, ("sx", "sy"))
        else:
            total = allreduce(partial)
        norm_sq = total[0]
        if j == 0:
            squares = norm_sq
        norms.append(jnp.sqrt(norm_sq))
        for i in range(j):
            gram[(i, j)] = total[2 + j + i] / (norms[i] * norms[j])
        listed = []
        for i in range(j + 1):
            projected = total[1 + i] / (norms[i] * norms[j])
            for l in range(i):
                projected = projected - listed[l] * gram[(l, i)]
            listed.append(projected)
        following = mapped / norms[j]
        for i in range(j + 1):
            following = following - (listed[i] / norms[i]) * basis[i]
        basis.append(following)
        if j + 1 < ITERS:
            moved = flat_gather(mapped_out) / norms[j]
            image = mapped_rows / norms[j]
            for i in range(j + 1):
                moved = moved - (listed[i] / norms[i]) * spread[i]
                image = image - (listed[i] / norms[i]) * images[i]
            spread.append(moved)
            images.append(image)
        columns.append(listed)
    last = allreduce(jnp.stack([dot(basis[ITERS], basis[ITERS])]))
    norms.append(jnp.sqrt(last[0]))
    full_columns = []
    for j in range(ITERS):
        full_columns.append(
            jnp.concatenate(
                [jnp.stack(columns[j]), norms[j + 1][None], jnp.zeros((ITERS - 1 - j,), jnp.float32)]
            )
        )
    hessenberg = jnp.stack(full_columns, 1)
    forcing_rms = jnp.sqrt(squares / entry_count)
    initial_norm = jnp.sqrt(squares)
    weights, relative = least_squares(hessenberg, initial_norm)
    solution = (weights[0] / norms[0]) * precon[0]
    for j in range(1, ITERS):
        solution = solution + (weights[j] / norms[j]) * precon[j]
    return (solution, relative, forcing_rms)


def solution(mesh):
    return jax.shard_map(
        shards,
        mesh=mesh,
        in_specs=(
            P("sx", "sy", "wall", None),
            P("sx", "sy", "wall", None, None),
            P("sx", "sy", "wall", None, None),
            P("sx", "sy", "wall", None, None),
            P("sx", "sy", "wall", None, None, None),
            P("sx", "sy", "wall", None),
        ),
        out_specs=(P("sx", "sy", "wall", None), P(), P()),
        check_vma=False,
    )
```

```python
import numpy as np
import jax
import jax.numpy as jnp
from jax import lax
from jax.sharding import PartitionSpec as P

PTS = 4
VARS = 6
BLOCK = 384
FACE = 96
ITERS = 3


precise = lax.Precision.HIGHEST


def mm(matrix, columns):
    return jnp.einsum("xyab,xybk->xyak", matrix, columns, precision=precise)


def unit(size, shift=0):
    hidden = jnp.minimum(lax.axis_index("wall"), 0)
    rows = lax.broadcasted_iota(jnp.int32, (FACE, size), 0)
    cols = lax.broadcasted_iota(jnp.int32, (FACE, size), 1)
    return (cols == rows + shift + hidden).astype(jnp.float32)


def wall_gather(part, sums):
    count = lax.axis_size("wall")
    slots = lax.broadcasted_iota(jnp.int32, (count,) + part.shape, 0)
    spread = jnp.where(slots == lax.axis_index("wall"), part[None], 0.0)
    packed = allreduce(jnp.concatenate([sums, spread.reshape(-1)]), ("wall",))
    return packed[sums.shape[0] :].reshape(spread.shape), packed[: sums.shape[0]]


def wall_stack(part):
    axis = "wall"
    count = lax.axis_size(axis)
    place = lax.axis_index(axis)
    block = part[None]
    step = 1
    while step < count:
        pairs = [(i, i ^ step) for i in range(count)]
        other = lax.ppermute(block, axis, pairs)
        upper = (place // step) % 2 == 1
        block = jnp.where(
            upper, jnp.concatenate([other, block], 0), jnp.concatenate([block, other], 0)
        )
        step *= 2
    return block


def allreduce(values, axes=("wall", "sx", "sy")):
    for axis in axes:
        count = lax.axis_size(axis)
        step = 1
        while step < count:
            pairs = [(i, i ^ step) for i in range(count)]
            values = values + lax.ppermute(values, axis, pairs)
            step *= 2
    return values


def mv(matrix, vector):
    return jnp.sum(matrix * vector[..., None, :], -1)


def lateral_maps(side_coupling, orientation):
    grid = side_coupling.reshape(side_coupling.shape[:-1] + (PTS, PTS, VARS))
    picked = None
    for quarter in range(4):
        turned = jnp.rot90(grid, -quarter, axes=(-3, -2)).reshape(side_coupling.shape)
        if picked is None:
            picked = turned
        else:
            picked = jnp.where((orientation == quarter)[..., None, None], turned, picked)
    lead = picked.shape[:3]
    none = [(0, 0)] * len(lead)
    placed = []
    for face, (shape, gap) in enumerate(
        [
            ((PTS, PTS, 1), (0, 0, (0, PTS - 1))),
            ((PTS, PTS, 1), (0, 0, (PTS - 1, 0))),
            ((PTS, 1, PTS), (0, (0, PTS - 1), 0)),
            ((PTS, 1, PTS), (0, (PTS - 1, 0), 0)),
        ]
    ):
        one = picked[..., face, :, :].reshape(lead + shape + (VARS, FACE))
        widths = none + [g if g else (0, 0) for g in gap] + [(0, 0), (0, 0)]
        placed.append(jnp.pad(one, widths).reshape(lead + (BLOCK, FACE)))
    return jnp.concatenate(placed, -1)


def neighbour(values, axis, dim, later):
    count = lax.axis_size(axis)
    size = values.shape[dim]
    if later:
        pairs = [(i + 1, i) for i in range(count - 1)]
        moved = lax.ppermute(lax.slice_in_dim(values, 0, 1, axis=dim), axis, pairs)
        return jnp.concatenate([lax.slice_in_dim(values, 1, size, axis=dim), moved], dim)
    pairs = [(i, i + 1) for i in range(count - 1)]
    moved = lax.ppermute(lax.slice_in_dim(values, size - 1, size, axis=dim), axis, pairs)
    return jnp.concatenate([moved, lax.slice_in_dim(values, 0, size - 1, axis=dim)], dim)


def lateral_from(direction, coupling):
    lead = direction.shape[:3]
    grid = direction.reshape(lead + (PTS, PTS, PTS, VARS))
    faces = [
        grid[..., :, :, 0, :],
        grid[..., :, :, PTS - 1, :],
        grid[..., :, 0, :, :],
        grid[..., :, PTS - 1, :, :],
    ]
    faces = [one.reshape(lead + (FACE,)) for one in faces]
    across = jnp.concatenate(
        [
            neighbour(faces[1], "sx", 0, False),
            neighbour(faces[0], "sx", 0, True),
            neighbour(faces[3], "sy", 1, False),
            neighbour(faces[2], "sy", 1, True),
        ],
        -1,
    )
    return mv(coupling, across)


def line_maps(pivot_inverse, lower_face, upper_face):
    lead = pivot_inverse.shape[:2]
    elements = pivot_inverse.shape[2]
    from_below = -jnp.einsum(
        "xyeab,xyebc->xyeac", pivot_inverse[..., :FACE], lower_face, precision=precise
    )
    from_above = -jnp.einsum(
        "xyeab,xyebc->xyeac", pivot_inverse[..., BLOCK - FACE :], upper_face, precision=precise
    )
    lower_maps = from_below[..., BLOCK - FACE :, :]
    trail_maps = from_below[..., :FACE, :]
    upper_maps = from_above[..., :FACE, :]
    inputs = (2 + 2 * elements) * FACE
    entering_low = unit(inputs, 0)
    entering_high = unit(inputs, FACE)
    ahead = [unit(inputs, (2 + i) * FACE) for i in range(elements)]
    trail0 = [unit(inputs, (2 + elements + i) * FACE) for i in range(elements)]
    carried = jnp.broadcast_to(entering_low, lead + entering_low.shape)
    before = []
    for i in range(elements):
        before.append(carried)
        carried = ahead[i] + mm(lower_maps[:, :, i], carried)
    leaving_high = carried
    trails = [trail0[i] + mm(trail_maps[:, :, i], before[i]) for i in range(elements)]
    carried = jnp.broadcast_to(entering_high, lead + entering_high.shape)
    after = [None] * elements
    for i in reversed(range(elements)):
        after[i] = carried
        carried = trails[i] + mm(upper_maps[:, :, i], carried)
    leaving_low = carried
    carries = jnp.stack(before + after, 2)
    leaving = jnp.stack([leaving_high, leaving_low], 2)
    return from_below, from_above, carries, leaving


def wall_maps(gathered):
    axis = "wall"
    count = lax.axis_size(axis)
    place = lax.axis_index(axis)
    lead = gathered.shape[1:3]
    half = count * FACE
    low = [jnp.zeros(lead + (FACE, half), jnp.float32)]
    for d in range(count - 1):
        low.append(unit(half, d * FACE) + mm(gathered[d, :, :, 0], low[d]))
    zeros = jnp.zeros(lead + (FACE, half), jnp.float32)
    picked_low = zeros
    for d in range(count):
        picked_low = jnp.where(place == d, low[d], picked_low)
    high = jnp.zeros(lead + (FACE, 2 * half), jnp.float32)
    picked_high = jnp.where(place == count - 1, high, high)
    for d in range(count - 1, 0, -1):
        high = mm(gathered[d, :, :, 1], high) + jnp.concatenate(
            [
                mm(gathered[d, :, :, 2], low[d]),
                jnp.broadcast_to(unit(half, d * FACE), lead + (FACE, half)),
            ],
            -1,
        )
        picked_high = jnp.where(place == d - 1, high, picked_high)
    picked_low = jnp.concatenate([picked_low, zeros], -1)
    return jnp.stack([picked_low, picked_high], 2)


def solve_small(matrix, vector):
    extent = matrix.shape[0]
    index_ids = jnp.arange(extent)
    for k in range(extent):
        factor_col = jnp.where(index_ids > k, matrix[:, k] / matrix[k, k], 0.0)
        matrix = matrix - factor_col[:, None] * matrix[k][None, :]
        vector = vector - factor_col * vector[k]
    solved = jnp.zeros((extent,), jnp.float32)
    for k in reversed(range(extent)):
        solved = solved.at[k].set((vector[k] - jnp.sum(matrix[k] * solved)) / matrix[k, k])
    return solved


def least_squares(hessenberg, initial_norm):
    target = jnp.zeros((hessenberg.shape[0],), jnp.float32).at[0].set(initial_norm)
    normal = jnp.dot(hessenberg.T, hessenberg, precision=precise)
    weights = solve_small(normal, jnp.dot(hessenberg.T, target, precision=precise))
    misfit = target - jnp.dot(hessenberg, weights, precision=precise)
    return (weights, jnp.sqrt(jnp.sum(misfit * misfit)) / initial_norm)


def shards(forcing, pivot_inverse, lower_face, upper_face, side_coupling, orientation):
    lead = forcing.shape[:2]
    elements = forcing.shape[2]
    from_below, from_above, carries, leaving = line_maps(pivot_inverse, lower_face, upper_face)
    coupling = lateral_maps(side_coupling, orientation)
    local_leaving = leaving[..., 2 * FACE :]

    def local_of(rows):
        return jnp.concatenate(
            [rows[..., BLOCK - FACE :], rows[..., :FACE]], 2
        ).reshape(lead + (2 * elements * FACE,))

    def outgoing(rows):
        return mv(local_leaving, local_of(rows)[:, :, None]).reshape(lead + (2 * FACE,))

    def flat_gather(block):
        count = block.shape[0]
        block = block.reshape((count,) + lead + (2, FACE))
        return jnp.transpose(block, (1, 2, 3, 0, 4)).reshape(lead + (-1,))

    def precond(rows, gathered):
        local = local_of(rows)
        entering = mv(entry, gathered[:, :, None])
        full = jnp.concatenate([entering.reshape(lead + (2 * FACE,)), local], -1)
        faces = mv(carries, full[:, :, None])
        return (
            rows
            + mv(from_below, faces[:, :, :elements])
            + mv(from_above, faces[:, :, elements:])
        )

    def dot(a, b):
        return jnp.sum(a * b)

    entry_count = forcing.size * lax.axis_size("wall") * lax.axis_size("sx") * lax.axis_size("sy")
    basis = [forcing]
    images = [mv(pivot_inverse, forcing)]
    needed = jnp.stack(
        [leaving[..., 0, :, :FACE], leaving[..., 1, :, FACE : 2 * FACE], leaving[..., 1, :, :FACE]], 2
    )
    entry = wall_maps(wall_stack(needed))
    first, _ = wall_gather(outgoing(images[0]), jnp.zeros((1,), jnp.float32))
    spread = [flat_gather(first)]
    precon = []
    norms = []
    gram = {}
    columns = []
    squares = None
    for j in range(ITERS):
        current = basis[j]
        pre = precond(images[j], spread[j])
        precon.append(pre)
        mapped = current + lateral_from(pre, coupling)
        pair = jnp.stack([current, mapped], 0)
        known = jnp.stack(basis[: j + 1], 0)
        block = jnp.sum(pair[:, None] * known[None], axis=tuple(range(2, pair.ndim + 1)))
        partial = jnp.concatenate([block[0, j:], block[1], block[0, :j]])
        if j + 1 < ITERS:
            mapped_rows = mv(pivot_inverse, mapped)
            mapped_out, partial = wall_gather(outgoing(mapped_rows), partial)
            total = allreduce(partial, ("sx", "sy"))
        else:
            total = allreduce(partial)
        norm_sq = total[0]
        if j == 0:
            squares = norm_sq
        norms.append(jnp.sqrt(norm_sq))
        for i in range(j):
            gram[(i, j)] = total[2 + j + i] / (norms[i] * norms[j])
        listed = []
        for i in range(j + 1):
            projected = total[1 + i] / (norms[i] * norms[j])
            for l in range(i):
                projected = projected - listed[l] * gram[(l, i)]
            listed.append(projected)
        following = mapped / norms[j]
        for i in range(j + 1):
            following = following - (listed[i] / norms[i]) * basis[i]
        basis.append(following)
        if j + 1 < ITERS:
            moved = flat_gather(mapped_out) / norms[j]
            image = mapped_rows / norms[j]
            for i in range(j + 1):
                moved = moved - (listed[i] / norms[i]) * spread[i]
                image = image - (listed[i] / norms[i]) * images[i]
            spread.append(moved)
            images.append(image)
        columns.append(listed)
    last = allreduce(jnp.stack([dot(basis[ITERS], basis[ITERS])]))
    norms.append(jnp.sqrt(last[0]))
    full_columns = []
    for j in range(ITERS):
        full_columns.append(
            jnp.concatenate(
                [jnp.stack(columns[j]), norms[j + 1][None], jnp.zeros((ITERS - 1 - j,), jnp.float32)]
            )
        )
    hessenberg = jnp.stack(full_columns, 1)
    forcing_rms = jnp.sqrt(squares / entry_count)
    initial_norm = jnp.sqrt(squares)
    weights, relative = least_squares(hessenberg, initial_norm)
    solution = (weights[0] / norms[0]) * precon[0]
    for j in range(1, ITERS):
        solution = solution + (weights[j] / norms[j]) * precon[j]
    return (solution, relative, forcing_rms)


def solution(mesh):
    return jax.shard_map(
        shards,
        mesh=mesh,
        in_specs=(
            P("sx", "sy", "wall", None),
            P("sx", "sy", "wall", None, None),
            P("sx", "sy", "wall", None, None),
            P("sx", "sy", "wall", None, None),
            P("sx", "sy", "wall", None, None, None),
            P("sx", "sy", "wall", None),
        ),
        out_specs=(P("sx", "sy", "wall", None), P(), P()),
        check_vma=False,
    )
```

```python
import numpy as np
import jax
import jax.numpy as jnp
from jax import lax
from jax.sharding import PartitionSpec as P

PTS = 4
VARS = 6
BLOCK = 384
FACE = 96
ITERS = 3


precise = lax.Precision.HIGHEST


def mm(matrix, columns):
    return jnp.einsum("xyab,xybk->xyak", matrix, columns, precision=precise)


def unit(size, shift=0):
    hidden = jnp.minimum(lax.axis_index("wall"), 0)
    rows = lax.broadcasted_iota(jnp.int32, (FACE, size), 0)
    cols = lax.broadcasted_iota(jnp.int32, (FACE, size), 1)
    return (cols == rows + shift + hidden).astype(jnp.float32)


def wall_gather(part, sums):
    count = lax.axis_size("wall")
    slots = lax.broadcasted_iota(jnp.int32, (count,) + part.shape, 0)
    spread = jnp.where(slots == lax.axis_index("wall"), part[None], 0.0)
    packed = allreduce(jnp.concatenate([sums, spread.reshape(-1)]), ("wall",))
    return packed[sums.shape[0] :].reshape(spread.shape), packed[: sums.shape[0]]


def allreduce(values, axes=("wall", "sx", "sy")):
    for axis in axes:
        count = lax.axis_size(axis)
        step = 1
        while step < count:
            pairs = [(i, i ^ step) for i in range(count)]
            values = values + lax.ppermute(values, axis, pairs)
            step *= 2
    return values


def mv(matrix, vector):
    return jnp.sum(matrix * vector[..., None, :], -1)


def lateral_maps(side_coupling, orientation):
    index = np.arange(FACE).reshape(PTS, PTS, VARS)
    turns = None
    for quarter in range(4):
        order = np.rot90(index, quarter, axes=(0, 1)).reshape(-1)
        matrix = jnp.asarray(np.eye(FACE, dtype=np.float32)[order])
        if turns is None:
            turns = jnp.broadcast_to(matrix, orientation.shape + (FACE, FACE))
        else:
            turns = jnp.where((orientation == quarter)[..., None, None], matrix, turns)
    picked = side_coupling
    lead = picked.shape[:3]
    none = [(0, 0)] * len(lead)
    placed = []
    for face, (shape, gap) in enumerate(
        [
            ((PTS, PTS, 1), (0, 0, (0, PTS - 1))),
            ((PTS, PTS, 1), (0, 0, (PTS - 1, 0))),
            ((PTS, 1, PTS), (0, (0, PTS - 1), 0)),
            ((PTS, 1, PTS), (0, (PTS - 1, 0), 0)),
        ]
    ):
        one = picked[..., face, :, :].reshape(lead + shape + (VARS, FACE))
        widths = none + [g if g else (0, 0) for g in gap] + [(0, 0), (0, 0)]
        placed.append(jnp.pad(one, widths).reshape(lead + (BLOCK, FACE)))
    return jnp.concatenate(placed, -1), turns


def neighbour(values, axis, dim, later):
    count = lax.axis_size(axis)
    size = values.shape[dim]
    if later:
        pairs = [(i + 1, i) for i in range(count - 1)]
        moved = lax.ppermute(lax.slice_in_dim(values, 0, 1, axis=dim), axis, pairs)
        return jnp.concatenate([lax.slice_in_dim(values, 1, size, axis=dim), moved], dim)
    pairs = [(i, i + 1) for i in range(count - 1)]
    moved = lax.ppermute(lax.slice_in_dim(values, size - 1, size, axis=dim), axis, pairs)
    return jnp.concatenate([moved, lax.slice_in_dim(values, 0, size - 1, axis=dim)], dim)


def lateral_from(direction, maps):
    coupling, turns = maps
    lead = direction.shape[:3]
    grid = direction.reshape(lead + (PTS, PTS, PTS, VARS))
    faces = [
        grid[..., :, :, 0, :],
        grid[..., :, :, PTS - 1, :],
        grid[..., :, 0, :, :],
        grid[..., :, PTS - 1, :, :],
    ]
    faces = [one.reshape(lead + (FACE,)) for one in faces]
    across = jnp.concatenate(
        [
            neighbour(faces[1], "sx", 0, False),
            neighbour(faces[0], "sx", 0, True),
            neighbour(faces[3], "sy", 1, False),
            neighbour(faces[2], "sy", 1, True),
        ],
        -1,
    )
    across = mv(turns, across.reshape(lead + (4, FACE))).reshape(lead + (4 * FACE,))
    return mv(coupling, across)


def line_maps(pivot_inverse, lower_face, upper_face):
    lead = pivot_inverse.shape[:2]
    elements = pivot_inverse.shape[2]
    from_below = -jnp.einsum(
        "xyeab,xyebc->xyeac", pivot_inverse[..., :FACE], lower_face, precision=precise
    )
    from_above = -jnp.einsum(
        "xyeab,xyebc->xyeac", pivot_inverse[..., BLOCK - FACE :], upper_face, precision=precise
    )
    lower_maps = from_below[..., BLOCK - FACE :, :]
    trail_maps = from_below[..., :FACE, :]
    upper_maps = from_above[..., :FACE, :]
    inputs = (2 + 2 * elements) * FACE
    entering_low = unit(inputs, 0)
    entering_high = unit(inputs, FACE)
    ahead = [unit(inputs, (2 + i) * FACE) for i in range(elements)]
    trail0 = [unit(inputs, (2 + elements + i) * FACE) for i in range(elements)]
    carried = jnp.broadcast_to(entering_low, lead + entering_low.shape)
    before = []
    for i in range(elements):
        before.append(carried)
        carried = ahead[i] + mm(lower_maps[:, :, i], carried)
    leaving_high = carried
    trails = [trail0[i] + mm(trail_maps[:, :, i], before[i]) for i in range(elements)]
    carried = jnp.broadcast_to(entering_high, lead + entering_high.shape)
    after = [None] * elements
    for i in reversed(range(elements)):
        after[i] = carried
        carried = trails[i] + mm(upper_maps[:, :, i], carried)
    leaving_low = carried
    carries = jnp.stack(before + after, 2)
    leaving = jnp.stack([leaving_high, leaving_low], 2)
    return from_below, from_above, carries, leaving


def wall_maps(gathered):
    axis = "wall"
    count = lax.axis_size(axis)
    place = lax.axis_index(axis)
    lead = gathered.shape[1:3]
    half = count * FACE
    low = [jnp.zeros(lead + (FACE, half), jnp.float32)]
    for d in range(count - 1):
        low.append(unit(half, d * FACE) + mm(gathered[d, :, :, 0], low[d]))
    zeros = jnp.zeros(lead + (FACE, half), jnp.float32)
    picked_low = zeros
    for d in range(count):
        picked_low = jnp.where(place == d, low[d], picked_low)
    high = jnp.zeros(lead + (FACE, 2 * half), jnp.float32)
    picked_high = jnp.where(place == count - 1, high, high)
    for d in range(count - 1, 0, -1):
        high = mm(gathered[d, :, :, 1], high) + jnp.concatenate(
            [
                mm(gathered[d, :, :, 2], low[d]),
                jnp.broadcast_to(unit(half, d * FACE), lead + (FACE, half)),
            ],
            -1,
        )
        picked_high = jnp.where(place == d - 1, high, picked_high)
    picked_low = jnp.concatenate([picked_low, zeros], -1)
    return jnp.stack([picked_low, picked_high], 2)


def solve_small(matrix, vector):
    extent = matrix.shape[0]
    index_ids = jnp.arange(extent)
    for k in range(extent):
        factor_col = jnp.where(index_ids > k, matrix[:, k] / matrix[k, k], 0.0)
        matrix = matrix - factor_col[:, None] * matrix[k][None, :]
        vector = vector - factor_col * vector[k]
    solved = jnp.zeros((extent,), jnp.float32)
    for k in reversed(range(extent)):
        solved = solved.at[k].set((vector[k] - jnp.sum(matrix[k] * solved)) / matrix[k, k])
    return solved


def least_squares(hessenberg, initial_norm):
    target = jnp.zeros((hessenberg.shape[0],), jnp.float32).at[0].set(initial_norm)
    normal = jnp.dot(hessenberg.T, hessenberg, precision=precise)
    weights = solve_small(normal, jnp.dot(hessenberg.T, target, precision=precise))
    misfit = target - jnp.dot(hessenberg, weights, precision=precise)
    return (weights, jnp.sqrt(jnp.sum(misfit * misfit)) / initial_norm)


def shards(forcing, pivot_inverse, lower_face, upper_face, side_coupling, orientation):
    lead = forcing.shape[:2]
    elements = forcing.shape[2]
    from_below, from_above, carries, leaving = line_maps(pivot_inverse, lower_face, upper_face)
    coupling = lateral_maps(side_coupling, orientation)
    local_leaving = leaving[..., 2 * FACE :]

    def local_of(rows):
        return jnp.concatenate(
            [rows[..., BLOCK - FACE :], rows[..., :FACE]], 2
        ).reshape(lead + (2 * elements * FACE,))

    def outgoing(rows):
        return mv(local_leaving, local_of(rows)[:, :, None]).reshape(lead + (2 * FACE,))

    def flat_gather(block):
        count = block.shape[0]
        block = block.reshape((count,) + lead + (2, FACE))
        return jnp.transpose(block, (1, 2, 3, 0, 4)).reshape(lead + (-1,))

    def precond(rows, gathered):
        local = local_of(rows)
        entering = mv(entry, gathered[:, :, None])
        full = jnp.concatenate([entering.reshape(lead + (2 * FACE,)), local], -1)
        faces = mv(carries, full[:, :, None])
        return (
            rows
            + mv(from_below, faces[:, :, :elements])
            + mv(from_above, faces[:, :, elements:])
        )

    def dot(a, b):
        return jnp.sum(a * b)

    entry_count = forcing.size * lax.axis_size("wall") * lax.axis_size("sx") * lax.axis_size("sy")
    basis = [forcing]
    images = [mv(pivot_inverse, forcing)]
    needed = jnp.stack(
        [leaving[..., 0, :, :FACE], leaving[..., 1, :, FACE : 2 * FACE], leaving[..., 1, :, :FACE]], 2
    )
    entry = wall_maps(lax.all_gather(needed, "wall"))
    first, _ = wall_gather(outgoing(images[0]), jnp.zeros((1,), jnp.float32))
    spread = [flat_gather(first)]
    precon = []
    norms = []
    gram = {}
    columns = []
    squares = None
    for j in range(ITERS):
        current = basis[j]
        pre = precond(images[j], spread[j])
        precon.append(pre)
        mapped = current + lateral_from(pre, coupling)
        pair = jnp.stack([current, mapped], 0)
        known = jnp.stack(basis[: j + 1], 0)
        block = jnp.sum(pair[:, None] * known[None], axis=tuple(range(2, pair.ndim + 1)))
        partial = jnp.concatenate([block[0, j:], block[1], block[0, :j]])
        if j + 1 < ITERS:
            mapped_rows = mv(pivot_inverse, mapped)
            mapped_out, partial = wall_gather(outgoing(mapped_rows), partial)
            total = allreduce(partial, ("sx", "sy"))
        else:
            total = allreduce(partial)
        norm_sq = total[0]
        if j == 0:
            squares = norm_sq
        norms.append(jnp.sqrt(norm_sq))
        for i in range(j):
            gram[(i, j)] = total[2 + j + i] / (norms[i] * norms[j])
        listed = []
        for i in range(j + 1):
            projected = total[1 + i] / (norms[i] * norms[j])
            for l in range(i):
                projected = projected - listed[l] * gram[(l, i)]
            listed.append(projected)
        following = mapped / norms[j]
        for i in range(j + 1):
            following = following - (listed[i] / norms[i]) * basis[i]
        basis.append(following)
        if j + 1 < ITERS:
            moved = flat_gather(mapped_out) / norms[j]
            image = mapped_rows / norms[j]
            for i in range(j + 1):
                moved = moved - (listed[i] / norms[i]) * spread[i]
                image = image - (listed[i] / norms[i]) * images[i]
            spread.append(moved)
            images.append(image)
        columns.append(listed)
    last = allreduce(jnp.stack([dot(basis[ITERS], basis[ITERS])]))
    norms.append(jnp.sqrt(last[0]))
    full_columns = []
    for j in range(ITERS):
        full_columns.append(
            jnp.concatenate(
                [jnp.stack(columns[j]), norms[j + 1][None], jnp.zeros((ITERS - 1 - j,), jnp.float32)]
            )
        )
    hessenberg = jnp.stack(full_columns, 1)
    forcing_rms = jnp.sqrt(squares / entry_count)
    initial_norm = jnp.sqrt(squares)
    weights, relative = least_squares(hessenberg, initial_norm)
    solution = (weights[0] / norms[0]) * precon[0]
    for j in range(1, ITERS):
        solution = solution + (weights[j] / norms[j]) * precon[j]
    return (solution, relative, forcing_rms)


def solution(mesh):
    return jax.shard_map(
        shards,
        mesh=mesh,
        in_specs=(
            P("sx", "sy", "wall", None),
            P("sx", "sy", "wall", None, None),
            P("sx", "sy", "wall", None, None),
            P("sx", "sy", "wall", None, None),
            P("sx", "sy", "wall", None, None, None),
            P("sx", "sy", "wall", None),
        ),
        out_specs=(P("sx", "sy", "wall", None), P(), P()),
        check_vma=False,
    )
```

```python
import numpy as np
import jax
import jax.numpy as jnp
from jax import lax
from jax.sharding import PartitionSpec as P

PTS = 4
VARS = 6
BLOCK = 384
FACE = 96
ITERS = 3


precise = lax.Precision.HIGHEST


def mm(matrix, columns):
    return jnp.einsum("xyab,xybk->xyak", matrix, columns, precision=precise)


def unit(size, shift=0):
    hidden = jnp.minimum(lax.axis_index("wall"), 0)
    rows = lax.broadcasted_iota(jnp.int32, (FACE, size), 0)
    cols = lax.broadcasted_iota(jnp.int32, (FACE, size), 1)
    return (cols == rows + shift + hidden).astype(jnp.float32)


def wall_gather(part, sums):
    count = lax.axis_size("wall")
    slots = lax.broadcasted_iota(jnp.int32, (count,) + part.shape, 0)
    spread = jnp.where(slots == lax.axis_index("wall"), part[None], 0.0)
    packed = allreduce(jnp.concatenate([sums, spread.reshape(-1)]), ("wall",))
    return packed[sums.shape[0] :].reshape(spread.shape), packed[: sums.shape[0]]


def allreduce(values, axes=("wall", "sx", "sy")):
    for axis in axes:
        count = lax.axis_size(axis)
        step = 1
        while step < count:
            pairs = [(i, i ^ step) for i in range(count)]
            values = values + lax.ppermute(values, axis, pairs)
            step *= 2
    return values


def mv(matrix, vector):
    return jnp.sum(matrix * vector[..., None, :], -1)


def lateral_maps(side_coupling, orientation):
    grid = side_coupling.reshape(side_coupling.shape[:-1] + (PTS, PTS, VARS))
    picked = None
    for quarter in range(4):
        turned = jnp.rot90(grid, -quarter, axes=(-3, -2)).reshape(side_coupling.shape)
        if picked is None:
            picked = turned
        else:
            picked = jnp.where((orientation == quarter)[..., None, None], turned, picked)
    lead = picked.shape[:3]
    none = [(0, 0)] * len(lead)
    placed = []
    for face, (shape, gap) in enumerate(
        [
            ((PTS, PTS, 1), (0, 0, (0, PTS - 1))),
            ((PTS, PTS, 1), (0, 0, (PTS - 1, 0))),
            ((PTS, 1, PTS), (0, (0, PTS - 1), 0)),
            ((PTS, 1, PTS), (0, (PTS - 1, 0), 0)),
        ]
    ):
        one = picked[..., face, :, :].reshape(lead + shape + (VARS, FACE))
        widths = none + [g if g else (0, 0) for g in gap] + [(0, 0), (0, 0)]
        placed.append(jnp.pad(one, widths).reshape(lead + (BLOCK, FACE)))
    return jnp.concatenate(placed, -1)


def neighbour(values, axis, dim, later):
    count = lax.axis_size(axis)
    size = values.shape[dim]
    if later:
        pairs = [(i + 1, i) for i in range(count - 1)]
        moved = lax.ppermute(lax.slice_in_dim(values, 0, 1, axis=dim), axis, pairs)
        return jnp.concatenate([lax.slice_in_dim(values, 1, size, axis=dim), moved], dim)
    pairs = [(i, i + 1) for i in range(count - 1)]
    moved = lax.ppermute(lax.slice_in_dim(values, size - 1, size, axis=dim), axis, pairs)
    return jnp.concatenate([moved, lax.slice_in_dim(values, 0, size - 1, axis=dim)], dim)


def lateral_from(direction, coupling):
    lead = direction.shape[:3]
    grid = direction.reshape(lead + (PTS, PTS, PTS, VARS))
    faces = [
        grid[..., :, :, 0, :],
        grid[..., :, :, PTS - 1, :],
        grid[..., :, 0, :, :],
        grid[..., :, PTS - 1, :, :],
    ]
    faces = [one.reshape(lead + (FACE,)) for one in faces]
    across = jnp.concatenate(
        [
            neighbour(faces[1], "sx", 0, False),
            neighbour(faces[0], "sx", 0, True),
            neighbour(faces[3], "sy", 1, False),
            neighbour(faces[2], "sy", 1, True),
        ],
        -1,
    )
    return mv(coupling, across)


def line_maps(pivot_inverse, lower_face, upper_face):
    lead = pivot_inverse.shape[:2]
    elements = pivot_inverse.shape[2]
    from_below = -jnp.einsum(
        "xyeab,xyebc->xyeac", pivot_inverse[..., :FACE], lower_face, precision=precise
    )
    from_above = -jnp.einsum(
        "xyeab,xyebc->xyeac", pivot_inverse[..., BLOCK - FACE :], upper_face, precision=precise
    )
    lower_maps = from_below[..., BLOCK - FACE :, :]
    trail_maps = from_below[..., :FACE, :]
    upper_maps = from_above[..., :FACE, :]
    inputs = (2 + 2 * elements) * FACE
    entering_low = unit(inputs, 0)
    entering_high = unit(inputs, FACE)
    ahead = [unit(inputs, (2 + i) * FACE) for i in range(elements)]
    trail0 = [unit(inputs, (2 + elements + i) * FACE) for i in range(elements)]
    carried = jnp.broadcast_to(entering_low, lead + entering_low.shape)
    before = []
    for i in range(elements):
        before.append(carried)
        carried = ahead[i] + mm(lower_maps[:, :, i], carried)
    leaving_high = carried
    trails = [trail0[i] + mm(trail_maps[:, :, i], before[i]) for i in range(elements)]
    carried = jnp.broadcast_to(entering_high, lead + entering_high.shape)
    after = [None] * elements
    for i in reversed(range(elements)):
        after[i] = carried
        carried = trails[i] + mm(upper_maps[:, :, i], carried)
    leaving_low = carried
    carries = jnp.stack(before + after, 2)
    leaving = jnp.stack([leaving_high, leaving_low], 2)
    return from_below, from_above, carries, leaving


def wall_maps(gathered):
    axis = "wall"
    count = lax.axis_size(axis)
    place = lax.axis_index(axis)
    lead = gathered.shape[1:3]
    half = count * FACE
    low = [jnp.zeros(lead + (FACE, half), jnp.float32)]
    for d in range(count - 1):
        low.append(unit(half, d * FACE) + mm(gathered[d, :, :, 0], low[d]))
    zeros = jnp.zeros(lead + (FACE, half), jnp.float32)
    picked_low = zeros
    for d in range(count):
        picked_low = jnp.where(place == d, low[d], picked_low)
    high = jnp.zeros(lead + (FACE, 2 * half), jnp.float32)
    picked_high = jnp.where(place == count - 1, high, high)
    for d in range(count - 1, 0, -1):
        high = mm(gathered[d, :, :, 1], high) + jnp.concatenate(
            [
                mm(gathered[d, :, :, 2], low[d]),
                jnp.broadcast_to(unit(half, d * FACE), lead + (FACE, half)),
            ],
            -1,
        )
        picked_high = jnp.where(place == d - 1, high, picked_high)
    picked_low = jnp.concatenate([picked_low, zeros], -1)
    return jnp.stack([picked_low, picked_high], 2)


def solve_small(matrix, vector):
    extent = matrix.shape[0]
    index_ids = jnp.arange(extent)
    for k in range(extent):
        factor_col = jnp.where(index_ids > k, matrix[:, k] / matrix[k, k], 0.0)
        matrix = matrix - factor_col[:, None] * matrix[k][None, :]
        vector = vector - factor_col * vector[k]
    solved = jnp.zeros((extent,), jnp.float32)
    for k in reversed(range(extent)):
        solved = solved.at[k].set((vector[k] - jnp.sum(matrix[k] * solved)) / matrix[k, k])
    return solved


def least_squares(hessenberg, initial_norm):
    target = jnp.zeros((hessenberg.shape[0],), jnp.float32).at[0].set(initial_norm)
    normal = jnp.dot(hessenberg.T, hessenberg, precision=precise)
    weights = solve_small(normal, jnp.dot(hessenberg.T, target, precision=precise))
    misfit = target - jnp.dot(hessenberg, weights, precision=precise)
    return (weights, jnp.sqrt(jnp.sum(misfit * misfit)) / initial_norm)


def shards(forcing, pivot_inverse, lower_face, upper_face, side_coupling, orientation):
    lead = forcing.shape[:2]
    elements = forcing.shape[2]
    from_below, from_above, carries, leaving = line_maps(pivot_inverse, lower_face, upper_face)
    coupling = lateral_maps(side_coupling, orientation)
    local_leaving = leaving[..., 2 * FACE :]

    def local_of(rows):
        return jnp.concatenate(
            [rows[..., BLOCK - FACE :], rows[..., :FACE]], 2
        ).reshape(lead + (2 * elements * FACE,))

    def outgoing(rows):
        return mv(local_leaving, local_of(rows)[:, :, None]).reshape(lead + (2 * FACE,))

    def flat_gather(block):
        count = block.shape[0]
        block = block.reshape((count,) + lead + (2, FACE))
        return jnp.transpose(block, (1, 2, 3, 0, 4)).reshape(lead + (-1,))

    both_sides = jnp.concatenate([from_below, from_above], -1)

    def precond(rows, gathered):
        local = local_of(rows)
        entering = mv(entry, gathered[:, :, None])
        full = jnp.concatenate([entering.reshape(lead + (2 * FACE,)), local], -1)
        faces = mv(carries, full[:, :, None])
        paired = jnp.concatenate([faces[:, :, :elements], faces[:, :, elements:]], -1)
        return rows + mv(both_sides, paired)

    def dot(a, b):
        return jnp.sum(a * b)

    entry_count = forcing.size * lax.axis_size("wall") * lax.axis_size("sx") * lax.axis_size("sy")
    basis = [forcing]
    images = [mv(pivot_inverse, forcing)]
    needed = jnp.stack(
        [leaving[..., 0, :, :FACE], leaving[..., 1, :, FACE : 2 * FACE], leaving[..., 1, :, :FACE]], 2
    )
    entry = wall_maps(lax.all_gather(needed, "wall"))
    first, _ = wall_gather(outgoing(images[0]), jnp.zeros((1,), jnp.float32))
    spread = [flat_gather(first)]
    precon = []
    norms = []
    gram = {}
    columns = []
    squares = None
    for j in range(ITERS):
        current = basis[j]
        pre = precond(images[j], spread[j])
        precon.append(pre)
        mapped = current + lateral_from(pre, coupling)
        pair = jnp.stack([current, mapped], 0)
        known = jnp.stack(basis[: j + 1], 0)
        block = jnp.sum(pair[:, None] * known[None], axis=tuple(range(2, pair.ndim + 1)))
        partial = jnp.concatenate([block[0, j:], block[1], block[0, :j]])
        if j + 1 < ITERS:
            mapped_rows = mv(pivot_inverse, mapped)
            mapped_out, partial = wall_gather(outgoing(mapped_rows), partial)
            total = allreduce(partial, ("sx", "sy"))
        else:
            total = allreduce(partial)
        norm_sq = total[0]
        if j == 0:
            squares = norm_sq
        norms.append(jnp.sqrt(norm_sq))
        for i in range(j):
            gram[(i, j)] = total[2 + j + i] / (norms[i] * norms[j])
        listed = []
        for i in range(j + 1):
            projected = total[1 + i] / (norms[i] * norms[j])
            for l in range(i):
                projected = projected - listed[l] * gram[(l, i)]
            listed.append(projected)
        following = mapped / norms[j]
        for i in range(j + 1):
            following = following - (listed[i] / norms[i]) * basis[i]
        basis.append(following)
        if j + 1 < ITERS:
            moved = flat_gather(mapped_out) / norms[j]
            image = mapped_rows / norms[j]
            for i in range(j + 1):
                moved = moved - (listed[i] / norms[i]) * spread[i]
                image = image - (listed[i] / norms[i]) * images[i]
            spread.append(moved)
            images.append(image)
        columns.append(listed)
    last = allreduce(jnp.stack([dot(basis[ITERS], basis[ITERS])]))
    norms.append(jnp.sqrt(last[0]))
    full_columns = []
    for j in range(ITERS):
        full_columns.append(
            jnp.concatenate(
                [jnp.stack(columns[j]), norms[j + 1][None], jnp.zeros((ITERS - 1 - j,), jnp.float32)]
            )
        )
    hessenberg = jnp.stack(full_columns, 1)
    forcing_rms = jnp.sqrt(squares / entry_count)
    initial_norm = jnp.sqrt(squares)
    weights, relative = least_squares(hessenberg, initial_norm)
    solution = (weights[0] / norms[0]) * precon[0]
    for j in range(1, ITERS):
        solution = solution + (weights[j] / norms[j]) * precon[j]
    return (solution, relative, forcing_rms)


def solution(mesh):
    return jax.shard_map(
        shards,
        mesh=mesh,
        in_specs=(
            P("sx", "sy", "wall", None),
            P("sx", "sy", "wall", None, None),
            P("sx", "sy", "wall", None, None),
            P("sx", "sy", "wall", None, None),
            P("sx", "sy", "wall", None, None, None),
            P("sx", "sy", "wall", None),
        ),
        out_specs=(P("sx", "sy", "wall", None), P(), P()),
        check_vma=False,
    )
```
